32 devices in a mesh: row: 8 (over z, core), col: 4 (over y, x).
Axes of the slice: x: 2, y: 2, z: 4, core: 2. Of those that a mesh axis runs over, the one named last changes fastest.
Arguments:
- demand: float32 [2048, 4096], P('row', 'col'), may hold values from 0.2 to 2
- leakage: float32 [2048, 4096], P('row', 'col'), may hold values from 0.05 to 0.5
- conductance: float32 [2048, 4096], P('row', 'col'), may hold values from 0.5 to 4
- vias: int32 [2048, 4096], P('row', 'col'), may hold values 0 or 1
- layer_of: int32 [256, 512], P('row'), may hold values from 0 to 31
- lateral_k: float32 [32, 256, 512], P('col', 'row'), may hold values from 0.3 to 3
- vertical_k: float32 [32, 256, 512], P('col', 'row'), may hold values from 0.1 to 1
Outputs:
- drop: float32 [2048, 4096], P('row', 'col')
- temperature: float32 [32, 256, 512], P('col', 'row')
The draws below stay inside these ranges and needn't reach their ends.
All inputs are finite; a program needn't handle non-finite values. No bound on the sum of `vias` on one device may be relied on, other than what follows from the above.
Results may differ from the reference program's by a relative error of at most 0.0001.
Values sent between devices are 32-bit elements; how exact they have to be, the bound alone decides.
No kernel may reach another device: no remote copies, remote signals or barrier semaphores. Data moves between devices by JAX's collectives and lax.ppermute only.
A program may use at most 128 MiB of HBM per device.

```python
import math
import jax
import jax.numpy as jnp

COARSE = 8
SWEEPS = 4
HEAT_SWEEPS = 4
OUTER = 2
POWER_ROWS = 2048
POWER_COLS = 4096
THERM_ROWS = 256
THERM_COLS = 512
LAYERS = 32


def set_ends(result, own_key, smallest, top_value):
    extent = result.shape
    spot = [jax.random.randint(jax.random.fold_in(own_key, axis), (), 0, extent[axis]) for axis in range(len(extent))]
    result = result.at[tuple(spot)].set(smallest)
    longest = extent.index(max(extent))
    spot[longest] = (spot[longest] + 1) % extent[longest]
    return result.at[tuple(spot)].set(top_value)


def level_of(stream_key, dims, pieces, low, top_value):
    factor_of = 1.0
    for position, shards_of in pieces:
        steps = jax.random.uniform(jax.random.fold_in(jax.random.fold_in(stream_key, 6), position), (shards_of,), jnp.float32, low / len(pieces), top_value / len(pieces))
        factor_of = factor_of * jnp.repeat(jnp.exp(steps), dims[position] // shards_of).reshape((-1,) + (1,) * (len(dims) - 1 - position))
    return factor_of


def setup_inputs(seed: int = 0) -> dict:
    splits = jax.random.split(jax.random.key(seed), 8)
    return {
        "demand": jnp.clip(jnp.exp(math.log(2.0) - 2.3025851 * jax.random.uniform(splits[0], (POWER_ROWS, POWER_COLS), jnp.float32) ** level_of(splits[0], (POWER_ROWS, POWER_COLS), ((0, 8), (1, 4)), -0.2, 0.2)), 0.2, 2.0),
        "leakage": jnp.clip(jnp.exp(math.log(0.5) - 2.3025851 * jax.random.uniform(splits[1], (POWER_ROWS, POWER_COLS), jnp.float32) ** level_of(splits[1], (POWER_ROWS, POWER_COLS), ((0, 8), (1, 4)), -0.2, 0.2)), 0.05, 0.5),
        "conductance": jnp.clip(jnp.exp(math.log(4.0) - 2.0794415 * jax.random.uniform(splits[2], (POWER_ROWS, POWER_COLS), jnp.float32) ** level_of(splits[2], (POWER_ROWS, POWER_COLS), ((0, 8), (1, 4)), -0.2, 0.2)), 0.5, 4.0),
        "vias": set_ends((jax.random.randint(splits[3], (POWER_ROWS, POWER_COLS), 0, 8) < 1).astype(jnp.int32), jax.random.fold_in(splits[3], 1), 0, 1),
        "layer_of": set_ends(jax.random.randint(splits[4], (THERM_ROWS, THERM_COLS), 0, LAYERS), jax.random.fold_in(splits[4], 1), 0, LAYERS - 1).astype(jnp.int32),
        "lateral_k": jnp.clip(jnp.exp(math.log(3.0) - 2.3025851 * jax.random.uniform(splits[5], (LAYERS, THERM_ROWS, THERM_COLS), jnp.float32) ** level_of(splits[5], (LAYERS, THERM_ROWS, THERM_COLS), ((0, 4), (1, 8)), -0.2, 0.2)), 0.3, 3.0),
        "vertical_k": jnp.clip(jnp.exp(math.log(1.0) - 2.3025851 * jax.random.uniform(splits[6], (LAYERS, THERM_ROWS, THERM_COLS), jnp.float32) ** level_of(splits[6], (LAYERS, THERM_ROWS, THERM_COLS), ((0, 4), (1, 8)), -0.2, 0.2)), 0.1, 1.0),
    }


COND_SLOPE = 0.5
LEAK_SLOPE = 0.7
VIA_CONDUCT = 4.0


def fine_of(coarse):
    count_rows, count_cols = coarse.shape
    spread = jnp.broadcast_to(coarse[:, None, :, None], (count_rows, COARSE, count_cols, COARSE))
    return spread.reshape(count_rows * COARSE, count_cols * COARSE)


def coarse_of(fine):
    count_rows = fine.shape[0] // COARSE
    count_cols = fine.shape[1] // COARSE
    return jnp.mean(fine.reshape(count_rows, COARSE, count_cols, COARSE), axis=(1, 3))


def relax_power(drop, cond, load, via_g):
    drop_pad = jnp.pad(drop, 1)
    cond_pad = jnp.pad(cond, 1)
    w_north = (cond + cond_pad[:-2, 1:-1]) * 0.5
    w_south = (cond + cond_pad[2:, 1:-1]) * 0.5
    w_west = (cond + cond_pad[1:-1, :-2]) * 0.5
    w_east = (cond + cond_pad[1:-1, 2:]) * 0.5
    summed = load + w_north * drop_pad[:-2, 1:-1] + w_south * drop_pad[2:, 1:-1] + w_west * drop_pad[1:-1, :-2] + w_east * drop_pad[1:-1, 2:]
    return summed / (w_north + w_south + w_west + w_east + via_g)


def relax_thermal(temp, source, lateral_k, vertical_k):
    temp_pad = jnp.pad(temp, 1)
    lat_pad = jnp.pad(lateral_k, 1)
    vert_pad = jnp.pad(vertical_k, 1)
    w_north = (lateral_k + lat_pad[1:-1, :-2, 1:-1]) * 0.5
    w_south = (lateral_k + lat_pad[1:-1, 2:, 1:-1]) * 0.5
    w_west = (lateral_k + lat_pad[1:-1, 1:-1, :-2]) * 0.5
    w_east = (lateral_k + lat_pad[1:-1, 1:-1, 2:]) * 0.5
    w_below = (vertical_k + vert_pad[:-2, 1:-1, 1:-1]) * 0.5
    w_above = (vertical_k + vert_pad[2:, 1:-1, 1:-1]) * 0.5
    summed = source + w_north * temp_pad[1:-1, :-2, 1:-1] + w_south * temp_pad[1:-1, 2:, 1:-1] + w_west * temp_pad[1:-1, 1:-1, :-2] + w_east * temp_pad[1:-1, 1:-1, 2:] + w_below * temp_pad[:-2, 1:-1, 1:-1] + w_above * temp_pad[2:, 1:-1, 1:-1]
    return summed / (w_north + w_south + w_west + w_east + w_below + w_above)


def reference(demand, leakage, conductance, vias, layer_of, lateral_k, vertical_k):
    drop = jnp.zeros(demand.shape, jnp.float32)
    temp = jnp.zeros(lateral_k.shape, jnp.float32)
    via_g = VIA_CONDUCT * vias.astype(jnp.float32)
    layers = jnp.arange(lateral_k.shape[0], dtype=jnp.int32)
    picker = layer_of[None, :, :] == layers[:, None, None]
    cell_temp = jnp.zeros(layer_of.shape, jnp.float32)
    for outer in range(OUTER):
        if outer > 0:
            cell_temp = jnp.sum(jnp.where(picker, temp, jnp.zeros_like(temp)), axis=0)
        fine_temp = fine_of(cell_temp)
        cond = conductance / (1.0 + COND_SLOPE * fine_temp)
        load = demand + leakage * jnp.exp(LEAK_SLOPE * fine_temp)
        for sweep in range(SWEEPS):
            drop = relax_power(drop, cond, load, via_g)
        heat = coarse_of(load * (1.0 - drop) + cond * drop * drop)
        source = jnp.where(picker, heat[None, :, :], jnp.zeros_like(temp))
        for sweep in range(HEAT_SWEEPS):
            temp = relax_thermal(temp, source, lateral_k, vertical_k)
    return drop, temp
```

```python
import jax
import jax.numpy as jnp
from jax import lax
from jax.sharding import PartitionSpec as P

COARSE = 8
SWEEPS = 4
HEAT_SWEEPS = 4
OUTER = 2


COND_SLOPE = 0.5
LEAK_SLOPE = 0.7
VIA_CONDUCT = 4.0

HALO = 4
OFFSETS = [(dr, dc) for dr in (-1, 0, 1) for dc in (-1, 0, 1) if (dr, dc) != (0, 0)]


def piece(x, ax_r, ax_c, h, dr, dc):
    for ax, d in ((ax_r, dr), (ax_c, dc)):
        if ax is None:
            continue
        if d == 1:
            x = lax.slice_in_dim(x, x.shape[ax] - h, None, axis=ax)
        elif d == -1:
            x = lax.slice_in_dim(x, 0, h, axis=ax)
    return x


def exchange(items):
    n_r = lax.axis_size("row")
    n_c = lax.axis_size("col")
    received = [dict() for _ in items]
    for dr, dc in OFFSETS:
        sends = []
        for idx, (x, ax_r, ax_c, h) in enumerate(items):
            if (ax_r is None and dr != 0) or (ax_c is None and dc != 0):
                continue
            sends.append((idx, piece(x, ax_r, ax_c, h, dr, dc)))
        if not sends:
            continue
        flat = jnp.concatenate([p.reshape(-1) for _, p in sends])
        pairs = []
        for r in range(n_r):
            for c in range(n_c):
                rr, cc = r + dr, c + dc
                if 0 <= rr < n_r and 0 <= cc < n_c:
                    pairs.append((r * n_c + c, rr * n_c + cc))
        got = lax.ppermute(flat, ("row", "col"), pairs)
        start = 0
        for idx, p in sends:
            size = p.size
            received[idx][(dr, dc)] = got[start:start + size].reshape(p.shape)
            start += size
    return received


def assemble(x, recv, ax_r, ax_c):
    def get(dr, dc):
        if (dr, dc) == (0, 0):
            return x
        return recv[(dr, dc)]

    rows_r = (1, 0, -1) if ax_r is not None else (0,)
    rows_c = (1, 0, -1) if ax_c is not None else (0,)
    bands = []
    for dr in rows_r:
        blocks = [get(dr, dc) for dc in rows_c]
        bands.append(jnp.concatenate(blocks, axis=ax_c) if len(blocks) > 1 else blocks[0])
    return jnp.concatenate(bands, axis=ax_r) if len(bands) > 1 else bands[0]


def spread_cols(coarse, fine_cols):
    n = coarse.shape[1]
    ids = jnp.arange(fine_cols, dtype=jnp.int32) // COARSE
    onehot = (jnp.arange(n, dtype=jnp.int32)[:, None] == ids[None, :]).astype(jnp.float32)
    return jnp.dot(coarse, onehot, precision=lax.Precision.HIGHEST)


def fine_of(coarse, fine_cols):
    wide = spread_cols(coarse, fine_cols)
    rows = wide.shape[0]
    return jnp.broadcast_to(wide[:, None, :], (rows, COARSE, fine_cols)).reshape(rows * COARSE, fine_cols)


def coarse_of(fine):
    rows, cols = fine.shape
    summed_rows = jnp.sum(fine.reshape(rows // COARSE, COARSE, cols), axis=1)
    n = cols // COARSE
    ids = jnp.arange(cols, dtype=jnp.int32) // COARSE
    onehot = (ids[:, None] == jnp.arange(n, dtype=jnp.int32)[None, :]).astype(jnp.float32)
    return jnp.dot(summed_rows, onehot, precision=lax.Precision.HIGHEST) * (1.0 / (COARSE * COARSE))


def power_sweeps(drop_ext, cond_ext, load_ext, via_ext, inside):
    h = HALO
    c = cond_ext[1:-1, 1:-1]
    w_north = (c + cond_ext[:-2, 1:-1]) * 0.5
    w_south = (c + cond_ext[2:, 1:-1]) * 0.5
    w_west = (c + cond_ext[1:-1, :-2]) * 0.5
    w_east = (c + cond_ext[1:-1, 2:]) * 0.5
    denom = w_north + w_south + w_west + w_east + via_ext[1:-1, 1:-1]
    load = load_ext[1:-1, 1:-1]
    mask = inside[1:-1, 1:-1]
    d = drop_ext
    for s in range(SWEEPS):
        o = s
        e = denom.shape[0] - s
        f = denom.shape[1] - s
        sl = lambda a: a[o:e, o:f]
        summed = (
            sl(load)
            + sl(w_north) * d[:-2, 1:-1]
            + sl(w_south) * d[2:, 1:-1]
            + sl(w_west) * d[1:-1, :-2]
            + sl(w_east) * d[1:-1, 2:]
        )
        d = jnp.where(sl(mask), summed / sl(denom), 0.0)
    return d


def shift_cols(a, toward):
    zero = jnp.zeros(a.shape[:-1] + (1,), a.dtype)
    if toward == "west":
        return jnp.concatenate([zero, a[..., :-1]], axis=-1)
    return jnp.concatenate([a[..., 1:], zero], axis=-1)


def thermal_sweeps(temp_ext, source_ext, lat_ext, vert_ext, inside):
    lk = lat_ext[1:-1, 1:-1]
    vk = vert_ext[1:-1, 1:-1]
    w_north = (lk + lat_ext[1:-1, :-2]) * 0.5
    w_south = (lk + lat_ext[1:-1, 2:]) * 0.5
    w_west = (lk + shift_cols(lk, "west")) * 0.5
    w_east = (lk + shift_cols(lk, "east")) * 0.5
    w_below = (vk + vert_ext[:-2, 1:-1]) * 0.5
    w_above = (vk + vert_ext[2:, 1:-1]) * 0.5
    denom = w_north + w_south + w_west + w_east + w_below + w_above
    source = source_ext[1:-1, 1:-1]
    mask = inside[1:-1, 1:-1]
    t = temp_ext
    for s in range(HEAT_SWEEPS):
        o = s
        e0 = denom.shape[0] - s
        e1 = denom.shape[1] - s
        sl = lambda a: a[o:e0, o:e1]
        mid = t[1:-1, 1:-1]
        summed = (
            sl(source)
            + sl(w_north) * t[1:-1, :-2]
            + sl(w_south) * t[1:-1, 2:]
            + sl(w_west) * shift_cols(mid, "west")
            + sl(w_east) * shift_cols(mid, "east")
            + sl(w_below) * t[:-2, 1:-1]
            + sl(w_above) * t[2:, 1:-1]
        )
        t = jnp.where(sl(mask), summed / sl(denom), 0.0)
    return t


def body(demand, leakage, conductance, vias, layer_of, lateral_k, vertical_k):
    h = HALO
    tile_rows, tile_cols = demand.shape
    group_layers, cell_rows, therm_cols = lateral_k.shape
    cell_cols = tile_cols // COARSE
    n_r = lax.axis_size("row")
    n_c = lax.axis_size("col")
    r_idx = lax.axis_index("row")
    c_idx = lax.axis_index("col")
    all_layers = group_layers * n_c
    all_rows = cell_rows * n_r

    via_g = VIA_CONDUCT * vias.astype(jnp.float32)
    load0 = demand + leakage

    items = [
        (conductance, 0, 1, h),
        (load0, 0, 1, h),
        (via_g, 0, 1, h),
        (lateral_k, 1, 0, h),
        (vertical_k, 1, 0, h),
        (layer_of.astype(jnp.float32), 0, None, h),
    ]
    got = exchange(items)
    cond0_ext = assemble(conductance, got[0], 0, 1)
    load0_ext = assemble(load0, got[1], 0, 1)
    via_ext = assemble(via_g, got[2], 0, 1)
    lat_ext = assemble(lateral_k, got[3], 1, 0)
    vert_ext = assemble(vertical_k, got[4], 1, 0)
    layer_ext = assemble(layer_of.astype(jnp.float32), got[5], 0, None).astype(jnp.int32)

    prow = r_idx * tile_rows - h + jnp.arange(tile_rows + 2 * h, dtype=jnp.int32)
    pcol = c_idx * tile_cols - h + jnp.arange(tile_cols + 2 * h, dtype=jnp.int32)
    p_inside = ((prow >= 0) & (prow < tile_rows * n_r))[:, None] & ((pcol >= 0) & (pcol < tile_cols * n_c))[None, :]
    tlay = c_idx * group_layers - h + jnp.arange(group_layers + 2 * h, dtype=jnp.int32)
    trow = r_idx * cell_rows - h + jnp.arange(cell_rows + 2 * h, dtype=jnp.int32)
    t_inside = (((tlay >= 0) & (tlay < all_layers))[:, None] & ((trow >= 0) & (trow < all_rows))[None, :])[:, :, None]
    picker_ext = layer_ext[None, :, :] == tlay[:, None, None]
    own_layers = c_idx * group_layers + jnp.arange(group_layers, dtype=jnp.int32)
    picker_own = layer_of[None, :, :] == own_layers[:, None, None]

    drop = None
    temp = None
    drop_ext = jnp.zeros(cond0_ext.shape, jnp.float32)
    temp_ext = jnp.zeros(lat_ext.shape, jnp.float32)
    cond_ext = cond0_ext
    load_ext = load0_ext
    for outer in range(OUTER):
        if outer > 0:
            partial = jnp.sum(jnp.where(picker_own, temp, 0.0), axis=0)
            band = lax.psum(partial, "col")
            cell_temp = lax.dynamic_slice_in_dim(band, c_idx * cell_cols, cell_cols, 1)
            denom_c = 1.0 + COND_SLOPE * cell_temp
            grow_c = jnp.exp(LEAK_SLOPE * cell_temp)
            denom_f = fine_of(denom_c, tile_cols)
            grow_f = fine_of(grow_c, tile_cols)
            cond = conductance / denom_f
            load = demand + leakage * grow_f
            got = exchange([
                (drop, 0, 1, h),
                (cond, 0, 1, h),
                (load, 0, 1, h),
                (temp, 1, 0, h),
            ])
            drop_ext = assemble(drop, got[0], 0, 1)
            cond_ext = assemble(cond, got[1], 0, 1)
            load_ext = assemble(load, got[2], 0, 1)
            temp_ext = assemble(temp, got[3], 1, 0)
        drop = power_sweeps(drop_ext, cond_ext, load_ext, via_ext, p_inside)
        cond_own = cond_ext[h:-h, h:-h]
        load_own = load_ext[h:-h, h:-h]
        heat = coarse_of(load_own * (1.0 - drop) + cond_own * drop * drop)
        gathered = lax.all_gather(heat, ("row", "col"), axis=0, tiled=False)
        full = gathered.reshape(n_r, n_c, cell_rows, cell_cols).transpose(0, 2, 1, 3).reshape(all_rows, n_c * cell_cols)
        full = jnp.pad(full, ((h, h), (0, 0)))
        heat_ext = lax.dynamic_slice_in_dim(full, r_idx * cell_rows, cell_rows + 2 * h, 0)
        source_ext = jnp.where(picker_ext, heat_ext[None, :, :], 0.0)
        temp = thermal_sweeps(temp_ext, source_ext, lat_ext, vert_ext, t_inside)
    return (drop, temp)


def solution(mesh):
    in_specs = (
        P("row", "col"),
        P("row", "col"),
        P("row", "col"),
        P("row", "col"),
        P("row", None),
        P("col", "row", None),
        P("col", "row", None),
    )
    out_specs = (P("row", "col"), P("col", "row", None))
    return jax.shard_map(body, mesh=mesh, in_specs=in_specs, out_specs=out_specs, check_vma=False)
```

```python
import jax
import jax.numpy as jnp
from jax import lax
from jax.sharding import PartitionSpec as P

COARSE = 8
SWEEPS = 4
HEAT_SWEEPS = 4
OUTER = 2


COND_SLOPE = 0.5
LEAK_SLOPE = 0.7
VIA_CONDUCT = 4.0

HALO = 4


def extended(block, sides, width):
    for axis, dim in sides:
        count = lax.axis_size(axis)
        forward = [(i, i + 1) for i in range(count - 1)]
        backward = [(target, source) for source, target in forward]
        low = lax.ppermute(
            lax.slice_in_dim(block, block.shape[dim] - width, None, axis=dim), axis, forward
        )
        high = lax.ppermute(lax.slice_in_dim(block, 0, width, axis=dim), axis, backward)
        block = jnp.concatenate([low, block, high], axis=dim)
    return block


def spread_cols(coarse, fine_cols):
    n = coarse.shape[1]
    ids = jnp.arange(fine_cols, dtype=jnp.int32) // COARSE
    onehot = (jnp.arange(n, dtype=jnp.int32)[:, None] == ids[None, :]).astype(jnp.float32)
    return jnp.dot(coarse, onehot, precision=lax.Precision.HIGHEST)


def fine_of(coarse, fine_cols):
    wide = spread_cols(coarse, fine_cols)
    rows = wide.shape[0]
    return jnp.broadcast_to(wide[:, None, :], (rows, COARSE, fine_cols)).reshape(rows * COARSE, fine_cols)


def coarse_of(fine):
    rows, cols = fine.shape
    summed_rows = jnp.sum(fine.reshape(rows // COARSE, COARSE, cols), axis=1)
    n = cols // COARSE
    ids = jnp.arange(cols, dtype=jnp.int32) // COARSE
    onehot = (ids[:, None] == jnp.arange(n, dtype=jnp.int32)[None, :]).astype(jnp.float32)
    return jnp.dot(summed_rows, onehot, precision=lax.Precision.HIGHEST) * (1.0 / (COARSE * COARSE))


def power_sweeps(drop_ext, cond_ext, load_ext, via_ext, inside):
    h = HALO
    c = cond_ext[1:-1, 1:-1]
    w_north = (c + cond_ext[:-2, 1:-1]) * 0.5
    w_south = (c + cond_ext[2:, 1:-1]) * 0.5
    w_west = (c + cond_ext[1:-1, :-2]) * 0.5
    w_east = (c + cond_ext[1:-1, 2:]) * 0.5
    denom = w_north + w_south + w_west + w_east + via_ext[1:-1, 1:-1]
    load = load_ext[1:-1, 1:-1]
    mask = inside[1:-1, 1:-1]
    d = drop_ext
    for s in range(SWEEPS):
        o = s
        e = denom.shape[0] - s
        f = denom.shape[1] - s
        sl = lambda a: a[o:e, o:f]
        summed = (
            sl(load)
            + sl(w_north) * d[:-2, 1:-1]
            + sl(w_south) * d[2:, 1:-1]
            + sl(w_west) * d[1:-1, :-2]
            + sl(w_east) * d[1:-1, 2:]
        )
        d = jnp.where(sl(mask), summed / sl(denom), 0.0)
    return d


def shift_cols(a, toward):
    zero = jnp.zeros(a.shape[:-1] + (1,), a.dtype)
    if toward == "west":
        return jnp.concatenate([zero, a[..., :-1]], axis=-1)
    return jnp.concatenate([a[..., 1:], zero], axis=-1)


def thermal_sweeps(temp_ext, source_ext, lat_ext, vert_ext, inside):
    lk = lat_ext[1:-1, 1:-1]
    vk = vert_ext[1:-1, 1:-1]
    w_north = (lk + lat_ext[1:-1, :-2]) * 0.5
    w_south = (lk + lat_ext[1:-1, 2:]) * 0.5
    w_west = (lk + shift_cols(lk, "west")) * 0.5
    w_east = (lk + shift_cols(lk, "east")) * 0.5
    w_below = (vk + vert_ext[:-2, 1:-1]) * 0.5
    w_above = (vk + vert_ext[2:, 1:-1]) * 0.5
    denom = w_north + w_south + w_west + w_east + w_below + w_above
    source = source_ext[1:-1, 1:-1]
    mask = inside[1:-1, 1:-1]
    t = temp_ext
    for s in range(HEAT_SWEEPS):
        o = s
        e0 = denom.shape[0] - s
        e1 = denom.shape[1] - s
        sl = lambda a: a[o:e0, o:e1]
        mid = t[1:-1, 1:-1]
        summed = (
            sl(source)
            + sl(w_north) * t[1:-1, :-2]
            + sl(w_south) * t[1:-1, 2:]
            + sl(w_west) * shift_cols(mid, "west")
            + sl(w_east) * shift_cols(mid, "east")
            + sl(w_below) * t[:-2, 1:-1]
            + sl(w_above) * t[2:, 1:-1]
        )
        t = jnp.where(sl(mask), summed / sl(denom), 0.0)
    return t


def body(demand, leakage, conductance, vias, layer_of, lateral_k, vertical_k):
    h = HALO
    tile_rows, tile_cols = demand.shape
    group_layers, cell_rows, therm_cols = lateral_k.shape
    cell_cols = tile_cols // COARSE
    n_r = lax.axis_size("row")
    n_c = lax.axis_size("col")
    r_idx = lax.axis_index("row")
    c_idx = lax.axis_index("col")
    all_layers = group_layers * n_c
    all_rows = cell_rows * n_r

    via_g = VIA_CONDUCT * vias.astype(jnp.float32)
    load0 = demand + leakage

    power_sides = (("row", 1), ("col", 2))
    therm_sides = (("row", 2), ("col", 1))
    p_ext = extended(jnp.stack([conductance, load0, via_g]), power_sides, h)
    cond0_ext, load0_ext, via_ext = p_ext[0], p_ext[1], p_ext[2]
    k_ext = extended(jnp.stack([lateral_k, vertical_k]), therm_sides, h)
    lat_ext, vert_ext = k_ext[0], k_ext[1]
    layer_ext = extended(layer_of, (("row", 0),), h)

    prow = r_idx * tile_rows - h + jnp.arange(tile_rows + 2 * h, dtype=jnp.int32)
    pcol = c_idx * tile_cols - h + jnp.arange(tile_cols + 2 * h, dtype=jnp.int32)
    p_inside = ((prow >= 0) & (prow < tile_rows * n_r))[:, None] & ((pcol >= 0) & (pcol < tile_cols * n_c))[None, :]
    tlay = c_idx * group_layers - h + jnp.arange(group_layers + 2 * h, dtype=jnp.int32)
    trow = r_idx * cell_rows - h + jnp.arange(cell_rows + 2 * h, dtype=jnp.int32)
    t_inside = (((tlay >= 0) & (tlay < all_layers))[:, None] & ((trow >= 0) & (trow < all_rows))[None, :])[:, :, None]
    picker_ext = (layer_ext[None, :, :] == tlay[:, None, None]) & t_inside
    own_layers = c_idx * group_layers + jnp.arange(group_layers, dtype=jnp.int32)
    picker_own = layer_of[None, :, :] == own_layers[:, None, None]

    drop = None
    temp = None
    drop_ext = jnp.zeros(cond0_ext.shape, jnp.float32)
    temp_ext = jnp.zeros(lat_ext.shape, jnp.float32)
    cond_ext = cond0_ext
    load_ext = load0_ext
    for outer in range(OUTER):
        if outer > 0:
            partial = jnp.sum(jnp.where(picker_own, temp, 0.0), axis=0)
            band = lax.psum(partial, "col")
            cell_temp = lax.dynamic_slice_in_dim(band, c_idx * cell_cols, cell_cols, 1)
            denom_c = 1.0 + COND_SLOPE * cell_temp
            grow_c = jnp.exp(LEAK_SLOPE * cell_temp)
            denom_f = fine_of(denom_c, tile_cols)
            grow_f = fine_of(grow_c, tile_cols)
            cond = conductance / denom_f
            load = demand + leakage * grow_f
            p_ext = extended(jnp.stack([drop, cond, load]), power_sides, h)
            drop_ext, cond_ext, load_ext = p_ext[0], p_ext[1], p_ext[2]
            temp_ext = extended(temp, (("row", 1), ("col", 0)), h)
        drop = power_sweeps(drop_ext, cond_ext, load_ext, via_ext, p_inside)
        cond_own = cond_ext[h:-h, h:-h]
        load_own = load_ext[h:-h, h:-h]
        heat = coarse_of(load_own * (1.0 - drop) + cond_own * drop * drop)
        heat_rows = extended(heat, (("row", 0),), h)
        gathered = lax.all_gather(heat_rows, "col", axis=0, tiled=False)
        heat_ext = gathered.transpose(1, 0, 2).reshape(cell_rows + 2 * h, n_c * cell_cols)
        source_ext = jnp.where(picker_ext, heat_ext[None, :, :], 0.0)
        temp = thermal_sweeps(temp_ext, source_ext, lat_ext, vert_ext, t_inside)
    return (drop, temp)


def solution(mesh):
    in_specs = (
        P("row", "col"),
        P("row", "col"),
        P("row", "col"),
        P("row", "col"),
        P("row", None),
        P("col", "row", None),
        P("col", "row", None),
    )
    out_specs = (P("row", "col"), P("col", "row", None))
    return jax.shard_map(body, mesh=mesh, in_specs=in_specs, out_specs=out_specs, check_vma=False)
```

```python
import jax
import jax.numpy as jnp
from jax import lax
from jax.sharding import PartitionSpec as P

COARSE = 8
SWEEPS = 4
HEAT_SWEEPS = 4
OUTER = 2


COND_SLOPE = 0.5
LEAK_SLOPE = 0.7
VIA_CONDUCT = 4.0

HALO = 4


def extended(block, sides, width):
    for axis, dim in sides:
        count = lax.axis_size(axis)
        forward = [(i, i + 1) for i in range(count - 1)]
        backward = [(target, source) for source, target in forward]
        low = lax.ppermute(
            lax.slice_in_dim(block, block.shape[dim] - width, None, axis=dim), axis, forward
        )
        high = lax.ppermute(lax.slice_in_dim(block, 0, width, axis=dim), axis, backward)
        block = jnp.concatenate([low, block, high], axis=dim)
    return block


def spread_cols(coarse, fine_cols):
    n = coarse.shape[1]
    ids = jnp.arange(fine_cols, dtype=jnp.int32) // COARSE
    onehot = (jnp.arange(n, dtype=jnp.int32)[:, None] == ids[None, :]).astype(jnp.float32)
    return jnp.dot(coarse, onehot, precision=lax.Precision.HIGHEST)


def fine_of(coarse, fine_cols):
    wide = spread_cols(coarse, fine_cols)
    rows = wide.shape[0]
    return jnp.broadcast_to(wide[:, None, :], (rows, COARSE, fine_cols)).reshape(rows * COARSE, fine_cols)


def coarse_of(fine):
    rows, cols = fine.shape
    summed_rows = jnp.sum(fine.reshape(rows // COARSE, COARSE, cols), axis=1)
    n = cols // COARSE
    ids = jnp.arange(cols, dtype=jnp.int32) // COARSE
    onehot = (ids[:, None] == jnp.arange(n, dtype=jnp.int32)[None, :]).astype(jnp.float32)
    return jnp.dot(summed_rows, onehot, precision=lax.Precision.HIGHEST) * (1.0 / (COARSE * COARSE))


def power_sweeps(drop_ext, cond_ext, load_ext, via_ext, inside):
    h = HALO
    c = cond_ext[1:-1, 1:-1]
    w_north = (c + cond_ext[:-2, 1:-1]) * 0.5
    w_south = (c + cond_ext[2:, 1:-1]) * 0.5
    w_west = (c + cond_ext[1:-1, :-2]) * 0.5
    w_east = (c + cond_ext[1:-1, 2:]) * 0.5
    denom = w_north + w_south + w_west + w_east + via_ext[1:-1, 1:-1]
    load = load_ext[1:-1, 1:-1]
    mask = inside[1:-1, 1:-1]
    d = drop_ext
    for s in range(SWEEPS):
        o = s
        e = denom.shape[0] - s
        f = denom.shape[1] - s
        sl = lambda a: a[o:e, o:f]
        summed = (
            sl(load)
            + sl(w_north) * d[:-2, 1:-1]
            + sl(w_south) * d[2:, 1:-1]
            + sl(w_west) * d[1:-1, :-2]
            + sl(w_east) * d[1:-1, 2:]
        )
        d = jnp.where(sl(mask), summed / sl(denom), 0.0)
    return d


def shift_cols(a, toward):
    zero = jnp.zeros(a.shape[:-1] + (1,), a.dtype)
    if toward == "west":
        return jnp.concatenate([zero, a[..., :-1]], axis=-1)
    return jnp.concatenate([a[..., 1:], zero], axis=-1)


def thermal_sweeps(temp_ext, source_ext, lat_ext, vert_ext, inside):
    lk = lat_ext[1:-1, 1:-1]
    vk = vert_ext[1:-1, 1:-1]
    w_north = (lk + lat_ext[1:-1, :-2]) * 0.5
    w_south = (lk + lat_ext[1:-1, 2:]) * 0.5
    w_west = (lk + shift_cols(lk, "west")) * 0.5
    w_east = (lk + shift_cols(lk, "east")) * 0.5
    w_below = (vk + vert_ext[:-2, 1:-1]) * 0.5
    w_above = (vk + vert_ext[2:, 1:-1]) * 0.5
    denom = w_north + w_south + w_west + w_east + w_below + w_above
    source = source_ext[1:-1, 1:-1]
    mask = inside[1:-1, 1:-1]
    t = temp_ext
    for s in range(HEAT_SWEEPS):
        o = s
        e0 = denom.shape[0] - s
        e1 = denom.shape[1] - s
        sl = lambda a: a[o:e0, o:e1]
        mid = t[1:-1, 1:-1]
        summed = (
            sl(source)
            + sl(w_north) * t[1:-1, :-2]
            + sl(w_south) * t[1:-1, 2:]
            + sl(w_west) * shift_cols(mid, "west")
            + sl(w_east) * shift_cols(mid, "east")
            + sl(w_below) * t[:-2, 1:-1]
            + sl(w_above) * t[2:, 1:-1]
        )
        t = jnp.where(sl(mask), summed / sl(denom), 0.0)
    return t


def body(demand, leakage, conductance, vias, layer_of, lateral_k, vertical_k):
    h = HALO
    tile_rows, tile_cols = demand.shape
    group_layers, cell_rows, therm_cols = lateral_k.shape
    cell_cols = tile_cols // COARSE
    n_r = lax.axis_size("row")
    n_c = lax.axis_size("col")
    r_idx = lax.axis_index("row")
    c_idx = lax.axis_index("col")
    all_layers = group_layers * n_c
    all_rows = cell_rows * n_r

    via_g = VIA_CONDUCT * vias.astype(jnp.float32)
    load0 = demand + leakage

    power_sides = (("row", 1), ("col", 2))
    therm_sides = (("row", 2), ("col", 1))
    p_ext = extended(jnp.stack([conductance, load0, via_g]), power_sides, h)
    cond0_ext, load0_ext, via_ext = p_ext[0], p_ext[1], p_ext[2]
    k_ext = extended(jnp.stack([lateral_k, vertical_k]), therm_sides, h)
    lat_ext, vert_ext = k_ext[0], k_ext[1]
    layer_ext = extended(layer_of, (("row", 0),), h)

    prow = r_idx * tile_rows - h + jnp.arange(tile_rows + 2 * h, dtype=jnp.int32)
    pcol = c_idx * tile_cols - h + jnp.arange(tile_cols + 2 * h, dtype=jnp.int32)
    p_inside = ((prow >= 0) & (prow < tile_rows * n_r))[:, None] & ((pcol >= 0) & (pcol < tile_cols * n_c))[None, :]
    tlay = c_idx * group_layers - h + jnp.arange(group_layers + 2 * h, dtype=jnp.int32)
    trow = r_idx * cell_rows - h + jnp.arange(cell_rows + 2 * h, dtype=jnp.int32)
    t_inside = (((tlay >= 0) & (tlay < all_layers))[:, None] & ((trow >= 0) & (trow < all_rows))[None, :])[:, :, None]
    picker_ext = (layer_ext[None, :, :] == tlay[:, None, None]) & t_inside
    own_layers = c_idx * group_layers + jnp.arange(group_layers, dtype=jnp.int32)
    picker_own = layer_of[None, :, :] == own_layers[:, None, None]

    drop = None
    temp = None
    drop_ext = jnp.zeros(cond0_ext.shape, jnp.float32)
    temp_ext = jnp.zeros(lat_ext.shape, jnp.float32)
    cond_ext = cond0_ext
    load_ext = load0_ext
    for outer in range(OUTER):
        if outer > 0:
            partial = jnp.sum(jnp.where(picker_own, temp, 0.0), axis=0)
            parts = partial.reshape(cell_rows, n_c, cell_cols).transpose(1, 0, 2)
            parts = lax.all_to_all(parts, "col", split_axis=0, concat_axis=0, tiled=True)
            cell_temp = jnp.sum(parts, axis=0)
            denom_c = 1.0 + COND_SLOPE * cell_temp
            grow_c = jnp.exp(LEAK_SLOPE * cell_temp)
            denom_f = fine_of(denom_c, tile_cols)
            grow_f = fine_of(grow_c, tile_cols)
            cond = conductance / denom_f
            load = demand + leakage * grow_f
            p_ext = extended(jnp.stack([drop, cond, load]), power_sides, h)
            drop_ext, cond_ext, load_ext = p_ext[0], p_ext[1], p_ext[2]
            temp_ext = extended(temp, (("row", 1), ("col", 0)), h)
        drop = power_sweeps(drop_ext, cond_ext, load_ext, via_ext, p_inside)
        cond_own = cond_ext[h:-h, h:-h]
        load_own = load_ext[h:-h, h:-h]
        heat = coarse_of(load_own * (1.0 - drop) + cond_own * drop * drop)
        heat_rows = extended(heat, (("row", 0),), h)
        copies = jnp.broadcast_to(heat_rows[None], (n_c,) + heat_rows.shape)
        gathered = lax.all_to_all(copies, "col", split_axis=0, concat_axis=0, tiled=True)
        heat_ext = gathered.transpose(1, 0, 2).reshape(cell_rows + 2 * h, n_c * cell_cols)
        source_ext = jnp.where(picker_ext, heat_ext[None, :, :], 0.0)
        temp = thermal_sweeps(temp_ext, source_ext, lat_ext, vert_ext, t_inside)
    return (drop, temp)


def solution(mesh):
    in_specs = (
        P("row", "col"),
        P("row", "col"),
        P("row", "col"),
        P("row", "col"),
        P("row", None),
        P("col", "row", None),
        P("col", "row", None),
    )
    out_specs = (P("row", "col"), P("col", "row", None))
    return jax.shard_map(body, mesh=mesh, in_specs=in_specs, out_specs=out_specs, check_vma=False)
```

```python
import jax
import jax.numpy as jnp
from jax import lax
from jax.sharding import PartitionSpec as P

COARSE = 8
SWEEPS = 4
HEAT_SWEEPS = 4
OUTER = 2


COND_SLOPE = 0.5
LEAK_SLOPE = 0.7
VIA_CONDUCT = 4.0

HALO = 4


def extended(block, sides):
    for axis, dim, width in sides:
        count = lax.axis_size(axis)
        forward = [(i, i + 1) for i in range(count - 1)]
        backward = [(target, source) for source, target in forward]
        low = lax.ppermute(
            lax.slice_in_dim(block, block.shape[dim] - width, None, axis=dim), axis, forward
        )
        high = lax.ppermute(lax.slice_in_dim(block, 0, width, axis=dim), axis, backward)
        block = jnp.concatenate([low, block, high], axis=dim)
    return block


def spread_cols(coarse, fine_cols):
    n = coarse.shape[1]
    ids = jnp.arange(fine_cols, dtype=jnp.int32) // COARSE
    onehot = (jnp.arange(n, dtype=jnp.int32)[:, None] == ids[None, :]).astype(jnp.float32)
    return jnp.dot(coarse, onehot, precision=lax.Precision.HIGHEST)


def fine_of(coarse, fine_cols):
    wide = spread_cols(coarse, fine_cols)
    rows = wide.shape[0]
    return jnp.broadcast_to(wide[:, None, :], (rows, COARSE, fine_cols)).reshape(rows * COARSE, fine_cols)


def coarse_of(fine):
    rows, cols = fine.shape
    summed_rows = jnp.sum(fine.reshape(rows // COARSE, COARSE, cols), axis=1)
    n = cols // COARSE
    ids = jnp.arange(cols, dtype=jnp.int32) // COARSE
    onehot = (ids[:, None] == jnp.arange(n, dtype=jnp.int32)[None, :]).astype(jnp.float32)
    return jnp.dot(summed_rows, onehot, precision=lax.Precision.HIGHEST) * (1.0 / (COARSE * COARSE))


def power_sweeps(drop_ext, cond_ext, load_ext, via_ext, inside):
    h = HALO
    c = cond_ext[1:-1, 1:-1]
    w_north = (c + cond_ext[:-2, 1:-1]) * 0.5
    w_south = (c + cond_ext[2:, 1:-1]) * 0.5
    w_west = (c + cond_ext[1:-1, :-2]) * 0.5
    w_east = (c + cond_ext[1:-1, 2:]) * 0.5
    denom = w_north + w_south + w_west + w_east + via_ext[1:-1, 1:-1]
    load = load_ext[1:-1, 1:-1]
    mask = inside[1:-1, 1:-1]
    d = drop_ext
    for s in range(SWEEPS):
        o = s
        e = denom.shape[0] - s
        f = denom.shape[1] - s
        sl = lambda a: a[o:e, o:f]
        summed = (
            sl(load)
            + sl(w_north) * d[:-2, 1:-1]
            + sl(w_south) * d[2:, 1:-1]
            + sl(w_west) * d[1:-1, :-2]
            + sl(w_east) * d[1:-1, 2:]
        )
        d = jnp.where(sl(mask), summed / sl(denom), 0.0)
    return d


def shift_cols(a, toward):
    zero = jnp.zeros(a.shape[:-1] + (1,), a.dtype)
    if toward == "west":
        return jnp.concatenate([zero, a[..., :-1]], axis=-1)
    return jnp.concatenate([a[..., 1:], zero], axis=-1)


def thermal_sweeps(temp_ext, source_in, lat_ext, vert_ext, inside):
    lk = lat_ext[1:-1, 1:-1]
    vk = vert_ext[1:-1, 1:-1]
    w_north = (lk + lat_ext[1:-1, :-2]) * 0.5
    w_south = (lk + lat_ext[1:-1, 2:]) * 0.5
    w_west = (lk + shift_cols(lk, "west")) * 0.5
    w_east = (lk + shift_cols(lk, "east")) * 0.5
    w_below = (vk + vert_ext[:-2, 1:-1]) * 0.5
    w_above = (vk + vert_ext[2:, 1:-1]) * 0.5
    denom = w_north + w_south + w_west + w_east + w_below + w_above
    source = source_in
    mask = inside[1:-1, 1:-1]
    t = temp_ext
    for s in range(HEAT_SWEEPS):
        o = s
        e0 = denom.shape[0] - s
        e1 = denom.shape[1] - s
        sl = lambda a: a[o:e0, o:e1]
        mid = t[1:-1, 1:-1]
        summed = (
            sl(source)
            + sl(w_north) * t[1:-1, :-2]
            + sl(w_south) * t[1:-1, 2:]
            + sl(w_west) * shift_cols(mid, "west")
            + sl(w_east) * shift_cols(mid, "east")
            + sl(w_below) * t[:-2, 1:-1]
            + sl(w_above) * t[2:, 1:-1]
        )
        t = jnp.where(sl(mask), summed / sl(denom), 0.0)
    return t


def power_mask(r0, c0, rows, cols, total_rows, total_cols):
    prow = r0 + jnp.arange(rows, dtype=jnp.int32)
    pcol = c0 + jnp.arange(cols, dtype=jnp.int32)
    return ((prow >= 0) & (prow < total_rows))[:, None] & ((pcol >= 0) & (pcol < total_cols))[None, :]


def body(demand, leakage, conductance, vias, layer_of, lateral_k, vertical_k):
    tile_rows, tile_cols = demand.shape
    group_layers, cell_rows, therm_cols = lateral_k.shape
    cell_cols = tile_cols // COARSE
    n_r = lax.axis_size("row")
    n_c = lax.axis_size("col")
    r_idx = lax.axis_index("row")
    c_idx = lax.axis_index("col")
    all_layers = group_layers * n_c
    all_rows = cell_rows * n_r
    total_rows = tile_rows * n_r
    total_cols = tile_cols * n_c

    T0 = 2 * HEAT_SWEEPS
    T1 = HEAT_SWEEPS
    H0 = T0 - 1
    H1 = T1 - 1
    S = SWEEPS
    R1 = H1 * COARSE + SWEEPS
    R0 = max(H0 * COARSE, R1) + SWEEPS
    C0 = 2 * S
    PR = -(-R1 // COARSE)

    via_g = VIA_CONDUCT * vias.astype(jnp.float32)
    load0 = demand + leakage

    p0 = extended(jnp.stack([conductance, load0, via_g]), (("row", 1, R0), ("col", 2, C0)))
    p1 = extended(jnp.stack([demand, leakage]), (("row", 1, R1), ("col", 2, S)))
    k_ext = extended(jnp.stack([lateral_k, vertical_k]), (("row", 2, T0), ("col", 1, T0)))
    layer_ext = extended(layer_of, (("row", 0, T0),))

    rows0 = tile_rows + 2 * R0
    cols0 = tile_cols + 2 * C0
    mask0 = power_mask(r_idx * tile_rows - R0, c_idx * tile_cols - C0, rows0, cols0, total_rows, total_cols)
    drop0 = power_sweeps(jnp.zeros((rows0, cols0), jnp.float32), p0[0], p0[1], p0[2], mask0)
    hr0 = H0 * COARSE
    a = R0 - S - hr0
    rows_h0 = tile_rows + 2 * hr0
    d_h = drop0[a:a + rows_h0, S:S + tile_cols]
    c_h = p0[0][R0 - hr0:R0 - hr0 + rows_h0, C0:C0 + tile_cols]
    l_h = p0[1][R0 - hr0:R0 - hr0 + rows_h0, C0:C0 + tile_cols]
    heat0 = coarse_of(l_h * (1.0 - d_h) + c_h * d_h * d_h)

    def gather_heat(heat):
        copies = jnp.broadcast_to(heat[None], (n_c,) + heat.shape)
        gathered = lax.all_to_all(copies, "col", split_axis=0, concat_axis=0, tiled=True)
        return gathered.transpose(1, 0, 2).reshape(heat.shape[0], n_c * cell_cols)

    def thermal(temp_ext, heat_ext, halo_in, halo_out):
        inner = halo_in - 1
        ks = k_ext[:, T0 - halo_in:T0 + group_layers + halo_in, T0 - halo_in:T0 + cell_rows + halo_in]
        tlay = c_idx * group_layers - halo_in + jnp.arange(group_layers + 2 * halo_in, dtype=jnp.int32)
        trow = r_idx * cell_rows - halo_in + jnp.arange(cell_rows + 2 * halo_in, dtype=jnp.int32)
        inside = (((tlay >= 0) & (tlay < all_layers))[:, None] & ((trow >= 0) & (trow < all_rows))[None, :])[:, :, None]
        lay_in = layer_ext[T0 - inner:T0 + cell_rows + inner]
        picker = (lay_in[None, :, :] == tlay[1:-1, None, None]) & inside[1:-1, 1:-1]
        source = jnp.where(picker, heat_ext[None, :, :], 0.0)
        return thermal_sweeps(temp_ext, source, ks[0], ks[1], inside)

    heat0_ext = gather_heat(heat0)
    temp0 = thermal(jnp.zeros((group_layers + 2 * T0, cell_rows + 2 * T0, therm_cols), jnp.float32), heat0_ext, T0, T1)

    own_layers = c_idx * group_layers + jnp.arange(group_layers, dtype=jnp.int32)
    t_own = temp0[T1:T1 + group_layers, T1 - PR:T1 + cell_rows + PR]
    lay_w = layer_ext[T0 - PR:T0 + cell_rows + PR]
    partial = jnp.sum(jnp.where(lay_w[None, :, :] == own_layers[:, None, None], t_own, 0.0), axis=0)
    partial = jnp.pad(partial, ((0, 0), (1, 1)))
    windows = jnp.stack([partial[:, j * cell_cols:j * cell_cols + cell_cols + 2] for j in range(n_c)])
    windows = lax.all_to_all(windows, "col", split_axis=0, concat_axis=0, tiled=True)
    cell_temp = jnp.sum(windows, axis=0)

    denom_c = 1.0 + COND_SLOPE * cell_temp
    grow_c = jnp.exp(LEAK_SLOPE * cell_temp)
    rows1 = tile_rows + 2 * R1
    cols1 = tile_cols + 2 * S
    fo = PR * COARSE - R1
    denom_f = fine_of(denom_c, tile_cols + 2 * COARSE)[fo:fo + rows1, COARSE - S:COARSE - S + cols1]
    grow_f = fine_of(grow_c, tile_cols + 2 * COARSE)[fo:fo + rows1, COARSE - S:COARSE - S + cols1]
    cond1 = p0[0][R0 - R1:R0 - R1 + rows1, C0 - S:C0 - S + cols1] / denom_f
    load1 = p1[0] + p1[1] * grow_f
    via1 = p0[2][R0 - R1:R0 - R1 + rows1, C0 - S:C0 - S + cols1]
    b = R0 - S - R1
    drop_start = drop0[b:b + rows1, :]
    mask1 = power_mask(r_idx * tile_rows - R1, c_idx * tile_cols - S, rows1, cols1, total_rows, total_cols)
    drop1 = power_sweeps(drop_start, cond1, load1, via1, mask1)
    hr1 = H1 * COARSE
    c_h1 = cond1[S:S + tile_rows + 2 * hr1, S:S + tile_cols]
    l_h1 = load1[S:S + tile_rows + 2 * hr1, S:S + tile_cols]
    heat1 = coarse_of(l_h1 * (1.0 - drop1) + c_h1 * drop1 * drop1)
    heat1_ext = gather_heat(heat1)
    temp1 = thermal(temp0, heat1_ext, T1, 0)
    drop_out = drop1[hr1:hr1 + tile_rows]
    return (drop_out, temp1)


def solution(mesh):
    in_specs = (
        P("row", "col"),
        P("row", "col"),
        P("row", "col"),
        P("row", "col"),
        P("row", None),
        P("col", "row", None),
        P("col", "row", None),
    )
    out_specs = (P("row", "col"), P("col", "row", None))
    return jax.shard_map(body, mesh=mesh, in_specs=in_specs, out_specs=out_specs, check_vma=False)
```

```python
import os

import jax
import jax.numpy as jnp
from jax import lax
from jax.experimental import pallas as pl
from jax.experimental.pallas import tpu as pltpu
from jax.sharding import PartitionSpec as P

INTERPRET = os.environ.get("SOL_INTERPRET") == "1"

COARSE = 8
SWEEPS = 4
HEAT_SWEEPS = 4
OUTER = 2


COND_SLOPE = 0.5
LEAK_SLOPE = 0.7
VIA_CONDUCT = 4.0

HALO = 4


def extended(block, sides):
    for axis, dim, width in sides:
        count = lax.axis_size(axis)
        forward = [(i, i + 1) for i in range(count - 1)]
        backward = [(target, source) for source, target in forward]
        low = lax.ppermute(
            lax.slice_in_dim(block, block.shape[dim] - width, None, axis=dim), axis, forward
        )
        high = lax.ppermute(lax.slice_in_dim(block, 0, width, axis=dim), axis, backward)
        block = jnp.concatenate([low, block, high], axis=dim)
    return block


def spread_cols(coarse, fine_cols):
    n = coarse.shape[1]
    ids = jnp.arange(fine_cols, dtype=jnp.int32) // COARSE
    onehot = (jnp.arange(n, dtype=jnp.int32)[:, None] == ids[None, :]).astype(jnp.float32)
    return jnp.dot(coarse, onehot, precision=lax.Precision.HIGHEST)


def fine_of(coarse, fine_cols):
    wide = spread_cols(coarse, fine_cols)
    rows = wide.shape[0]
    return jnp.broadcast_to(wide[:, None, :], (rows, COARSE, fine_cols)).reshape(rows * COARSE, fine_cols)


def coarse_of(fine):
    rows, cols = fine.shape
    summed_rows = jnp.sum(fine.reshape(rows // COARSE, COARSE, cols), axis=1)
    n = cols // COARSE
    ids = jnp.arange(cols, dtype=jnp.int32) // COARSE
    onehot = (ids[:, None] == jnp.arange(n, dtype=jnp.int32)[None, :]).astype(jnp.float32)
    return jnp.dot(summed_rows, onehot, precision=lax.Precision.HIGHEST) * (1.0 / (COARSE * COARSE))


def row_above(x, above):
    sub = lax.broadcasted_iota(jnp.int32, x.shape, 0)
    return jnp.where(sub == 0, pltpu.roll(above, 1, 0), pltpu.roll(x, 1, 0))


def row_below(x, below):
    n = x.shape[0]
    sub = lax.broadcasted_iota(jnp.int32, x.shape, 0)
    return jnp.where(sub == n - 1, pltpu.roll(below, n - 1, 0), pltpu.roll(x, n - 1, 0))


def rows_of(k):
    return pl.ds(pl.multiple_of(k * 8, 8), 8)


def chunk(ref, k, count):
    return ref[rows_of(jnp.clip(k, 0, count - 1)), :]


def power_kernel(d_ref, c_ref, l_ref, v_ref, rok_ref, cok_ref, o_ref, wn_ref, ws_ref, ww_ref, we_ref, den_ref, buf_ref):
    n, w = c_ref.shape
    count = n // 8

    def weights(k, carry):
        sl = rows_of(k)
        x = c_ref[sl, :]
        a = (x + row_above(x, chunk(c_ref, k - 1, count))) * 0.5
        b = (x + row_below(x, chunk(c_ref, k + 1, count))) * 0.5
        e = (x + pltpu.roll(x, 1, 1)) * 0.5
        f = (x + pltpu.roll(x, w - 1, 1)) * 0.5
        wn_ref[sl, :] = a
        ws_ref[sl, :] = b
        ww_ref[sl, :] = e
        we_ref[sl, :] = f
        den_ref[sl, :] = a + b + e + f + v_ref[sl, :]
        return carry

    lax.fori_loop(0, count, weights, 0)
    col_ok = cok_ref[...] > 0.5

    def sweep(src, dst):
        def body(k, carry):
            sl = rows_of(k)
            x = src[sl, :]
            summed = (
                l_ref[sl, :]
                + wn_ref[sl, :] * row_above(x, chunk(src, k - 1, count))
                + ws_ref[sl, :] * row_below(x, chunk(src, k + 1, count))
                + ww_ref[sl, :] * pltpu.roll(x, 1, 1)
                + we_ref[sl, :] * pltpu.roll(x, w - 1, 1)
            )
            ok = (rok_ref[sl, :] > 0.5) & col_ok
            dst[sl, :] = jnp.where(ok, summed / den_ref[sl, :], 0.0)
            return carry

        lax.fori_loop(0, count, body, 0)

    sweep(d_ref, buf_ref)
    sweep(buf_ref, o_ref)
    sweep(o_ref, buf_ref)
    sweep(buf_ref, o_ref)


def run_power(drop, cond, load, via, row_ok, col_ok):
    n, w = cond.shape
    return pl.pallas_call(
        power_kernel,
        out_shape=jax.ShapeDtypeStruct((n, w), jnp.float32),
        scratch_shapes=[pltpu.VMEM((n, w), jnp.float32) for _ in range(6)],
        compiler_params=pltpu.CompilerParams(vmem_limit_bytes=60 * 1024 * 1024),
        interpret=INTERPRET,
    )(drop, cond, load, via, row_ok, col_ok)


def thermal_kernel(t_ref, s_ref, lk_ref, vk_ref, rok_ref, o_ref, wb_ref, wa_ref, den_ref, buf_ref, *, stride):
    n, w = lk_ref.shape
    count = n // 8
    lane = lax.broadcasted_iota(jnp.int32, (8, w), 1)
    first = lane == 0
    last = lane == w - 1

    def lateral(x, k, ref):
        up = row_above(x, chunk(ref, k - 1, count))
        dn = row_below(x, chunk(ref, k + 1, count))
        lf = jnp.where(first, 0.0, pltpu.roll(x, 1, 1))
        rt = jnp.where(last, 0.0, pltpu.roll(x, w - 1, 1))
        return up, dn, lf, rt

    def weights(k, carry):
        sl = rows_of(k)
        x = lk_ref[sl, :]
        up, dn, lf, rt = lateral(x, k, lk_ref)
        v = vk_ref[sl, :]
        b = (v + chunk(vk_ref, k - stride, count)) * 0.5
        a = (v + chunk(vk_ref, k + stride, count)) * 0.5
        wb_ref[sl, :] = b
        wa_ref[sl, :] = a
        den_ref[sl, :] = (x + up) * 0.5 + (x + dn) * 0.5 + (x + lf) * 0.5 + (x + rt) * 0.5 + b + a
        return carry

    lax.fori_loop(0, count, weights, 0)

    def sweep(src, dst):
        def body(k, carry):
            sl = rows_of(k)
            lk = lk_ref[sl, :]
            kup, kdn, klf, krt = lateral(lk, k, lk_ref)
            x = src[sl, :]
            up, dn, lf, rt = lateral(x, k, src)
            summed = (
                s_ref[sl, :]
                + (lk + kup) * 0.5 * up
                + (lk + kdn) * 0.5 * dn
                + (lk + klf) * 0.5 * lf
                + (lk + krt) * 0.5 * rt
                + wb_ref[sl, :] * chunk(src, k - stride, count)
                + wa_ref[sl, :] * chunk(src, k + stride, count)
            )
            dst[sl, :] = jnp.where(rok_ref[sl, :] > 0.5, summed / den_ref[sl, :], 0.0)
            return carry

        lax.fori_loop(0, count, body, 0)

    sweep(t_ref, buf_ref)
    sweep(buf_ref, o_ref)
    sweep(o_ref, buf_ref)
    sweep(buf_ref, o_ref)


def run_thermal(temp, source, lat, vert, row_ok, stride):
    n, w = lat.shape
    return pl.pallas_call(
        lambda *refs: thermal_kernel(*refs, stride=stride),
        out_shape=jax.ShapeDtypeStruct((n, w), jnp.float32),
        scratch_shapes=[pltpu.VMEM((n, w), jnp.float32) for _ in range(4)],
        compiler_params=pltpu.CompilerParams(vmem_limit_bytes=60 * 1024 * 1024),
        interpret=INTERPRET,
    )(temp, source, lat, vert, row_ok)


def inside_of(start, count, total):
    idx = start + jnp.arange(count, dtype=jnp.int32)
    return (idx >= 0) & (idx < total)


def body(demand, leakage, conductance, vias, layer_of, lateral_k, vertical_k):
    tile_rows, tile_cols = demand.shape
    group_layers, cell_rows, therm_cols = lateral_k.shape
    cell_cols = tile_cols // COARSE
    n_r = lax.axis_size("row")
    n_c = lax.axis_size("col")
    r_idx = lax.axis_index("row")
    c_idx = lax.axis_index("col")
    all_layers = group_layers * n_c
    all_rows = cell_rows * n_r
    total_rows = tile_rows * n_r
    total_cols = tile_cols * n_c

    T0 = 2 * HEAT_SWEEPS
    T1 = HEAT_SWEEPS
    H0 = T0 - 1
    H1 = T1 - 1
    S = SWEEPS
    R1 = H1 * COARSE + SWEEPS
    R0 = max(H0 * COARSE, R1) + SWEEPS
    CW = 64
    PR = -(-R1 // COARSE)
    PC = CW // COARSE

    via_g = VIA_CONDUCT * vias.astype(jnp.float32)
    load0 = demand + leakage

    p0 = extended(jnp.stack([conductance, load0, via_g]), (("row", 1, R0), ("col", 2, CW)))
    p1 = extended(jnp.stack([demand, leakage]), (("row", 1, R1), ("col", 2, CW)))
    k_ext = extended(jnp.stack([lateral_k, vertical_k]), (("row", 2, T0), ("col", 1, T0)))
    layer_ext = extended(layer_of, (("row", 0, T0),))

    cols_w = tile_cols + 2 * CW
    col_ok = inside_of(c_idx * tile_cols - CW, cols_w, total_cols).astype(jnp.float32)[None, :]

    rows0 = tile_rows + 2 * R0
    row_ok0 = inside_of(r_idx * tile_rows - R0, rows0, total_rows).astype(jnp.float32)[:, None]
    drop0 = run_power(jnp.zeros((rows0, cols_w), jnp.float32), p0[0], p0[1], p0[2], row_ok0, col_ok)
    hr0 = H0 * COARSE
    rs = slice(R0 - hr0, R0 + tile_rows + hr0)
    cs = slice(CW, CW + tile_cols)
    d_h = drop0[rs, cs]
    heat0 = coarse_of(p0[1][rs, cs] * (1.0 - d_h) + p0[0][rs, cs] * d_h * d_h)

    def gather_heat(heat):
        copies = jnp.broadcast_to(heat[None], (n_c,) + heat.shape)
        gathered = lax.all_to_all(copies, "col", split_axis=0, concat_axis=0, tiled=True)
        gathered = gathered.transpose(1, 0, 2).reshape(heat.shape[0], n_c * cell_cols)
        return jnp.pad(gathered, ((1, 1), (0, 0)))

    def thermal(temp_ext, heat_ext, halo):
        layers = group_layers + 2 * halo
        rows = cell_rows + 2 * halo
        ks = k_ext[:, T0 - halo:T0 + group_layers + halo, T0 - halo:T0 + cell_rows + halo]
        tlay = c_idx * group_layers - halo + jnp.arange(layers, dtype=jnp.int32)
        inside = inside_of(c_idx * group_layers - halo, layers, all_layers)[:, None] & inside_of(r_idx * cell_rows - halo, rows, all_rows)[None, :]
        lay_in = layer_ext[T0 - halo:T0 + cell_rows + halo]
        picker = (lay_in[None, :, :] == tlay[:, None, None]) & inside[:, :, None]
        source = jnp.where(picker, heat_ext[None, :, :], 0.0)
        flat = (layers * rows, therm_cols)
        out = run_thermal(
            temp_ext.reshape(flat), source.reshape(flat), ks[0].reshape(flat), ks[1].reshape(flat),
            inside.astype(jnp.float32).reshape(layers * rows, 1), rows // 8,
        )
        return out.reshape(layers, rows, therm_cols)

    temp0 = thermal(jnp.zeros((group_layers + 2 * T0, cell_rows + 2 * T0, therm_cols), jnp.float32), gather_heat(heat0), T0)
    temp0 = temp0[T0 - T1:T0 + group_layers + T1, T0 - T1:T0 + cell_rows + T1]

    own_layers = c_idx * group_layers + jnp.arange(group_layers, dtype=jnp.int32)
    t_own = temp0[T1:T1 + group_layers, T1 - PR:T1 + cell_rows + PR]
    lay_w = layer_ext[T0 - PR:T0 + cell_rows + PR]
    partial = jnp.sum(jnp.where(lay_w[None, :, :] == own_layers[:, None, None], t_own, 0.0), axis=0)
    partial = jnp.pad(partial, ((0, 0), (PC, PC)))
    windows = jnp.stack([partial[:, j * cell_cols:j * cell_cols + cell_cols + 2 * PC] for j in range(n_c)])
    windows = lax.all_to_all(windows, "col", split_axis=0, concat_axis=0, tiled=True)
    cell_temp = jnp.sum(windows, axis=0)

    denom_c = 1.0 + COND_SLOPE * cell_temp
    grow_c = jnp.exp(LEAK_SLOPE * cell_temp)
    rows1 = tile_rows + 2 * R1
    fo = PR * COARSE - R1
    denom_f = fine_of(denom_c, cols_w)[fo:fo + rows1]
    grow_f = fine_of(grow_c, cols_w)[fo:fo + rows1]
    rs1 = slice(R0 - R1, R0 - R1 + rows1)
    cond1 = p0[0][rs1] / denom_f
    load1 = p1[0] + p1[1] * grow_f
    row_ok1 = inside_of(r_idx * tile_rows - R1, rows1, total_rows).astype(jnp.float32)[:, None]
    drop1 = run_power(drop0[rs1], cond1, load1, p0[2][rs1], row_ok1, col_ok)
    hr1 = H1 * COARSE
    rh = slice(R1 - hr1, R1 + tile_rows + hr1)
    d_h1 = drop1[rh, cs]
    heat1 = coarse_of(load1[rh, cs] * (1.0 - d_h1) + cond1[rh, cs] * d_h1 * d_h1)
    temp1 = thermal(temp0, gather_heat(heat1), T1)
    temp_out = temp1[T1:T1 + group_layers, T1:T1 + cell_rows]
    drop_out = drop1[R1:R1 + tile_rows, cs]
    return (drop_out, temp_out)


def solution(mesh):
    in_specs = (
        P("row", "col"),
        P("row", "col"),
        P("row", "col"),
        P("row", "col"),
        P("row", None),
        P("col", "row", None),
        P("col", "row", None),
    )
    out_specs = (P("row", "col"), P("col", "row", None))
    return jax.shard_map(body, mesh=mesh, in_specs=in_specs, out_specs=out_specs, check_vma=False)
```

```python
import functools
import os

import jax
import jax.numpy as jnp
from jax import lax
from jax.experimental import pallas as pl
from jax.experimental.pallas import tpu as pltpu
from jax.sharding import PartitionSpec as P

INTERPRET = os.environ.get("SOL_INTERPRET") == "1"

COARSE = 8
SWEEPS = 4
HEAT_SWEEPS = 4
OUTER = 2


COND_SLOPE = 0.5
LEAK_SLOPE = 0.7
VIA_CONDUCT = 4.0

HALO = 4


def extended(block, sides):
    for axis, dim, width in sides:
        count = lax.axis_size(axis)
        forward = [(i, i + 1) for i in range(count - 1)]
        backward = [(target, source) for source, target in forward]
        low = lax.ppermute(
            lax.slice_in_dim(block, block.shape[dim] - width, None, axis=dim), axis, forward
        )
        high = lax.ppermute(lax.slice_in_dim(block, 0, width, axis=dim), axis, backward)
        block = jnp.concatenate([low, block, high], axis=dim)
    return block


def spread_cols(coarse, fine_cols):
    n = coarse.shape[1]
    ids = jnp.arange(fine_cols, dtype=jnp.int32) // COARSE
    onehot = (jnp.arange(n, dtype=jnp.int32)[:, None] == ids[None, :]).astype(jnp.float32)
    return jnp.dot(coarse, onehot, precision=lax.Precision.HIGHEST)


def fine_of(coarse, fine_cols):
    wide = spread_cols(coarse, fine_cols)
    rows = wide.shape[0]
    return jnp.broadcast_to(wide[:, None, :], (rows, COARSE, fine_cols)).reshape(rows * COARSE, fine_cols)


def coarse_of(fine):
    rows, cols = fine.shape
    summed_rows = jnp.sum(fine.reshape(rows // COARSE, COARSE, cols), axis=1)
    n = cols // COARSE
    ids = jnp.arange(cols, dtype=jnp.int32) // COARSE
    onehot = (ids[:, None] == jnp.arange(n, dtype=jnp.int32)[None, :]).astype(jnp.float32)
    return jnp.dot(summed_rows, onehot, precision=lax.Precision.HIGHEST) * (1.0 / (COARSE * COARSE))


def row_above(x, above):
    sub = lax.broadcasted_iota(jnp.int32, x.shape, 0)
    edge = jnp.broadcast_to(above[x.shape[0] - 1:, :], x.shape)
    return jnp.where(sub == 0, edge, pltpu.roll(x, 1, 0))


def row_below(x, below):
    n = x.shape[0]
    sub = lax.broadcasted_iota(jnp.int32, x.shape, 0)
    edge = jnp.broadcast_to(below[:1, :], x.shape)
    return jnp.where(sub == n - 1, edge, pltpu.roll(x, n - 1, 0))


def rows_of(k):
    return pl.ds(pl.multiple_of(k * 8, 8), 8)


def chunk(ref, k, count):
    return ref[rows_of(jnp.clip(k, 0, count - 1)), :]


def power_kernel(d_ref, c_ref, l_ref, v_ref, rok_ref, cok_ref, o_ref, wn_ref, ws_ref, ww_ref, we_ref, inv_ref, buf_ref):
    n, w = c_ref.shape
    count = n // 8

    def weights(k, carry):
        sl = rows_of(k)
        x = c_ref[sl, :]
        a = (x + row_above(x, chunk(c_ref, k - 1, count))) * 0.5
        b = (x + row_below(x, chunk(c_ref, k + 1, count))) * 0.5
        e = (x + pltpu.roll(x, 1, 1)) * 0.5
        f = (x + pltpu.roll(x, w - 1, 1)) * 0.5
        wn_ref[sl, :] = a
        ws_ref[sl, :] = b
        ww_ref[sl, :] = e
        we_ref[sl, :] = f
        ok = (rok_ref[sl, :] > 0.5) & (cok_ref[...] > 0.5)
        inv_ref[sl, :] = jnp.where(ok, 1.0 / (a + b + e + f + v_ref[sl, :]), 0.0)
        return carry

    lax.fori_loop(0, count, weights, 0)

    def sweep(src, dst):
        def body(k, carry):
            sl = rows_of(k)
            x = src[sl, :]
            summed = (
                l_ref[sl, :]
                + wn_ref[sl, :] * row_above(x, chunk(src, k - 1, count))
                + ws_ref[sl, :] * row_below(x, chunk(src, k + 1, count))
                + ww_ref[sl, :] * pltpu.roll(x, 1, 1)
                + we_ref[sl, :] * pltpu.roll(x, w - 1, 1)
            )
            inv = inv_ref[sl, :]
            dst[sl, :] = jnp.where(inv != 0.0, summed * inv, 0.0)
            return carry

        lax.fori_loop(0, count, body, 0)

    sweep(d_ref, buf_ref)
    sweep(buf_ref, o_ref)
    sweep(o_ref, buf_ref)
    sweep(buf_ref, o_ref)


def run_power(drop, cond, load, via, row_ok, col_ok):
    n, w = cond.shape
    return pl.pallas_call(
        power_kernel,
        out_shape=jax.ShapeDtypeStruct((n, w), jnp.float32),
        scratch_shapes=[pltpu.VMEM((n, w), jnp.float32) for _ in range(6)],
        compiler_params=pltpu.CompilerParams(vmem_limit_bytes=60 * 1024 * 1024),
        interpret=INTERPRET,
    )(drop, cond, load, via, row_ok, col_ok)


def thermal_kernel(t_ref, s_ref, lk_ref, vk_ref, rok_ref, o_ref, *scratch, stride, stored):
    n, w = lk_ref.shape
    count = n // 8
    lane = lax.broadcasted_iota(jnp.int32, (8, w), 1)
    first = lane == 0
    last = lane == w - 1
    if stored:
        wn_ref, ws_ref, ww_ref, we_ref, wb_ref, wa_ref, inv_ref, buf_ref = scratch
    else:
        wb_ref, wa_ref, inv_ref, buf_ref = scratch

    def lateral(x, k, ref):
        up = row_above(x, chunk(ref, k - 1, count))
        dn = row_below(x, chunk(ref, k + 1, count))
        lf = jnp.where(first, 0.0, pltpu.roll(x, 1, 1))
        rt = jnp.where(last, 0.0, pltpu.roll(x, w - 1, 1))
        return up, dn, lf, rt

    def lateral_weights(k):
        sl = rows_of(k)
        x = lk_ref[sl, :]
        up, dn, lf, rt = lateral(x, k, lk_ref)
        return (x + up) * 0.5, (x + dn) * 0.5, (x + lf) * 0.5, (x + rt) * 0.5

    def weights(k, carry):
        sl = rows_of(k)
        a, b, e, f = lateral_weights(k)
        if stored:
            wn_ref[sl, :] = a
            ws_ref[sl, :] = b
            ww_ref[sl, :] = e
            we_ref[sl, :] = f
        v = vk_ref[sl, :]
        lo = (v + chunk(vk_ref, k - stride, count)) * 0.5
        hi = (v + chunk(vk_ref, k + stride, count)) * 0.5
        wb_ref[sl, :] = lo
        wa_ref[sl, :] = hi
        inv_ref[sl, :] = jnp.where(rok_ref[sl, :] > 0.5, 1.0 / (a + b + e + f + lo + hi), 0.0)
        return carry

    lax.fori_loop(0, count, weights, 0)

    def sweep(src, dst):
        def body(k, carry):
            sl = rows_of(k)
            if stored:
                a, b, e, f = wn_ref[sl, :], ws_ref[sl, :], ww_ref[sl, :], we_ref[sl, :]
            else:
                a, b, e, f = lateral_weights(k)
            x = src[sl, :]
            up, dn, lf, rt = lateral(x, k, src)
            summed = (
                s_ref[sl, :]
                + a * up
                + b * dn
                + e * lf
                + f * rt
                + wb_ref[sl, :] * chunk(src, k - stride, count)
                + wa_ref[sl, :] * chunk(src, k + stride, count)
            )
            inv = inv_ref[sl, :]
            dst[sl, :] = jnp.where(inv != 0.0, summed * inv, 0.0)
            return carry

        lax.fori_loop(0, count, body, 0)

    sweep(t_ref, buf_ref)
    sweep(buf_ref, o_ref)
    sweep(o_ref, buf_ref)
    sweep(buf_ref, o_ref)


def run_thermal(temp, source, lat, vert, row_ok, stride):
    n, w = lat.shape
    stored = 13 * n * w * 4 <= 40 * 1024 * 1024
    kernel = functools.partial(thermal_kernel, stride=stride, stored=stored)
    return pl.pallas_call(
        kernel,
        out_shape=jax.ShapeDtypeStruct((n, w), jnp.float32),
        scratch_shapes=[pltpu.VMEM((n, w), jnp.float32) for _ in range(8 if stored else 4)],
        compiler_params=pltpu.CompilerParams(vmem_limit_bytes=60 * 1024 * 1024),
        interpret=INTERPRET,
    )(temp, source, lat, vert, row_ok)


def inside_of(start, count, total):
    idx = start + jnp.arange(count, dtype=jnp.int32)
    return (idx >= 0) & (idx < total)


def body(demand, leakage, conductance, vias, layer_of, lateral_k, vertical_k):
    tile_rows, tile_cols = demand.shape
    group_layers, cell_rows, therm_cols = lateral_k.shape
    cell_cols = tile_cols // COARSE
    n_r = lax.axis_size("row")
    n_c = lax.axis_size("col")
    r_idx = lax.axis_index("row")
    c_idx = lax.axis_index("col")
    all_layers = group_layers * n_c
    all_rows = cell_rows * n_r
    total_rows = tile_rows * n_r
    total_cols = tile_cols * n_c

    T0 = 2 * HEAT_SWEEPS
    T1 = HEAT_SWEEPS
    H0 = T0 - 1
    H1 = T1 - 1
    S = SWEEPS
    R1 = H1 * COARSE + SWEEPS
    R0 = max(H0 * COARSE, R1) + SWEEPS
    CW = 64
    PR = -(-R1 // COARSE)
    PC = CW // COARSE

    via_g = VIA_CONDUCT * vias.astype(jnp.float32)
    load0 = demand + leakage

    p0 = extended(jnp.stack([conductance, load0, via_g]), (("row", 1, R0), ("col", 2, CW)))
    p1 = extended(jnp.stack([demand, leakage]), (("row", 1, R1), ("col", 2, CW)))
    k_ext = extended(jnp.stack([lateral_k, vertical_k]), (("row", 2, T0), ("col", 1, T0)))
    layer_ext = extended(layer_of, (("row", 0, T0),))

    cols_w = tile_cols + 2 * CW
    col_ok = inside_of(c_idx * tile_cols - CW, cols_w, total_cols).astype(jnp.float32)[None, :]

    rows0 = tile_rows + 2 * R0
    row_ok0 = inside_of(r_idx * tile_rows - R0, rows0, total_rows).astype(jnp.float32)[:, None]
    drop0 = run_power(jnp.zeros((rows0, cols_w), jnp.float32), p0[0], p0[1], p0[2], row_ok0, col_ok)
    hr0 = H0 * COARSE
    rs = slice(R0 - hr0, R0 + tile_rows + hr0)
    cs = slice(CW, CW + tile_cols)
    d_h = drop0[rs, cs]
    heat0 = coarse_of(p0[1][rs, cs] * (1.0 - d_h) + p0[0][rs, cs] * d_h * d_h)

    def gather_heat(heat):
        copies = jnp.broadcast_to(heat[None], (n_c,) + heat.shape)
        gathered = lax.all_to_all(copies, "col", split_axis=0, concat_axis=0, tiled=True)
        gathered = gathered.transpose(1, 0, 2).reshape(heat.shape[0], n_c * cell_cols)
        return jnp.pad(gathered, ((1, 1), (0, 0)))

    def thermal(temp_ext, heat_ext, halo):
        layers = group_layers + 2 * halo
        rows = cell_rows + 2 * halo
        ks = k_ext[:, T0 - halo:T0 + group_layers + halo, T0 - halo:T0 + cell_rows + halo]
        tlay = c_idx * group_layers - halo + jnp.arange(layers, dtype=jnp.int32)
        inside = inside_of(c_idx * group_layers - halo, layers, all_layers)[:, None] & inside_of(r_idx * cell_rows - halo, rows, all_rows)[None, :]
        lay_in = layer_ext[T0 - halo:T0 + cell_rows + halo]
        picker = (lay_in[None, :, :] == tlay[:, None, None]) & inside[:, :, None]
        source = jnp.where(picker, heat_ext[None, :, :], 0.0)
        flat = (layers * rows, therm_cols)
        out = run_thermal(
            temp_ext.reshape(flat), source.reshape(flat), ks[0].reshape(flat), ks[1].reshape(flat),
            inside.astype(jnp.float32).reshape(layers * rows, 1), rows // 8,
        )
        return out.reshape(layers, rows, therm_cols)

    temp0 = thermal(jnp.zeros((group_layers + 2 * T0, cell_rows + 2 * T0, therm_cols), jnp.float32), gather_heat(heat0), T0)
    temp0 = temp0[T0 - T1:T0 + group_layers + T1, T0 - T1:T0 + cell_rows + T1]

    own_layers = c_idx * group_layers + jnp.arange(group_layers, dtype=jnp.int32)
    t_own = temp0[T1:T1 + group_layers, T1 - PR:T1 + cell_rows + PR]
    lay_w = layer_ext[T0 - PR:T0 + cell_rows + PR]
    partial = jnp.sum(jnp.where(lay_w[None, :, :] == own_layers[:, None, None], t_own, 0.0), axis=0)
    partial = jnp.pad(partial, ((0, 0), (PC, PC)))
    windows = jnp.stack([partial[:, j * cell_cols:j * cell_cols + cell_cols + 2 * PC] for j in range(n_c)])
    windows = lax.all_to_all(windows, "col", split_axis=0, concat_axis=0, tiled=True)
    cell_temp = jnp.sum(windows, axis=0)

    denom_c = 1.0 + COND_SLOPE * cell_temp
    grow_c = jnp.exp(LEAK_SLOPE * cell_temp)
    rows1 = tile_rows + 2 * R1
    fo = PR * COARSE - R1
    denom_f = fine_of(denom_c, cols_w)[fo:fo + rows1]
    grow_f = fine_of(grow_c, cols_w)[fo:fo + rows1]
    rs1 = slice(R0 - R1, R0 - R1 + rows1)
    cond1 = p0[0][rs1] / denom_f
    load1 = p1[0] + p1[1] * grow_f
    row_ok1 = inside_of(r_idx * tile_rows - R1, rows1, total_rows).astype(jnp.float32)[:, None]
    drop1 = run_power(drop0[rs1], cond1, load1, p0[2][rs1], row_ok1, col_ok)
    hr1 = H1 * COARSE
    rh = slice(R1 - hr1, R1 + tile_rows + hr1)
    d_h1 = drop1[rh, cs]
    heat1 = coarse_of(load1[rh, cs] * (1.0 - d_h1) + cond1[rh, cs] * d_h1 * d_h1)
    temp1 = thermal(temp0, gather_heat(heat1), T1)
    temp_out = temp1[T1:T1 + group_layers, T1:T1 + cell_rows]
    drop_out = drop1[R1:R1 + tile_rows, cs]
    return (drop_out, temp_out)


def solution(mesh):
    in_specs = (
        P("row", "col"),
        P("row", "col"),
        P("row", "col"),
        P("row", "col"),
        P("row", None),
        P("col", "row", None),
        P("col", "row", None),
    )
    out_specs = (P("row", "col"), P("col", "row", None))
    return jax.shard_map(body, mesh=mesh, in_specs=in_specs, out_specs=out_specs, check_vma=False)
```

```python
import functools
import os

import jax
import jax.numpy as jnp
from jax import lax
from jax.experimental import pallas as pl
from jax.experimental.pallas import tpu as pltpu
from jax.sharding import PartitionSpec as P

INTERPRET = os.environ.get("SOL_INTERPRET") == "1"
UNROLL = 4

COARSE = 8
SWEEPS = 4
HEAT_SWEEPS = 4
OUTER = 2


COND_SLOPE = 0.5
LEAK_SLOPE = 0.7
VIA_CONDUCT = 4.0

HALO = 4


def extended(block, sides):
    for axis, dim, width in sides:
        count = lax.axis_size(axis)
        forward = [(i, i + 1) for i in range(count - 1)]
        backward = [(target, source) for source, target in forward]
        low = lax.ppermute(
            lax.slice_in_dim(block, block.shape[dim] - width, None, axis=dim), axis, forward
        )
        high = lax.ppermute(lax.slice_in_dim(block, 0, width, axis=dim), axis, backward)
        block = jnp.concatenate([low, block, high], axis=dim)
    return block


def spread_cols(coarse, fine_cols):
    n = coarse.shape[1]
    ids = jnp.arange(fine_cols, dtype=jnp.int32) // COARSE
    onehot = (jnp.arange(n, dtype=jnp.int32)[:, None] == ids[None, :]).astype(jnp.float32)
    return jnp.dot(coarse, onehot, precision=lax.Precision.HIGHEST)


def fine_of(coarse, fine_cols):
    wide = spread_cols(coarse, fine_cols)
    rows = wide.shape[0]
    return jnp.broadcast_to(wide[:, None, :], (rows, COARSE, fine_cols)).reshape(rows * COARSE, fine_cols)


def coarse_of(fine):
    rows, cols = fine.shape
    summed_rows = jnp.sum(fine.reshape(rows // COARSE, COARSE, cols), axis=1)
    n = cols // COARSE
    ids = jnp.arange(cols, dtype=jnp.int32) // COARSE
    onehot = (ids[:, None] == jnp.arange(n, dtype=jnp.int32)[None, :]).astype(jnp.float32)
    return jnp.dot(summed_rows, onehot, precision=lax.Precision.HIGHEST) * (1.0 / (COARSE * COARSE))


def row_above(x, above):
    sub = lax.broadcasted_iota(jnp.int32, x.shape, 0)
    edge = jnp.broadcast_to(above[x.shape[0] - 1:, :], x.shape)
    return jnp.where(sub == 0, edge, pltpu.roll(x, 1, 0))


def row_below(x, below):
    n = x.shape[0]
    sub = lax.broadcasted_iota(jnp.int32, x.shape, 0)
    edge = jnp.broadcast_to(below[:1, :], x.shape)
    return jnp.where(sub == n - 1, edge, pltpu.roll(x, n - 1, 0))


def rows_of(k):
    return pl.ds(pl.multiple_of(k * 8, 8), 8)


def chunk(ref, k, count):
    return ref[rows_of(jnp.clip(k, 0, count - 1)), :]


def power_kernel(d_ref, c_ref, l_ref, v_ref, rok_ref, cok_ref, o_ref, wn_ref, ws_ref, ww_ref, we_ref, inv_ref, buf_ref):
    n, w = c_ref.shape
    count = n // 8

    def weights(k, carry):
        sl = rows_of(k)
        x = c_ref[sl, :]
        a = (x + row_above(x, chunk(c_ref, k - 1, count))) * 0.5
        b = (x + row_below(x, chunk(c_ref, k + 1, count))) * 0.5
        e = (x + pltpu.roll(x, 1, 1)) * 0.5
        f = (x + pltpu.roll(x, w - 1, 1)) * 0.5
        wn_ref[sl, :] = a
        ws_ref[sl, :] = b
        ww_ref[sl, :] = e
        we_ref[sl, :] = f
        ok = (rok_ref[sl, :] > 0.5) & (cok_ref[...] > 0.5)
        inv_ref[sl, :] = jnp.where(ok, 1.0 / (a + b + e + f + v_ref[sl, :]), 0.0)
        return carry

    lax.fori_loop(0, count, weights, 0, unroll=UNROLL)

    def sweep(src, dst):
        def body(k, carry):
            sl = rows_of(k)
            x = src[sl, :]
            summed = (
                l_ref[sl, :]
                + wn_ref[sl, :] * row_above(x, chunk(src, k - 1, count))
                + ws_ref[sl, :] * row_below(x, chunk(src, k + 1, count))
                + ww_ref[sl, :] * pltpu.roll(x, 1, 1)
                + we_ref[sl, :] * pltpu.roll(x, w - 1, 1)
            )
            inv = inv_ref[sl, :]
            dst[sl, :] = jnp.where(inv != 0.0, summed * inv, 0.0)
            return carry

        lax.fori_loop(0, count, body, 0, unroll=UNROLL)

    sweep(d_ref, buf_ref)
    sweep(buf_ref, o_ref)
    sweep(o_ref, buf_ref)
    sweep(buf_ref, o_ref)


def run_power(drop, cond, load, via, row_ok, col_ok):
    n, w = cond.shape
    return pl.pallas_call(
        power_kernel,
        out_shape=jax.ShapeDtypeStruct((n, w), jnp.float32),
        scratch_shapes=[pltpu.VMEM((n, w), jnp.float32) for _ in range(6)],
        compiler_params=pltpu.CompilerParams(vmem_limit_bytes=60 * 1024 * 1024),
        interpret=INTERPRET,
    )(drop, cond, load, via, row_ok, col_ok)


def thermal_kernel(t_ref, s_ref, lk_ref, vk_ref, rok_ref, o_ref, *scratch, stride, stored):
    n, w = lk_ref.shape
    count = n // 8
    lane = lax.broadcasted_iota(jnp.int32, (8, w), 1)
    first = lane == 0
    last = lane == w - 1
    if stored:
        wn_ref, ws_ref, ww_ref, we_ref, wb_ref, wa_ref, inv_ref, buf_ref = scratch
    else:
        wb_ref, wa_ref, inv_ref, buf_ref = scratch

    def lateral(x, k, ref):
        up = row_above(x, chunk(ref, k - 1, count))
        dn = row_below(x, chunk(ref, k + 1, count))
        lf = jnp.where(first, 0.0, pltpu.roll(x, 1, 1))
        rt = jnp.where(last, 0.0, pltpu.roll(x, w - 1, 1))
        return up, dn, lf, rt

    def lateral_weights(k):
        sl = rows_of(k)
        x = lk_ref[sl, :]
        up, dn, lf, rt = lateral(x, k, lk_ref)
        return (x + up) * 0.5, (x + dn) * 0.5, (x + lf) * 0.5, (x + rt) * 0.5

    def weights(k, carry):
        sl = rows_of(k)
        a, b, e, f = lateral_weights(k)
        if stored:
            wn_ref[sl, :] = a
            ws_ref[sl, :] = b
            ww_ref[sl, :] = e
            we_ref[sl, :] = f
        v = vk_ref[sl, :]
        lo = (v + chunk(vk_ref, k - stride, count)) * 0.5
        hi = (v + chunk(vk_ref, k + stride, count)) * 0.5
        wb_ref[sl, :] = lo
        wa_ref[sl, :] = hi
        inv_ref[sl, :] = jnp.where(rok_ref[sl, :] > 0.5, 1.0 / (a + b + e + f + lo + hi), 0.0)
        return carry

    lax.fori_loop(0, count, weights, 0, unroll=UNROLL)

    def sweep(src, dst):
        def body(k, carry):
            sl = rows_of(k)
            if stored:
                a, b, e, f = wn_ref[sl, :], ws_ref[sl, :], ww_ref[sl, :], we_ref[sl, :]
            else:
                a, b, e, f = lateral_weights(k)
            x = src[sl, :]
            up, dn, lf, rt = lateral(x, k, src)
            summed = (
                s_ref[sl, :]
                + a * up
                + b * dn
                + e * lf
                + f * rt
                + wb_ref[sl, :] * chunk(src, k - stride, count)
                + wa_ref[sl, :] * chunk(src, k + stride, count)
            )
            inv = inv_ref[sl, :]
            dst[sl, :] = jnp.where(inv != 0.0, summed * inv, 0.0)
            return carry

        lax.fori_loop(0, count, body, 0, unroll=UNROLL)

    sweep(t_ref, buf_ref)
    sweep(buf_ref, o_ref)
    sweep(o_ref, buf_ref)
    sweep(buf_ref, o_ref)


def run_thermal(temp, source, lat, vert, row_ok, stride):
    n, w = lat.shape
    stored = 13 * n * w * 4 <= 40 * 1024 * 1024
    kernel = functools.partial(thermal_kernel, stride=stride, stored=stored)
    return pl.pallas_call(
        kernel,
        out_shape=jax.ShapeDtypeStruct((n, w), jnp.float32),
        scratch_shapes=[pltpu.VMEM((n, w), jnp.float32) for _ in range(8 if stored else 4)],
        compiler_params=pltpu.CompilerParams(vmem_limit_bytes=60 * 1024 * 1024),
        interpret=INTERPRET,
    )(temp, source, lat, vert, row_ok)


def inside_of(start, count, total):
    idx = start + jnp.arange(count, dtype=jnp.int32)
    return (idx >= 0) & (idx < total)


def body(demand, leakage, conductance, vias, layer_of, lateral_k, vertical_k):
    tile_rows, tile_cols = demand.shape
    group_layers, cell_rows, therm_cols = lateral_k.shape
    cell_cols = tile_cols // COARSE
    n_r = lax.axis_size("row")
    n_c = lax.axis_size("col")
    r_idx = lax.axis_index("row")
    c_idx = lax.axis_index("col")
    all_layers = group_layers * n_c
    all_rows = cell_rows * n_r
    total_rows = tile_rows * n_r
    total_cols = tile_cols * n_c

    T0 = 2 * HEAT_SWEEPS
    T1 = HEAT_SWEEPS
    H0 = T0 - 1
    H1 = T1 - 1
    S = SWEEPS
    R1 = H1 * COARSE + SWEEPS
    R0 = max(H0 * COARSE, R1) + SWEEPS
    CW = 64
    PR = -(-R1 // COARSE)
    PC = CW // COARSE

    via_g = VIA_CONDUCT * vias.astype(jnp.float32)
    load0 = demand + leakage

    p0 = extended(jnp.stack([conductance, load0, via_g]), (("row", 1, R0), ("col", 2, CW)))
    p1 = extended(jnp.stack([demand, leakage]), (("row", 1, R1), ("col", 2, CW)))
    k_ext = extended(jnp.stack([lateral_k, vertical_k]), (("row", 2, T0), ("col", 1, T0)))
    layer_ext = extended(layer_of, (("row", 0, T0),))

    cols_w = tile_cols + 2 * CW
    col_ok = inside_of(c_idx * tile_cols - CW, cols_w, total_cols).astype(jnp.float32)[None, :]

    rows0 = tile_rows + 2 * R0
    row_ok0 = inside_of(r_idx * tile_rows - R0, rows0, total_rows).astype(jnp.float32)[:, None]
    drop0 = run_power(jnp.zeros((rows0, cols_w), jnp.float32), p0[0], p0[1], p0[2], row_ok0, col_ok)
    hr0 = H0 * COARSE
    rs = slice(R0 - hr0, R0 + tile_rows + hr0)
    cs = slice(CW, CW + tile_cols)
    d_h = drop0[rs, cs]
    heat0 = coarse_of(p0[1][rs, cs] * (1.0 - d_h) + p0[0][rs, cs] * d_h * d_h)

    def gather_heat(heat):
        copies = jnp.broadcast_to(heat[None], (n_c,) + heat.shape)
        gathered = lax.all_to_all(copies, "col", split_axis=0, concat_axis=0, tiled=True)
        gathered = gathered.transpose(1, 0, 2).reshape(heat.shape[0], n_c * cell_cols)
        return jnp.pad(gathered, ((1, 1), (0, 0)))

    def thermal(temp_ext, heat_ext, halo):
        layers = group_layers + 2 * halo
        rows = cell_rows + 2 * halo
        ks = k_ext[:, T0 - halo:T0 + group_layers + halo, T0 - halo:T0 + cell_rows + halo]
        tlay = c_idx * group_layers - halo + jnp.arange(layers, dtype=jnp.int32)
        inside = inside_of(c_idx * group_layers - halo, layers, all_layers)[:, None] & inside_of(r_idx * cell_rows - halo, rows, all_rows)[None, :]
        lay_in = layer_ext[T0 - halo:T0 + cell_rows + halo]
        picker = (lay_in[None, :, :] == tlay[:, None, None]) & inside[:, :, None]
        source = jnp.where(picker, heat_ext[None, :, :], 0.0)
        flat = (layers * rows, therm_cols)
        out = run_thermal(
            temp_ext.reshape(flat), source.reshape(flat), ks[0].reshape(flat), ks[1].reshape(flat),
            inside.astype(jnp.float32).reshape(layers * rows, 1), rows // 8,
        )
        return out.reshape(layers, rows, therm_cols)

    temp0 = thermal(jnp.zeros((group_layers + 2 * T0, cell_rows + 2 * T0, therm_cols), jnp.float32), gather_heat(heat0), T0)
    temp0 = temp0[T0 - T1:T0 + group_layers + T1, T0 - T1:T0 + cell_rows + T1]

    own_layers = c_idx * group_layers + jnp.arange(group_layers, dtype=jnp.int32)
    t_own = temp0[T1:T1 + group_layers, T1 - PR:T1 + cell_rows + PR]
    lay_w = layer_ext[T0 - PR:T0 + cell_rows + PR]
    partial = jnp.sum(jnp.where(lay_w[None, :, :] == own_layers[:, None, None], t_own, 0.0), axis=0)
    partial = jnp.pad(partial, ((0, 0), (PC, PC)))
    windows = jnp.stack([partial[:, j * cell_cols:j * cell_cols + cell_cols + 2 * PC] for j in range(n_c)])
    windows = lax.all_to_all(windows, "col", split_axis=0, concat_axis=0, tiled=True)
    cell_temp = jnp.sum(windows, axis=0)

    denom_c = 1.0 + COND_SLOPE * cell_temp
    grow_c = jnp.exp(LEAK_SLOPE * cell_temp)
    rows1 = tile_rows + 2 * R1
    fo = PR * COARSE - R1
    denom_f = fine_of(denom_c, cols_w)[fo:fo + rows1]
    grow_f = fine_of(grow_c, cols_w)[fo:fo + rows1]
    rs1 = slice(R0 - R1, R0 - R1 + rows1)
    cond1 = p0[0][rs1] / denom_f
    load1 = p1[0] + p1[1] * grow_f
    row_ok1 = inside_of(r_idx * tile_rows - R1, rows1, total_rows).astype(jnp.float32)[:, None]
    drop1 = run_power(drop0[rs1], cond1, load1, p0[2][rs1], row_ok1, col_ok)
    hr1 = H1 * COARSE
    rh = slice(R1 - hr1, R1 + tile_rows + hr1)
    d_h1 = drop1[rh, cs]
    heat1 = coarse_of(load1[rh, cs] * (1.0 - d_h1) + cond1[rh, cs] * d_h1 * d_h1)
    temp1 = thermal(temp0, gather_heat(heat1), T1)
    temp_out = temp1[T1:T1 + group_layers, T1:T1 + cell_rows]
    drop_out = drop1[R1:R1 + tile_rows, cs]
    return (drop_out, temp_out)


def solution(mesh):
    in_specs = (
        P("row", "col"),
        P("row", "col"),
        P("row", "col"),
        P("row", "col"),
        P("row", None),
        P("col", "row", None),
        P("col", "row", None),
    )
    out_specs = (P("row", "col"), P("col", "row", None))
    return jax.shard_map(body, mesh=mesh, in_specs=in_specs, out_specs=out_specs, check_vma=False)
```

```python
import functools
import os

import jax
import jax.numpy as jnp
from jax import lax
from jax.experimental import pallas as pl
from jax.experimental.pallas import tpu as pltpu
from jax.sharding import PartitionSpec as P

INTERPRET = os.environ.get("SOL_INTERPRET") == "1"
UNROLL = 4

COARSE = 8
SWEEPS = 4
HEAT_SWEEPS = 4
OUTER = 2


COND_SLOPE = 0.5
LEAK_SLOPE = 0.7
VIA_CONDUCT = 4.0

HALO = 4


def extended(block, sides):
    for axis, dim, width in sides:
        count = lax.axis_size(axis)
        forward = [(i, i + 1) for i in range(count - 1)]
        backward = [(target, source) for source, target in forward]
        low = lax.ppermute(
            lax.slice_in_dim(block, block.shape[dim] - width, None, axis=dim), axis, forward
        )
        high = lax.ppermute(lax.slice_in_dim(block, 0, width, axis=dim), axis, backward)
        block = jnp.concatenate([low, block, high], axis=dim)
    return block


def spread_cols(coarse, fine_cols):
    n = coarse.shape[1]
    ids = jnp.arange(fine_cols, dtype=jnp.int32) // COARSE
    onehot = (jnp.arange(n, dtype=jnp.int32)[:, None] == ids[None, :]).astype(jnp.float32)
    return jnp.dot(coarse, onehot, precision=lax.Precision.HIGHEST)


def fine_of(coarse, fine_cols):
    wide = spread_cols(coarse, fine_cols)
    rows = wide.shape[0]
    return jnp.broadcast_to(wide[:, None, :], (rows, COARSE, fine_cols)).reshape(rows * COARSE, fine_cols)


def coarse_of(fine):
    rows, cols = fine.shape
    summed_rows = jnp.sum(fine.reshape(rows // COARSE, COARSE, cols), axis=1)
    n = cols // COARSE
    ids = jnp.arange(cols, dtype=jnp.int32) // COARSE
    onehot = (ids[:, None] == jnp.arange(n, dtype=jnp.int32)[None, :]).astype(jnp.float32)
    return jnp.dot(summed_rows, onehot, precision=lax.Precision.HIGHEST) * (1.0 / (COARSE * COARSE))


def row_above(x, above):
    sub = lax.broadcasted_iota(jnp.int32, x.shape, 0)
    edge = jnp.broadcast_to(above[x.shape[0] - 1:, :], x.shape)
    return jnp.where(sub == 0, edge, pltpu.roll(x, 1, 0))


def row_below(x, below):
    n = x.shape[0]
    sub = lax.broadcasted_iota(jnp.int32, x.shape, 0)
    edge = jnp.broadcast_to(below[:1, :], x.shape)
    return jnp.where(sub == n - 1, edge, pltpu.roll(x, n - 1, 0))


def rows_of(k):
    return pl.ds(pl.multiple_of(k * 8, 8), 8)


def chunk(ref, k, count):
    return ref[rows_of(jnp.clip(k, 0, count - 1)), :]


def power_kernel(d_ref, c_ref, l_ref, v_ref, rok_ref, cok_ref, o_ref, wn_ref, ws_ref, ww_ref, we_ref, inv_ref, buf_ref):
    n, w = c_ref.shape
    count = n // 8

    def weights(k, carry):
        sl = rows_of(k)
        x = c_ref[sl, :]
        a = (x + row_above(x, chunk(c_ref, k - 1, count))) * 0.5
        b = (x + row_below(x, chunk(c_ref, k + 1, count))) * 0.5
        e = (x + pltpu.roll(x, 1, 1)) * 0.5
        f = (x + pltpu.roll(x, w - 1, 1)) * 0.5
        wn_ref[sl, :] = a
        ws_ref[sl, :] = b
        ww_ref[sl, :] = e
        we_ref[sl, :] = f
        ok = (rok_ref[sl, :] > 0.5) & (cok_ref[...] > 0.5)
        inv_ref[sl, :] = jnp.where(ok, 1.0 / (a + b + e + f + v_ref[sl, :]), 0.0)
        return carry

    lax.fori_loop(0, count, weights, 0, unroll=UNROLL)

    def sweep(src, dst):
        def body(k, carry):
            sl = rows_of(k)
            x = src[sl, :]
            summed = (
                l_ref[sl, :]
                + wn_ref[sl, :] * row_above(x, chunk(src, k - 1, count))
                + ws_ref[sl, :] * row_below(x, chunk(src, k + 1, count))
                + ww_ref[sl, :] * pltpu.roll(x, 1, 1)
                + we_ref[sl, :] * pltpu.roll(x, w - 1, 1)
            )
            inv = inv_ref[sl, :]
            dst[sl, :] = jnp.where(inv != 0.0, summed * inv, 0.0)
            return carry

        lax.fori_loop(0, count, body, 0, unroll=UNROLL)

    sweep(d_ref, buf_ref)
    sweep(buf_ref, o_ref)
    sweep(o_ref, buf_ref)
    sweep(buf_ref, o_ref)


def run_power(drop, cond, load, via, row_ok, col_ok):
    n, w = cond.shape
    return pl.pallas_call(
        power_kernel,
        out_shape=jax.ShapeDtypeStruct((n, w), jnp.float32),
        scratch_shapes=[pltpu.VMEM((n, w), jnp.float32) for _ in range(6)],
        compiler_params=pltpu.CompilerParams(vmem_limit_bytes=60 * 1024 * 1024),
        interpret=INTERPRET,
    )(drop, cond, load, via, row_ok, col_ok)


def thermal_kernel(t_ref, s_ref, lk_ref, vk_ref, rok_ref, o_ref, *scratch, stride, stored):
    n, w = lk_ref.shape
    count = n // 8
    lane = lax.broadcasted_iota(jnp.int32, (8, w), 1)
    first = lane == 0
    last = lane == w - 1
    if stored:
        wn_ref, ws_ref, ww_ref, we_ref, wb_ref, wa_ref, inv_ref, buf_ref = scratch
    else:
        wb_ref, wa_ref, inv_ref, buf_ref = scratch

    def lateral(x, k, ref):
        up = row_above(x, chunk(ref, k - 1, count))
        dn = row_below(x, chunk(ref, k + 1, count))
        lf = jnp.where(first, 0.0, pltpu.roll(x, 1, 1))
        rt = jnp.where(last, 0.0, pltpu.roll(x, w - 1, 1))
        return up, dn, lf, rt

    def lateral_weights(k):
        sl = rows_of(k)
        x = lk_ref[sl, :]
        up, dn, lf, rt = lateral(x, k, lk_ref)
        return (x + up) * 0.5, (x + dn) * 0.5, (x + lf) * 0.5, (x + rt) * 0.5

    def weights(k, carry):
        sl = rows_of(k)
        a, b, e, f = lateral_weights(k)
        if stored:
            wn_ref[sl, :] = a
            ws_ref[sl, :] = b
            ww_ref[sl, :] = e
            we_ref[sl, :] = f
        v = vk_ref[sl, :]
        lo = (v + chunk(vk_ref, k - stride, count)) * 0.5
        hi = (v + chunk(vk_ref, k + stride, count)) * 0.5
        wb_ref[sl, :] = lo
        wa_ref[sl, :] = hi
        inv_ref[sl, :] = jnp.where(rok_ref[sl, :] > 0.5, 1.0 / (a + b + e + f + lo + hi), 0.0)
        return carry

    lax.fori_loop(0, count, weights, 0, unroll=UNROLL)

    def sweep(src, dst):
        def body(k, carry):
            sl = rows_of(k)
            if stored:
                a, b, e, f = wn_ref[sl, :], ws_ref[sl, :], ww_ref[sl, :], we_ref[sl, :]
            else:
                a, b, e, f = lateral_weights(k)
            x = src[sl, :]
            up, dn, lf, rt = lateral(x, k, src)
            summed = (
                s_ref[sl, :]
                + a * up
                + b * dn
                + e * lf
                + f * rt
                + wb_ref[sl, :] * chunk(src, k - stride, count)
                + wa_ref[sl, :] * chunk(src, k + stride, count)
            )
            inv = inv_ref[sl, :]
            dst[sl, :] = jnp.where(inv != 0.0, summed * inv, 0.0)
            return carry

        lax.fori_loop(0, count, body, 0, unroll=UNROLL)

    sweep(t_ref, buf_ref)
    sweep(buf_ref, o_ref)
    sweep(o_ref, buf_ref)
    sweep(buf_ref, o_ref)


def run_thermal(temp, source, lat, vert, row_ok, stride):
    n, w = lat.shape
    stored = 13 * n * w * 4 <= 40 * 1024 * 1024
    kernel = functools.partial(thermal_kernel, stride=stride, stored=stored)
    return pl.pallas_call(
        kernel,
        out_shape=jax.ShapeDtypeStruct((n, w), jnp.float32),
        scratch_shapes=[pltpu.VMEM((n, w), jnp.float32) for _ in range(8 if stored else 4)],
        compiler_params=pltpu.CompilerParams(vmem_limit_bytes=60 * 1024 * 1024),
        interpret=INTERPRET,
    )(temp, source, lat, vert, row_ok)


def inside_of(start, count, total):
    idx = start + jnp.arange(count, dtype=jnp.int32)
    return (idx >= 0) & (idx < total)


def body(demand, leakage, conductance, vias, layer_of, lateral_k, vertical_k):
    tile_rows, tile_cols = demand.shape
    group_layers, cell_rows, therm_cols = lateral_k.shape
    cell_cols = tile_cols // COARSE
    n_r = lax.axis_size("row")
    n_c = lax.axis_size("col")
    r_idx = lax.axis_index("row")
    c_idx = lax.axis_index("col")
    all_layers = group_layers * n_c
    all_rows = cell_rows * n_r
    total_rows = tile_rows * n_r
    total_cols = tile_cols * n_c

    T0 = 2 * HEAT_SWEEPS
    T1 = HEAT_SWEEPS
    H0 = T0 - 1
    H1 = T1 - 1
    S = SWEEPS
    R1 = H1 * COARSE + SWEEPS
    R0 = max(H0 * COARSE, R1) + SWEEPS
    CW = 64
    PR = -(-R1 // COARSE)
    PC = CW // COARSE

    via_g = VIA_CONDUCT * vias.astype(jnp.float32)
    load0 = demand + leakage

    p0 = extended(jnp.stack([conductance, load0, via_g]), (("row", 1, R0), ("col", 2, CW)))
    p1 = extended(jnp.stack([demand, leakage]), (("row", 1, R1), ("col", 2, CW)))
    k_ext = extended(jnp.stack([lateral_k, vertical_k]), (("col", 1, T1), ("row", 2, T0)))
    layer_ext = extended(layer_of, (("row", 0, T0),))

    cols_w = tile_cols + 2 * CW
    col_ok = inside_of(c_idx * tile_cols - CW, cols_w, total_cols).astype(jnp.float32)[None, :]

    rows0 = tile_rows + 2 * R0
    row_ok0 = inside_of(r_idx * tile_rows - R0, rows0, total_rows).astype(jnp.float32)[:, None]
    drop0 = run_power(jnp.zeros((rows0, cols_w), jnp.float32), p0[0], p0[1], p0[2], row_ok0, col_ok)
    hr0 = H0 * COARSE
    rs = slice(R0 - hr0, R0 + tile_rows + hr0)
    cs = slice(CW, CW + tile_cols)
    d_h = drop0[rs, cs]
    heat0 = coarse_of(p0[1][rs, cs] * (1.0 - d_h) + p0[0][rs, cs] * d_h * d_h)

    def gather_heat(heat):
        copies = jnp.broadcast_to(heat[None], (n_c,) + heat.shape)
        gathered = lax.all_to_all(copies, "col", split_axis=0, concat_axis=0, tiled=True)
        gathered = gathered.transpose(1, 0, 2).reshape(heat.shape[0], n_c * cell_cols)
        return jnp.pad(gathered, ((1, 1), (0, 0)))

    def thermal(temp_ext, heat_ext, halo):
        layers = group_layers + 2 * T1
        rows = cell_rows + 2 * halo
        ks = k_ext[:, :, T0 - halo:T0 + cell_rows + halo]
        tlay = c_idx * group_layers - T1 + jnp.arange(layers, dtype=jnp.int32)
        inside = inside_of(c_idx * group_layers - T1, layers, all_layers)[:, None] & inside_of(r_idx * cell_rows - halo, rows, all_rows)[None, :]
        lay_in = layer_ext[T0 - halo:T0 + cell_rows + halo]
        picker = (lay_in[None, :, :] == tlay[:, None, None]) & inside[:, :, None]
        source = jnp.where(picker, heat_ext[None, :, :], 0.0)
        flat = (layers * rows, therm_cols)
        out = run_thermal(
            temp_ext.reshape(flat), source.reshape(flat), ks[0].reshape(flat), ks[1].reshape(flat),
            inside.astype(jnp.float32).reshape(layers * rows, 1), rows // 8,
        )
        return out.reshape(layers, rows, therm_cols)

    temp0 = thermal(jnp.zeros((group_layers + 2 * T1, cell_rows + 2 * T0, therm_cols), jnp.float32), gather_heat(heat0), T0)
    temp0 = temp0[T1:T1 + group_layers, T0 - T1:T0 + cell_rows + T1]

    own_layers = c_idx * group_layers + jnp.arange(group_layers, dtype=jnp.int32)
    t_own = temp0[:, T1 - PR:T1 + cell_rows + PR]
    lay_w = layer_ext[T0 - PR:T0 + cell_rows + PR]
    partial = jnp.sum(jnp.where(lay_w[None, :, :] == own_layers[:, None, None], t_own, 0.0), axis=0)
    partial = jnp.pad(partial, ((0, 0), (PC, PC)))
    windows = jnp.stack([partial[:, j * cell_cols:j * cell_cols + cell_cols + 2 * PC] for j in range(n_c)])
    windows = lax.all_to_all(windows, "col", split_axis=0, concat_axis=0, tiled=True)
    cell_temp = jnp.sum(windows, axis=0)

    denom_c = 1.0 + COND_SLOPE * cell_temp
    grow_c = jnp.exp(LEAK_SLOPE * cell_temp)
    rows1 = tile_rows + 2 * R1
    fo = PR * COARSE - R1
    denom_f = fine_of(denom_c, cols_w)[fo:fo + rows1]
    grow_f = fine_of(grow_c, cols_w)[fo:fo + rows1]
    rs1 = slice(R0 - R1, R0 - R1 + rows1)
    cond1 = p0[0][rs1] / denom_f
    load1 = p1[0] + p1[1] * grow_f
    row_ok1 = inside_of(r_idx * tile_rows - R1, rows1, total_rows).astype(jnp.float32)[:, None]
    drop1 = run_power(drop0[rs1], cond1, load1, p0[2][rs1], row_ok1, col_ok)
    hr1 = H1 * COARSE
    rh = slice(R1 - hr1, R1 + tile_rows + hr1)
    d_h1 = drop1[rh, cs]
    heat1 = coarse_of(load1[rh, cs] * (1.0 - d_h1) + cond1[rh, cs] * d_h1 * d_h1)
    temp1 = thermal(extended(temp0, (("col", 0, T1),)), gather_heat(heat1), T1)
    temp_out = temp1[T1:T1 + group_layers, T1:T1 + cell_rows]
    drop_out = drop1[R1:R1 + tile_rows, cs]
    return (drop_out, temp_out)


def solution(mesh):
    in_specs = (
        P("row", "col"),
        P("row", "col"),
        P("row", "col"),
        P("row", "col"),
        P("row", None),
        P("col", "row", None),
        P("col", "row", None),
    )
    out_specs = (P("row", "col"), P("col", "row", None))
    return jax.shard_map(body, mesh=mesh, in_specs=in_specs, out_specs=out_specs, check_vma=False)
```

```python
import functools
import os

import jax
import jax.numpy as jnp
from jax import lax
from jax.experimental import pallas as pl
from jax.experimental.pallas import tpu as pltpu
from jax.sharding import PartitionSpec as P

INTERPRET = os.environ.get("SOL_INTERPRET") == "1"
UNROLL = 4

COARSE = 8
SWEEPS = 4
HEAT_SWEEPS = 4
OUTER = 2


COND_SLOPE = 0.5
LEAK_SLOPE = 0.7
VIA_CONDUCT = 4.0

HALO = 4


def extended(block, sides):
    for axis, dim, width in sides:
        count = lax.axis_size(axis)
        forward = [(i, i + 1) for i in range(count - 1)]
        backward = [(target, source) for source, target in forward]
        low = lax.ppermute(
            lax.slice_in_dim(block, block.shape[dim] - width, None, axis=dim), axis, forward
        )
        high = lax.ppermute(lax.slice_in_dim(block, 0, width, axis=dim), axis, backward)
        block = jnp.concatenate([low, block, high], axis=dim)
    return block


def spread_cols(coarse, fine_cols):
    n = coarse.shape[1]
    ids = jnp.arange(fine_cols, dtype=jnp.int32) // COARSE
    onehot = (jnp.arange(n, dtype=jnp.int32)[:, None] == ids[None, :]).astype(jnp.float32)
    return jnp.dot(coarse, onehot, precision=lax.Precision.HIGHEST)


def fine_of(coarse, fine_cols):
    wide = spread_cols(coarse, fine_cols)
    rows = wide.shape[0]
    return jnp.broadcast_to(wide[:, None, :], (rows, COARSE, fine_cols)).reshape(rows * COARSE, fine_cols)


def coarse_of(fine):
    rows, cols = fine.shape
    summed_rows = jnp.sum(fine.reshape(rows // COARSE, COARSE, cols), axis=1)
    n = cols // COARSE
    ids = jnp.arange(cols, dtype=jnp.int32) // COARSE
    onehot = (ids[:, None] == jnp.arange(n, dtype=jnp.int32)[None, :]).astype(jnp.float32)
    return jnp.dot(summed_rows, onehot, precision=lax.Precision.HIGHEST) * (1.0 / (COARSE * COARSE))


def row_above(x, above):
    sub = lax.broadcasted_iota(jnp.int32, x.shape, 0)
    edge = jnp.broadcast_to(above[x.shape[0] - 1:, :], x.shape)
    return jnp.where(sub == 0, edge, pltpu.roll(x, 1, 0))


def row_below(x, below):
    n = x.shape[0]
    sub = lax.broadcasted_iota(jnp.int32, x.shape, 0)
    edge = jnp.broadcast_to(below[:1, :], x.shape)
    return jnp.where(sub == n - 1, edge, pltpu.roll(x, n - 1, 0))


def rows_of(k):
    return pl.ds(pl.multiple_of(k * 8, 8), 8)


def chunk(ref, k, count):
    return ref[rows_of(jnp.clip(k, 0, count - 1)), :]


def power_kernel(*refs, zero_start, stacked):
    refs = list(refs)
    d_ref = None if zero_start else refs.pop(0)
    if stacked:
        p_ref = refs.pop(0)
        c_ref, l_ref, v_ref = p_ref.at[0], p_ref.at[1], p_ref.at[2]
    else:
        c_ref, l_ref, v_ref = refs.pop(0), refs.pop(0), refs.pop(0)
    rok_ref, cok_ref, o_ref, wn_ref, ws_ref, ww_ref, we_ref, inv_ref, buf_ref = refs
    n, w = o_ref.shape
    count = n // 8

    def weights(k, carry):
        sl = rows_of(k)
        x = c_ref[sl, :]
        a = (x + row_above(x, chunk(c_ref, k - 1, count))) * 0.5
        b = (x + row_below(x, chunk(c_ref, k + 1, count))) * 0.5
        e = (x + pltpu.roll(x, 1, 1)) * 0.5
        f = (x + pltpu.roll(x, w - 1, 1)) * 0.5
        wn_ref[sl, :] = a
        ws_ref[sl, :] = b
        ww_ref[sl, :] = e
        we_ref[sl, :] = f
        ok = (rok_ref[sl, :] > 0.5) & (cok_ref[...] > 0.5)
        inv = jnp.where(ok, 1.0 / (a + b + e + f + v_ref[sl, :]), 0.0)
        inv_ref[sl, :] = inv
        if zero_start:
            buf_ref[sl, :] = jnp.where(inv != 0.0, l_ref[sl, :] * inv, 0.0)
        return carry

    lax.fori_loop(0, count, weights, 0, unroll=UNROLL)

    def sweep(src, dst):
        def body(k, carry):
            sl = rows_of(k)
            x = src[sl, :]
            summed = (
                l_ref[sl, :]
                + wn_ref[sl, :] * row_above(x, chunk(src, k - 1, count))
                + ws_ref[sl, :] * row_below(x, chunk(src, k + 1, count))
                + ww_ref[sl, :] * pltpu.roll(x, 1, 1)
                + we_ref[sl, :] * pltpu.roll(x, w - 1, 1)
            )
            inv = inv_ref[sl, :]
            dst[sl, :] = jnp.where(inv != 0.0, summed * inv, 0.0)
            return carry

        lax.fori_loop(0, count, body, 0, unroll=UNROLL)

    if not zero_start:
        sweep(d_ref, buf_ref)
    sweep(buf_ref, o_ref)
    sweep(o_ref, buf_ref)
    sweep(buf_ref, o_ref)


def run_power(drop, parts, row_ok, col_ok):
    stacked = not isinstance(parts, (tuple, list))
    n, w = parts.shape[1:] if stacked else parts[0].shape
    operands = ([] if drop is None else [drop]) + ([parts] if stacked else list(parts)) + [row_ok, col_ok]
    kernel = functools.partial(power_kernel, zero_start=drop is None, stacked=stacked)
    return pl.pallas_call(
        kernel,
        out_shape=jax.ShapeDtypeStruct((n, w), jnp.float32),
        scratch_shapes=[pltpu.VMEM((n, w), jnp.float32) for _ in range(6)],
        compiler_params=pltpu.CompilerParams(vmem_limit_bytes=60 * 1024 * 1024),
        interpret=INTERPRET,
    )(*operands)


def thermal_kernel(*refs, stride, stored, zero_start):
    refs = list(refs)
    t_ref = None if zero_start else refs.pop(0)
    s_ref, lk_ref, vk_ref, rok_ref, o_ref = refs[:5]
    scratch = refs[5:]
    n, w = lk_ref.shape
    count = n // 8
    lane = lax.broadcasted_iota(jnp.int32, (8, w), 1)
    first = lane == 0
    last = lane == w - 1
    if stored:
        wn_ref, ws_ref, ww_ref, we_ref, wb_ref, wa_ref, inv_ref, buf_ref = scratch
    else:
        wb_ref, wa_ref, inv_ref, buf_ref = scratch

    def lateral(x, k, ref):
        up = row_above(x, chunk(ref, k - 1, count))
        dn = row_below(x, chunk(ref, k + 1, count))
        lf = jnp.where(first, 0.0, pltpu.roll(x, 1, 1))
        rt = jnp.where(last, 0.0, pltpu.roll(x, w - 1, 1))
        return up, dn, lf, rt

    def lateral_weights(k):
        sl = rows_of(k)
        x = lk_ref[sl, :]
        up, dn, lf, rt = lateral(x, k, lk_ref)
        return (x + up) * 0.5, (x + dn) * 0.5, (x + lf) * 0.5, (x + rt) * 0.5

    def weights(k, carry):
        sl = rows_of(k)
        a, b, e, f = lateral_weights(k)
        if stored:
            wn_ref[sl, :] = a
            ws_ref[sl, :] = b
            ww_ref[sl, :] = e
            we_ref[sl, :] = f
        v = vk_ref[sl, :]
        lo = (v + chunk(vk_ref, k - stride, count)) * 0.5
        hi = (v + chunk(vk_ref, k + stride, count)) * 0.5
        wb_ref[sl, :] = lo
        wa_ref[sl, :] = hi
        inv = jnp.where(rok_ref[sl, :] > 0.5, 1.0 / (a + b + e + f + lo + hi), 0.0)
        inv_ref[sl, :] = inv
        if zero_start:
            buf_ref[sl, :] = jnp.where(inv != 0.0, s_ref[sl, :] * inv, 0.0)
        return carry

    lax.fori_loop(0, count, weights, 0, unroll=UNROLL)

    def sweep(src, dst):
        def body(k, carry):
            sl = rows_of(k)
            if stored:
                a, b, e, f = wn_ref[sl, :], ws_ref[sl, :], ww_ref[sl, :], we_ref[sl, :]
            else:
                a, b, e, f = lateral_weights(k)
            x = src[sl, :]
            up, dn, lf, rt = lateral(x, k, src)
            summed = (
                s_ref[sl, :]
                + a * up
                + b * dn
                + e * lf
                + f * rt
                + wb_ref[sl, :] * chunk(src, k - stride, count)
                + wa_ref[sl, :] * chunk(src, k + stride, count)
            )
            inv = inv_ref[sl, :]
            dst[sl, :] = jnp.where(inv != 0.0, summed * inv, 0.0)
            return carry

        lax.fori_loop(0, count, body, 0, unroll=UNROLL)

    if not zero_start:
        sweep(t_ref, buf_ref)
    sweep(buf_ref, o_ref)
    sweep(o_ref, buf_ref)
    sweep(buf_ref, o_ref)


def run_thermal(temp, source, lat, vert, row_ok, stride):
    n, w = lat.shape
    stored = 13 * n * w * 4 <= 40 * 1024 * 1024
    kernel = functools.partial(thermal_kernel, stride=stride, stored=stored, zero_start=temp is None)
    return pl.pallas_call(
        kernel,
        out_shape=jax.ShapeDtypeStruct((n, w), jnp.float32),
        scratch_shapes=[pltpu.VMEM((n, w), jnp.float32) for _ in range(8 if stored else 4)],
        compiler_params=pltpu.CompilerParams(vmem_limit_bytes=60 * 1024 * 1024),
        interpret=INTERPRET,
    )(*([] if temp is None else [temp]), source, lat, vert, row_ok)


def inside_of(start, count, total):
    idx = start + jnp.arange(count, dtype=jnp.int32)
    return (idx >= 0) & (idx < total)


def body(demand, leakage, conductance, vias, layer_of, lateral_k, vertical_k):
    tile_rows, tile_cols = demand.shape
    group_layers, cell_rows, therm_cols = lateral_k.shape
    cell_cols = tile_cols // COARSE
    n_r = lax.axis_size("row")
    n_c = lax.axis_size("col")
    r_idx = lax.axis_index("row")
    c_idx = lax.axis_index("col")
    all_layers = group_layers * n_c
    all_rows = cell_rows * n_r
    total_rows = tile_rows * n_r
    total_cols = tile_cols * n_c

    T0 = 2 * HEAT_SWEEPS
    T1 = HEAT_SWEEPS
    H0 = T0 - 1
    H1 = T1 - 1
    S = SWEEPS
    R1 = H1 * COARSE + SWEEPS
    R0 = max(H0 * COARSE, R1) + SWEEPS
    CW = 64
    PR = -(-R1 // COARSE)
    PC = CW // COARSE

    via_g = VIA_CONDUCT * vias.astype(jnp.float32)
    load0 = demand + leakage

    p0 = extended(jnp.stack([conductance, load0, via_g]), (("row", 1, R0), ("col", 2, CW)))
    p1 = extended(jnp.stack([demand, leakage]), (("row", 1, R1), ("col", 2, CW)))
    k_ext = extended(jnp.stack([lateral_k, vertical_k]), (("col", 1, T1), ("row", 2, T0)))
    layer_ext = extended(layer_of, (("row", 0, T0),))

    cols_w = tile_cols + 2 * CW
    col_ok = inside_of(c_idx * tile_cols - CW, cols_w, total_cols).astype(jnp.float32)[None, :]

    rows0 = tile_rows + 2 * R0
    row_ok0 = inside_of(r_idx * tile_rows - R0, rows0, total_rows).astype(jnp.float32)[:, None]
    drop0 = run_power(None, p0, row_ok0, col_ok)
    hr0 = H0 * COARSE
    rs = slice(R0 - hr0, R0 + tile_rows + hr0)
    cs = slice(CW, CW + tile_cols)
    d_h = drop0[rs, cs]
    heat0 = coarse_of(p0[1][rs, cs] * (1.0 - d_h) + p0[0][rs, cs] * d_h * d_h)

    def gather_heat(heat):
        copies = jnp.broadcast_to(heat[None], (n_c,) + heat.shape)
        gathered = lax.all_to_all(copies, "col", split_axis=0, concat_axis=0, tiled=True)
        gathered = gathered.transpose(1, 0, 2).reshape(heat.shape[0], n_c * cell_cols)
        return jnp.pad(gathered, ((1, 1), (0, 0)))

    def thermal(temp_ext, heat_ext, halo):
        layers = group_layers + 2 * T1
        rows = cell_rows + 2 * halo
        ks = k_ext[:, :, T0 - halo:T0 + cell_rows + halo]
        tlay = c_idx * group_layers - T1 + jnp.arange(layers, dtype=jnp.int32)
        inside = inside_of(c_idx * group_layers - T1, layers, all_layers)[:, None] & inside_of(r_idx * cell_rows - halo, rows, all_rows)[None, :]
        lay_in = layer_ext[T0 - halo:T0 + cell_rows + halo]
        picker = (lay_in[None, :, :] == tlay[:, None, None]) & inside[:, :, None]
        source = jnp.where(picker, heat_ext[None, :, :], 0.0)
        flat = (layers * rows, therm_cols)
        out = run_thermal(
            None if temp_ext is None else temp_ext.reshape(flat), source.reshape(flat), ks[0].reshape(flat), ks[1].reshape(flat),
            inside.astype(jnp.float32).reshape(layers * rows, 1), rows // 8,
        )
        return out.reshape(layers, rows, therm_cols)

    temp0 = thermal(None, gather_heat(heat0), T0)
    temp0 = temp0[T1:T1 + group_layers, T0 - T1:T0 + cell_rows + T1]

    own_layers = c_idx * group_layers + jnp.arange(group_layers, dtype=jnp.int32)
    t_own = temp0[:, T1 - PR:T1 + cell_rows + PR]
    lay_w = layer_ext[T0 - PR:T0 + cell_rows + PR]
    partial = jnp.sum(jnp.where(lay_w[None, :, :] == own_layers[:, None, None], t_own, 0.0), axis=0)
    partial = jnp.pad(partial, ((0, 0), (PC, PC)))
    windows = jnp.stack([partial[:, j * cell_cols:j * cell_cols + cell_cols + 2 * PC] for j in range(n_c)])
    windows = lax.all_to_all(windows, "col", split_axis=0, concat_axis=0, tiled=True)
    cell_temp = jnp.sum(windows, axis=0)

    denom_c = 1.0 + COND_SLOPE * cell_temp
    grow_c = jnp.exp(LEAK_SLOPE * cell_temp)
    rows1 = tile_rows + 2 * R1
    fo = PR * COARSE - R1
    denom_f = fine_of(denom_c, cols_w)[fo:fo + rows1]
    grow_f = fine_of(grow_c, cols_w)[fo:fo + rows1]
    rs1 = slice(R0 - R1, R0 - R1 + rows1)
    cond1 = p0[0][rs1] / denom_f
    load1 = p1[0] + p1[1] * grow_f
    row_ok1 = inside_of(r_idx * tile_rows - R1, rows1, total_rows).astype(jnp.float32)[:, None]
    drop1 = run_power(drop0[rs1], (cond1, load1, p0[2][rs1]), row_ok1, col_ok)
    hr1 = H1 * COARSE
    rh = slice(R1 - hr1, R1 + tile_rows + hr1)
    d_h1 = drop1[rh, cs]
    heat1 = coarse_of(load1[rh, cs] * (1.0 - d_h1) + cond1[rh, cs] * d_h1 * d_h1)
    temp1 = thermal(extended(temp0, (("col", 0, T1),)), gather_heat(heat1), T1)
    temp_out = temp1[T1:T1 + group_layers, T1:T1 + cell_rows]
    drop_out = drop1[R1:R1 + tile_rows, cs]
    return (drop_out, temp_out)


def solution(mesh):
    in_specs = (
        P("row", "col"),
        P("row", "col"),
        P("row", "col"),
        P("row", "col"),
        P("row", None),
        P("col", "row", None),
        P("col", "row", None),
    )
    out_specs = (P("row", "col"), P("col", "row", None))
    return jax.shard_map(body, mesh=mesh, in_specs=in_specs, out_specs=out_specs, check_vma=False)
```

```python
import functools
import os

import jax
import jax.numpy as jnp
from jax import lax
from jax.experimental import pallas as pl
from jax.experimental.pallas import tpu as pltpu
from jax.sharding import PartitionSpec as P

INTERPRET = os.environ.get("SOL_INTERPRET") == "1"
UNROLL = 8

COARSE = 8
SWEEPS = 4
HEAT_SWEEPS = 4
OUTER = 2


COND_SLOPE = 0.5
LEAK_SLOPE = 0.7
VIA_CONDUCT = 4.0

HALO = 4


def extended(block, sides):
    for axis, dim, width in sides:
        count = lax.axis_size(axis)
        forward = [(i, i + 1) for i in range(count - 1)]
        backward = [(target, source) for source, target in forward]
        low = lax.ppermute(
            lax.slice_in_dim(block, block.shape[dim] - width, None, axis=dim), axis, forward
        )
        high = lax.ppermute(lax.slice_in_dim(block, 0, width, axis=dim), axis, backward)
        block = jnp.concatenate([low, block, high], axis=dim)
    return block


def spread_cols(coarse, fine_cols):
    n = coarse.shape[1]
    ids = jnp.arange(fine_cols, dtype=jnp.int32) // COARSE
    onehot = (jnp.arange(n, dtype=jnp.int32)[:, None] == ids[None, :]).astype(jnp.float32)
    return jnp.dot(coarse, onehot, precision=lax.Precision.HIGHEST)


def fine_of(coarse, fine_cols):
    wide = spread_cols(coarse, fine_cols)
    rows = wide.shape[0]
    return jnp.broadcast_to(wide[:, None, :], (rows, COARSE, fine_cols)).reshape(rows * COARSE, fine_cols)


def coarse_of(fine):
    rows, cols = fine.shape
    summed_rows = jnp.sum(fine.reshape(rows // COARSE, COARSE, cols), axis=1)
    n = cols // COARSE
    ids = jnp.arange(cols, dtype=jnp.int32) // COARSE
    onehot = (ids[:, None] == jnp.arange(n, dtype=jnp.int32)[None, :]).astype(jnp.float32)
    return jnp.dot(summed_rows, onehot, precision=lax.Precision.HIGHEST) * (1.0 / (COARSE * COARSE))


def row_above(x, above):
    sub = lax.broadcasted_iota(jnp.int32, x.shape, 0)
    edge = jnp.broadcast_to(above[x.shape[0] - 1:, :], x.shape)
    return jnp.where(sub == 0, edge, pltpu.roll(x, 1, 0))


def row_below(x, below):
    n = x.shape[0]
    sub = lax.broadcasted_iota(jnp.int32, x.shape, 0)
    edge = jnp.broadcast_to(below[:1, :], x.shape)
    return jnp.where(sub == n - 1, edge, pltpu.roll(x, n - 1, 0))


def rows_of(k):
    return pl.ds(pl.multiple_of(k * 8, 8), 8)


def chunk(ref, k, count):
    return ref[rows_of(jnp.clip(k, 0, count - 1)), :]


def power_kernel(*refs, zero_start, stacked, offset):
    refs = list(refs)
    d_ref = None if zero_start else refs.pop(0)
    if stacked:
        p_ref = refs.pop(0)
        c_ref, l_ref, v_ref = p_ref.at[0], p_ref.at[1], p_ref.at[2]
    else:
        c_ref, l_ref, v_ref = refs.pop(0), refs.pop(0), refs.pop(0)
        v_ref = v_ref.at[2]
    rok_ref, cok_ref, o_ref, wn_ref, ws_ref, ww_ref, we_ref, inv_ref, buf_ref = refs
    n, w = o_ref.shape
    count = n // 8

    def weights(k, carry):
        sl = rows_of(k)
        x = c_ref[sl, :]
        a = (x + row_above(x, chunk(c_ref, k - 1, count))) * 0.5
        b = (x + row_below(x, chunk(c_ref, k + 1, count))) * 0.5
        e = (x + pltpu.roll(x, 1, 1)) * 0.5
        f = (x + pltpu.roll(x, w - 1, 1)) * 0.5
        wn_ref[sl, :] = a
        ws_ref[sl, :] = b
        ww_ref[sl, :] = e
        we_ref[sl, :] = f
        ok = (rok_ref[sl, :] > 0.5) & (cok_ref[...] > 0.5)
        inv = jnp.where(ok, 1.0 / (a + b + e + f + v_ref[rows_of(k + offset), :]), 0.0)
        inv_ref[sl, :] = inv
        if zero_start:
            buf_ref[sl, :] = jnp.where(inv != 0.0, l_ref[sl, :] * inv, 0.0)
        return carry

    lax.fori_loop(0, count, weights, 0, unroll=UNROLL)

    def sweep(src, dst):
        def body(k, carry):
            sl = rows_of(k)
            x = src[sl, :]
            summed = (
                l_ref[sl, :]
                + wn_ref[sl, :] * row_above(x, chunk(src, k - 1, count))
                + ws_ref[sl, :] * row_below(x, chunk(src, k + 1, count))
                + ww_ref[sl, :] * pltpu.roll(x, 1, 1)
                + we_ref[sl, :] * pltpu.roll(x, w - 1, 1)
            )
            inv = inv_ref[sl, :]
            dst[sl, :] = jnp.where(inv != 0.0, summed * inv, 0.0)
            return carry

        lax.fori_loop(0, count, body, 0, unroll=UNROLL)

    def first_sweep(k, carry):
        sl = rows_of(k)
        x = d_ref[rows_of(k + offset), :]
        summed = (
            l_ref[sl, :]
            + wn_ref[sl, :] * row_above(x, d_ref[rows_of(jnp.maximum(k - 1, 0) + offset), :])
            + ws_ref[sl, :] * row_below(x, d_ref[rows_of(jnp.minimum(k + 1, count - 1) + offset), :])
            + ww_ref[sl, :] * pltpu.roll(x, 1, 1)
            + we_ref[sl, :] * pltpu.roll(x, w - 1, 1)
        )
        inv = inv_ref[sl, :]
        buf_ref[sl, :] = jnp.where(inv != 0.0, summed * inv, 0.0)
        return carry

    if not zero_start:
        lax.fori_loop(0, count, first_sweep, 0, unroll=UNROLL)
    sweep(buf_ref, o_ref)
    sweep(o_ref, buf_ref)
    sweep(buf_ref, o_ref)


def run_power(drop, parts, row_ok, col_ok, offset=0):
    stacked = not isinstance(parts, (tuple, list))
    n, w = parts.shape[1:] if stacked else parts[0].shape
    operands = ([] if drop is None else [drop]) + ([parts] if stacked else list(parts)) + [row_ok, col_ok]
    kernel = functools.partial(power_kernel, zero_start=drop is None, stacked=stacked, offset=offset)
    return pl.pallas_call(
        kernel,
        out_shape=jax.ShapeDtypeStruct((n, w), jnp.float32),
        scratch_shapes=[pltpu.VMEM((n, w), jnp.float32) for _ in range(6)],
        compiler_params=pltpu.CompilerParams(vmem_limit_bytes=60 * 1024 * 1024),
        interpret=INTERPRET,
    )(*operands)


def thermal_kernel(*refs, stride, stored, zero_start):
    refs = list(refs)
    t_ref = None if zero_start else refs.pop(0)
    s_ref, lk_ref, vk_ref, rok_ref, o_ref = refs[:5]
    scratch = refs[5:]
    n, w = lk_ref.shape
    count = n // 8
    lane = lax.broadcasted_iota(jnp.int32, (8, w), 1)
    first = lane == 0
    last = lane == w - 1
    if stored:
        wn_ref, ws_ref, ww_ref, we_ref, wb_ref, wa_ref, inv_ref, buf_ref = scratch
    else:
        wb_ref, wa_ref, inv_ref, buf_ref = scratch

    def lateral(x, k, ref):
        up = row_above(x, chunk(ref, k - 1, count))
        dn = row_below(x, chunk(ref, k + 1, count))
        lf = jnp.where(first, 0.0, pltpu.roll(x, 1, 1))
        rt = jnp.where(last, 0.0, pltpu.roll(x, w - 1, 1))
        return up, dn, lf, rt

    def lateral_weights(k):
        sl = rows_of(k)
        x = lk_ref[sl, :]
        up, dn, lf, rt = lateral(x, k, lk_ref)
        return (x + up) * 0.5, (x + dn) * 0.5, (x + lf) * 0.5, (x + rt) * 0.5

    def weights(k, carry):
        sl = rows_of(k)
        a, b, e, f = lateral_weights(k)
        if stored:
            wn_ref[sl, :] = a
            ws_ref[sl, :] = b
            ww_ref[sl, :] = e
            we_ref[sl, :] = f
        v = vk_ref[sl, :]
        lo = (v + chunk(vk_ref, k - stride, count)) * 0.5
        hi = (v + chunk(vk_ref, k + stride, count)) * 0.5
        wb_ref[sl, :] = lo
        wa_ref[sl, :] = hi
        inv = jnp.where(rok_ref[sl, :] > 0.5, 1.0 / (a + b + e + f + lo + hi), 0.0)
        inv_ref[sl, :] = inv
        if zero_start:
            buf_ref[sl, :] = jnp.where(inv != 0.0, s_ref[sl, :] * inv, 0.0)
        return carry

    lax.fori_loop(0, count, weights, 0, unroll=UNROLL)

    def sweep(src, dst):
        def body(k, carry):
            sl = rows_of(k)
            if stored:
                a, b, e, f = wn_ref[sl, :], ws_ref[sl, :], ww_ref[sl, :], we_ref[sl, :]
            else:
                a, b, e, f = lateral_weights(k)
            x = src[sl, :]
            up, dn, lf, rt = lateral(x, k, src)
            summed = (
                s_ref[sl, :]
                + a * up
                + b * dn
                + e * lf
                + f * rt
                + wb_ref[sl, :] * chunk(src, k - stride, count)
                + wa_ref[sl, :] * chunk(src, k + stride, count)
            )
            inv = inv_ref[sl, :]
            dst[sl, :] = jnp.where(inv != 0.0, summed * inv, 0.0)
            return carry

        lax.fori_loop(0, count, body, 0, unroll=UNROLL)

    if not zero_start:
        sweep(t_ref, buf_ref)
    sweep(buf_ref, o_ref)
    sweep(o_ref, buf_ref)
    sweep(buf_ref, o_ref)


def run_thermal(temp, source, lat, vert, row_ok, stride):
    n, w = lat.shape
    stored = 13 * n * w * 4 <= 40 * 1024 * 1024
    kernel = functools.partial(thermal_kernel, stride=stride, stored=stored, zero_start=temp is None)
    return pl.pallas_call(
        kernel,
        out_shape=jax.ShapeDtypeStruct((n, w), jnp.float32),
        scratch_shapes=[pltpu.VMEM((n, w), jnp.float32) for _ in range(8 if stored else 4)],
        compiler_params=pltpu.CompilerParams(vmem_limit_bytes=60 * 1024 * 1024),
        interpret=INTERPRET,
    )(*([] if temp is None else [temp]), source, lat, vert, row_ok)


def inside_of(start, count, total):
    idx = start + jnp.arange(count, dtype=jnp.int32)
    return (idx >= 0) & (idx < total)


def body(demand, leakage, conductance, vias, layer_of, lateral_k, vertical_k):
    tile_rows, tile_cols = demand.shape
    group_layers, cell_rows, therm_cols = lateral_k.shape
    cell_cols = tile_cols // COARSE
    n_r = lax.axis_size("row")
    n_c = lax.axis_size("col")
    r_idx = lax.axis_index("row")
    c_idx = lax.axis_index("col")
    all_layers = group_layers * n_c
    all_rows = cell_rows * n_r
    total_rows = tile_rows * n_r
    total_cols = tile_cols * n_c

    T0 = 2 * HEAT_SWEEPS
    T1 = HEAT_SWEEPS
    H0 = T0 - 1
    H1 = T1 - 1
    S = SWEEPS
    R1 = H1 * COARSE + SWEEPS
    R0 = max(H0 * COARSE, R1) + SWEEPS
    CW = 64
    PR = -(-R1 // COARSE)
    PC = CW // COARSE

    via_g = VIA_CONDUCT * vias.astype(jnp.float32)
    load0 = demand + leakage

    p0 = extended(jnp.stack([conductance, load0, via_g]), (("row", 1, R0), ("col", 2, CW)))
    p1 = extended(jnp.stack([demand, leakage]), (("row", 1, R1), ("col", 2, CW)))
    k_ext = extended(jnp.stack([lateral_k, vertical_k]), (("col", 1, T1), ("row", 2, T0)))
    layer_ext = extended(layer_of, (("row", 0, T0),))

    cols_w = tile_cols + 2 * CW
    col_ok = inside_of(c_idx * tile_cols - CW, cols_w, total_cols).astype(jnp.float32)[None, :]

    rows0 = tile_rows + 2 * R0
    row_ok0 = inside_of(r_idx * tile_rows - R0, rows0, total_rows).astype(jnp.float32)[:, None]
    drop0 = run_power(None, p0, row_ok0, col_ok)
    hr0 = H0 * COARSE
    rs = slice(R0 - hr0, R0 + tile_rows + hr0)
    cs = slice(CW, CW + tile_cols)
    d_h = drop0[rs, cs]
    heat0 = coarse_of(p0[1][rs, cs] * (1.0 - d_h) + p0[0][rs, cs] * d_h * d_h)

    def gather_heat(heat):
        copies = jnp.broadcast_to(heat[None], (n_c,) + heat.shape)
        gathered = lax.all_to_all(copies, "col", split_axis=0, concat_axis=0, tiled=True)
        gathered = gathered.transpose(1, 0, 2).reshape(heat.shape[0], n_c * cell_cols)
        return jnp.pad(gathered, ((1, 1), (0, 0)))

    def thermal(temp_ext, heat_ext, halo):
        layers = group_layers + 2 * T1
        rows = cell_rows + 2 * halo
        ks = k_ext[:, :, T0 - halo:T0 + cell_rows + halo]
        tlay = c_idx * group_layers - T1 + jnp.arange(layers, dtype=jnp.int32)
        inside = inside_of(c_idx * group_layers - T1, layers, all_layers)[:, None] & inside_of(r_idx * cell_rows - halo, rows, all_rows)[None, :]
        lay_in = layer_ext[T0 - halo:T0 + cell_rows + halo]
        picker = (lay_in[None, :, :] == tlay[:, None, None]) & inside[:, :, None]
        source = jnp.where(picker, heat_ext[None, :, :], 0.0)
        flat = (layers * rows, therm_cols)
        out = run_thermal(
            None if temp_ext is None else temp_ext.reshape(flat), source.reshape(flat), ks[0].reshape(flat), ks[1].reshape(flat),
            inside.astype(jnp.float32).reshape(layers * rows, 1), rows // 8,
        )
        return out.reshape(layers, rows, therm_cols)

    temp0 = thermal(None, gather_heat(heat0), T0)
    temp0 = temp0[T1:T1 + group_layers, T0 - T1:T0 + cell_rows + T1]

    own_layers = c_idx * group_layers + jnp.arange(group_layers, dtype=jnp.int32)
    t_own = temp0[:, T1 - PR:T1 + cell_rows + PR]
    lay_w = layer_ext[T0 - PR:T0 + cell_rows + PR]
    partial = jnp.sum(jnp.where(lay_w[None, :, :] == own_layers[:, None, None], t_own, 0.0), axis=0)
    partial = jnp.pad(partial, ((0, 0), (PC, PC)))
    windows = jnp.stack([partial[:, j * cell_cols:j * cell_cols + cell_cols + 2 * PC] for j in range(n_c)])
    windows = lax.all_to_all(windows, "col", split_axis=0, concat_axis=0, tiled=True)
    cell_temp = jnp.sum(windows, axis=0)

    denom_c = 1.0 + COND_SLOPE * cell_temp
    grow_c = jnp.exp(LEAK_SLOPE * cell_temp)
    rows1 = tile_rows + 2 * R1
    fo = PR * COARSE - R1
    denom_f = fine_of(denom_c, cols_w)[fo:fo + rows1]
    grow_f = fine_of(grow_c, cols_w)[fo:fo + rows1]
    rs1 = slice(R0 - R1, R0 - R1 + rows1)
    cond1 = p0[0][rs1] / denom_f
    load1 = p1[0] + p1[1] * grow_f
    row_ok1 = inside_of(r_idx * tile_rows - R1, rows1, total_rows).astype(jnp.float32)[:, None]
    drop1 = run_power(drop0, (cond1, load1, p0), row_ok1, col_ok, offset=(R0 - R1) // 8)
    hr1 = H1 * COARSE
    rh = slice(R1 - hr1, R1 + tile_rows + hr1)
    d_h1 = drop1[rh, cs]
    heat1 = coarse_of(load1[rh, cs] * (1.0 - d_h1) + cond1[rh, cs] * d_h1 * d_h1)
    temp1 = thermal(extended(temp0, (("col", 0, T1),)), gather_heat(heat1), T1)
    temp_out = temp1[T1:T1 + group_layers, T1:T1 + cell_rows]
    drop_out = drop1[R1:R1 + tile_rows, cs]
    return (drop_out, temp_out)


def solution(mesh):
    in_specs = (
        P("row", "col"),
        P("row", "col"),
        P("row", "col"),
        P("row", "col"),
        P("row", None),
        P("col", "row", None),
        P("col", "row", None),
    )
    out_specs = (P("row", "col"), P("col", "row", None))
    return jax.shard_map(body, mesh=mesh, in_specs=in_specs, out_specs=out_specs, check_vma=False)
```

```python
import functools
import os

import jax
import jax.numpy as jnp
from jax import lax
from jax.experimental import pallas as pl
from jax.experimental.pallas import tpu as pltpu
from jax.sharding import PartitionSpec as P

INTERPRET = os.environ.get("SOL_INTERPRET") == "1"
UNROLL = 8

COARSE = 8
SWEEPS = 4
HEAT_SWEEPS = 4
OUTER = 2


COND_SLOPE = 0.5
LEAK_SLOPE = 0.7
VIA_CONDUCT = 4.0

HALO = 4


def extended(block, sides):
    for axis, dim, width in sides:
        count = lax.axis_size(axis)
        forward = [(i, i + 1) for i in range(count - 1)]
        backward = [(target, source) for source, target in forward]
        low = lax.ppermute(
            lax.slice_in_dim(block, block.shape[dim] - width, None, axis=dim), axis, forward
        )
        high = lax.ppermute(lax.slice_in_dim(block, 0, width, axis=dim), axis, backward)
        block = jnp.concatenate([low, block, high], axis=dim)
    return block


def spread_cols(coarse, fine_cols):
    n = coarse.shape[1]
    ids = jnp.arange(fine_cols, dtype=jnp.int32) // COARSE
    onehot = (jnp.arange(n, dtype=jnp.int32)[:, None] == ids[None, :]).astype(jnp.float32)
    return jnp.dot(coarse, onehot, precision=lax.Precision.HIGHEST)


def fine_of(coarse, fine_cols):
    wide = spread_cols(coarse, fine_cols)
    rows = wide.shape[0]
    return jnp.broadcast_to(wide[:, None, :], (rows, COARSE, fine_cols)).reshape(rows * COARSE, fine_cols)


def coarse_of(fine):
    rows, cols = fine.shape
    summed_rows = jnp.sum(fine.reshape(rows // COARSE, COARSE, cols), axis=1)
    n = cols // COARSE
    ids = jnp.arange(cols, dtype=jnp.int32) // COARSE
    onehot = (ids[:, None] == jnp.arange(n, dtype=jnp.int32)[None, :]).astype(jnp.float32)
    return jnp.dot(summed_rows, onehot, precision=lax.Precision.HIGHEST) * (1.0 / (COARSE * COARSE))


def row_above(x, above):
    sub = lax.broadcasted_iota(jnp.int32, x.shape, 0)
    edge = jnp.broadcast_to(above[x.shape[0] - 1:, :], x.shape)
    return jnp.where(sub == 0, edge, pltpu.roll(x, 1, 0))


def row_below(x, below):
    n = x.shape[0]
    sub = lax.broadcasted_iota(jnp.int32, x.shape, 0)
    edge = jnp.broadcast_to(below[:1, :], x.shape)
    return jnp.where(sub == n - 1, edge, pltpu.roll(x, n - 1, 0))


def rows_of(k):
    return pl.ds(pl.multiple_of(k * 8, 8), 8)


def chunk(ref, k, count):
    return ref[rows_of(jnp.clip(k, 0, count - 1)), :]


def power_kernel(*refs, zero_start, stacked, offset):
    refs = list(refs)
    d_ref = None if zero_start else refs.pop(0)
    if stacked:
        p_ref = refs.pop(0)
        c_ref, l_ref, v_ref = p_ref.at[0], p_ref.at[1], p_ref.at[2]
    else:
        c_ref, l_ref, v_ref = refs.pop(0), refs.pop(0), refs.pop(0)
        v_ref = v_ref.at[2]
    rok_ref, cok_ref, o_ref, wn_ref, ws_ref, ww_ref, we_ref, inv_ref, buf_ref = refs
    n, w = o_ref.shape
    count = n // 8

    def weights(k, carry):
        sl = rows_of(k)
        x = c_ref[sl, :]
        a = (x + row_above(x, chunk(c_ref, k - 1, count))) * 0.5
        b = (x + row_below(x, chunk(c_ref, k + 1, count))) * 0.5
        e = (x + pltpu.roll(x, 1, 1)) * 0.5
        f = (x + pltpu.roll(x, w - 1, 1)) * 0.5
        wn_ref[sl, :] = a
        ws_ref[sl, :] = b
        ww_ref[sl, :] = e
        we_ref[sl, :] = f
        ok = (rok_ref[sl, :] > 0.5) & (cok_ref[...] > 0.5)
        inv = jnp.where(ok, 1.0 / (a + b + e + f + v_ref[rows_of(k + offset), :]), 0.0)
        inv_ref[sl, :] = inv
        if zero_start:
            buf_ref[sl, :] = jnp.where(inv != 0.0, l_ref[sl, :] * inv, 0.0)
        return carry

    lax.fori_loop(0, count, weights, 0, unroll=UNROLL)

    def sweep(src, dst):
        def body(k, carry):
            sl = rows_of(k)
            x = src[sl, :]
            summed = (
                l_ref[sl, :]
                + wn_ref[sl, :] * row_above(x, chunk(src, k - 1, count))
                + ws_ref[sl, :] * row_below(x, chunk(src, k + 1, count))
                + ww_ref[sl, :] * pltpu.roll(x, 1, 1)
                + we_ref[sl, :] * pltpu.roll(x, w - 1, 1)
            )
            inv = inv_ref[sl, :]
            dst[sl, :] = jnp.where(inv != 0.0, summed * inv, 0.0)
            return carry

        lax.fori_loop(0, count, body, 0, unroll=UNROLL)

    def first_sweep(k, carry):
        sl = rows_of(k)
        x = d_ref[rows_of(k + offset), :]
        summed = (
            l_ref[sl, :]
            + wn_ref[sl, :] * row_above(x, d_ref[rows_of(jnp.maximum(k - 1, 0) + offset), :])
            + ws_ref[sl, :] * row_below(x, d_ref[rows_of(jnp.minimum(k + 1, count - 1) + offset), :])
            + ww_ref[sl, :] * pltpu.roll(x, 1, 1)
            + we_ref[sl, :] * pltpu.roll(x, w - 1, 1)
        )
        inv = inv_ref[sl, :]
        buf_ref[sl, :] = jnp.where(inv != 0.0, summed * inv, 0.0)
        return carry

    if not zero_start:
        lax.fori_loop(0, count, first_sweep, 0, unroll=UNROLL)
    sweep(buf_ref, o_ref)
    sweep(o_ref, buf_ref)
    sweep(buf_ref, o_ref)


def run_power(drop, parts, row_ok, col_ok, offset=0):
    stacked = not isinstance(parts, (tuple, list))
    n, w = parts.shape[1:] if stacked else parts[0].shape
    operands = ([] if drop is None else [drop]) + ([parts] if stacked else list(parts)) + [row_ok, col_ok]
    kernel = functools.partial(power_kernel, zero_start=drop is None, stacked=stacked, offset=offset)
    return pl.pallas_call(
        kernel,
        out_shape=jax.ShapeDtypeStruct((n, w), jnp.float32),
        scratch_shapes=[pltpu.VMEM((n, w), jnp.float32) for _ in range(6)],
        compiler_params=pltpu.CompilerParams(vmem_limit_bytes=60 * 1024 * 1024),
        interpret=INTERPRET,
    )(*operands)


def thermal_kernel(*refs, stride, stored, zero_start):
    refs = list(refs)
    t_ref = None if zero_start else refs.pop(0)
    s_ref, lk_ref, vk_ref, rok_ref, o_ref = refs[:5]
    scratch = refs[5:]
    n, w = lk_ref.shape
    count = n // 8
    lane = lax.broadcasted_iota(jnp.int32, (8, w), 1)
    first = lane == 0
    last = lane == w - 1
    if stored:
        wn_ref, ws_ref, ww_ref, we_ref, wb_ref, wa_ref, inv_ref, buf_ref = scratch
    else:
        wb_ref, wa_ref, inv_ref, buf_ref = scratch

    def lateral(x, k, ref):
        up = row_above(x, chunk(ref, k - 1, count))
        dn = row_below(x, chunk(ref, k + 1, count))
        lf = jnp.where(first, 0.0, pltpu.roll(x, 1, 1))
        rt = jnp.where(last, 0.0, pltpu.roll(x, w - 1, 1))
        return up, dn, lf, rt

    def lateral_weights(k):
        sl = rows_of(k)
        x = lk_ref[sl, :]
        up, dn, lf, rt = lateral(x, k, lk_ref)
        return (x + up) * 0.5, (x + dn) * 0.5, (x + lf) * 0.5, (x + rt) * 0.5

    def weights(k, carry):
        sl = rows_of(k)
        a, b, e, f = lateral_weights(k)
        if stored:
            wn_ref[sl, :] = a
            ws_ref[sl, :] = b
            ww_ref[sl, :] = e
            we_ref[sl, :] = f
        v = vk_ref[sl, :]
        lo = (v + chunk(vk_ref, k - stride, count)) * 0.5
        hi = (v + chunk(vk_ref, k + stride, count)) * 0.5
        wb_ref[sl, :] = lo
        wa_ref[sl, :] = hi
        inv = jnp.where(rok_ref[sl, :] > 0.5, 1.0 / (a + b + e + f + lo + hi), 0.0)
        inv_ref[sl, :] = inv
        if zero_start:
            buf_ref[sl, :] = jnp.where(inv != 0.0, s_ref[sl, :] * inv, 0.0)
        return carry

    lax.fori_loop(0, count, weights, 0, unroll=UNROLL)

    def sweep(src, dst):
        def body(k, carry):
            sl = rows_of(k)
            if stored:
                a, b, e, f = wn_ref[sl, :], ws_ref[sl, :], ww_ref[sl, :], we_ref[sl, :]
            else:
                a, b, e, f = lateral_weights(k)
            x = src[sl, :]
            up, dn, lf, rt = lateral(x, k, src)
            summed = (
                s_ref[sl, :]
                + a * up
                + b * dn
                + e * lf
                + f * rt
                + wb_ref[sl, :] * chunk(src, k - stride, count)
                + wa_ref[sl, :] * chunk(src, k + stride, count)
            )
            inv = inv_ref[sl, :]
            dst[sl, :] = jnp.where(inv != 0.0, summed * inv, 0.0)
            return carry

        lax.fori_loop(0, count, body, 0, unroll=UNROLL)

    if not zero_start:
        sweep(t_ref, buf_ref)
    sweep(buf_ref, o_ref)
    sweep(o_ref, buf_ref)
    sweep(buf_ref, o_ref)


def run_thermal(temp, source, lat, vert, row_ok, stride):
    n, w = lat.shape
    stored = 13 * n * w * 4 <= 40 * 1024 * 1024
    kernel = functools.partial(thermal_kernel, stride=stride, stored=stored, zero_start=temp is None)
    return pl.pallas_call(
        kernel,
        out_shape=jax.ShapeDtypeStruct((n, w), jnp.float32),
        scratch_shapes=[pltpu.VMEM((n, w), jnp.float32) for _ in range(8 if stored else 4)],
        compiler_params=pltpu.CompilerParams(vmem_limit_bytes=60 * 1024 * 1024),
        interpret=INTERPRET,
    )(*([] if temp is None else [temp]), source, lat, vert, row_ok)


def inside_of(start, count, total):
    idx = start + jnp.arange(count, dtype=jnp.int32)
    return (idx >= 0) & (idx < total)


def body(demand, leakage, conductance, vias, layer_of, lateral_k, vertical_k):
    tile_rows, tile_cols = demand.shape
    group_layers, cell_rows, therm_cols = lateral_k.shape
    cell_cols = tile_cols // COARSE
    n_r = lax.axis_size("row")
    n_c = lax.axis_size("col")
    r_idx = lax.axis_index("row")
    c_idx = lax.axis_index("col")
    all_layers = group_layers * n_c
    all_rows = cell_rows * n_r
    total_rows = tile_rows * n_r
    total_cols = tile_cols * n_c

    T0 = 2 * HEAT_SWEEPS
    T1 = HEAT_SWEEPS
    H0 = T0 - 1
    H1 = T1 - 1
    S = SWEEPS
    R1 = H1 * COARSE + SWEEPS
    R0 = max(H0 * COARSE, R1) + SWEEPS
    CW = 64
    PR = -(-R1 // COARSE)
    PC = CW // COARSE

    via_g = VIA_CONDUCT * vias.astype(jnp.float32)
    load0 = demand + leakage

    p0 = extended(jnp.stack([conductance, load0, via_g]), (("row", 1, R0), ("col", 2, CW)))
    k_in, p0 = lax.optimization_barrier((jnp.stack([lateral_k, vertical_k]), p0))
    k_ext = extended(k_in, (("col", 1, T1), ("row", 2, T0)))

    cols_w = tile_cols + 2 * CW
    col_ok = inside_of(c_idx * tile_cols - CW, cols_w, total_cols).astype(jnp.float32)[None, :]

    rows0 = tile_rows + 2 * R0
    row_ok0 = inside_of(r_idx * tile_rows - R0, rows0, total_rows).astype(jnp.float32)[:, None]
    drop0 = run_power(None, p0, row_ok0, col_ok)
    p1_in, layer_in, drop0 = lax.optimization_barrier((jnp.stack([demand, leakage]), layer_of, drop0))
    p1 = extended(p1_in, (("row", 1, R1), ("col", 2, CW)))
    layer_ext = extended(layer_in, (("row", 0, T0),))
    hr0 = H0 * COARSE
    rs = slice(R0 - hr0, R0 + tile_rows + hr0)
    cs = slice(CW, CW + tile_cols)
    d_h = drop0[rs, cs]
    heat0 = coarse_of(p0[1][rs, cs] * (1.0 - d_h) + p0[0][rs, cs] * d_h * d_h)

    def gather_heat(heat):
        copies = jnp.broadcast_to(heat[None], (n_c,) + heat.shape)
        gathered = lax.all_to_all(copies, "col", split_axis=0, concat_axis=0, tiled=True)
        gathered = gathered.transpose(1, 0, 2).reshape(heat.shape[0], n_c * cell_cols)
        return jnp.pad(gathered, ((1, 1), (0, 0)))

    def thermal(temp_ext, heat_ext, halo):
        layers = group_layers + 2 * T1
        rows = cell_rows + 2 * halo
        ks = k_ext[:, :, T0 - halo:T0 + cell_rows + halo]
        tlay = c_idx * group_layers - T1 + jnp.arange(layers, dtype=jnp.int32)
        inside = inside_of(c_idx * group_layers - T1, layers, all_layers)[:, None] & inside_of(r_idx * cell_rows - halo, rows, all_rows)[None, :]
        lay_in = layer_ext[T0 - halo:T0 + cell_rows + halo]
        picker = (lay_in[None, :, :] == tlay[:, None, None]) & inside[:, :, None]
        source = jnp.where(picker, heat_ext[None, :, :], 0.0)
        flat = (layers * rows, therm_cols)
        out = run_thermal(
            None if temp_ext is None else temp_ext.reshape(flat), source.reshape(flat), ks[0].reshape(flat), ks[1].reshape(flat),
            inside.astype(jnp.float32).reshape(layers * rows, 1), rows // 8,
        )
        return out.reshape(layers, rows, therm_cols)

    temp0 = thermal(None, gather_heat(heat0), T0)
    temp0 = temp0[T1:T1 + group_layers, T0 - T1:T0 + cell_rows + T1]

    own_layers = c_idx * group_layers + jnp.arange(group_layers, dtype=jnp.int32)
    t_own = temp0[:, T1 - PR:T1 + cell_rows + PR]
    lay_w = layer_ext[T0 - PR:T0 + cell_rows + PR]
    partial = jnp.sum(jnp.where(lay_w[None, :, :] == own_layers[:, None, None], t_own, 0.0), axis=0)
    partial = jnp.pad(partial, ((0, 0), (PC, PC)))
    windows = jnp.stack([partial[:, j * cell_cols:j * cell_cols + cell_cols + 2 * PC] for j in range(n_c)])
    windows = lax.all_to_all(windows, "col", split_axis=0, concat_axis=0, tiled=True)
    cell_temp = jnp.sum(windows, axis=0)

    denom_c = 1.0 + COND_SLOPE * cell_temp
    grow_c = jnp.exp(LEAK_SLOPE * cell_temp)
    rows1 = tile_rows + 2 * R1
    fo = PR * COARSE - R1
    denom_f = fine_of(denom_c, cols_w)[fo:fo + rows1]
    grow_f = fine_of(grow_c, cols_w)[fo:fo + rows1]
    rs1 = slice(R0 - R1, R0 - R1 + rows1)
    cond1 = p0[0][rs1] / denom_f
    load1 = p1[0] + p1[1] * grow_f
    row_ok1 = inside_of(r_idx * tile_rows - R1, rows1, total_rows).astype(jnp.float32)[:, None]
    drop1 = run_power(drop0, (cond1, load1, p0), row_ok1, col_ok, offset=(R0 - R1) // 8)
    hr1 = H1 * COARSE
    rh = slice(R1 - hr1, R1 + tile_rows + hr1)
    d_h1 = drop1[rh, cs]
    heat1 = coarse_of(load1[rh, cs] * (1.0 - d_h1) + cond1[rh, cs] * d_h1 * d_h1)
    temp1 = thermal(extended(temp0, (("col", 0, T1),)), gather_heat(heat1), T1)
    temp_out = temp1[T1:T1 + group_layers, T1:T1 + cell_rows]
    drop_out = drop1[R1:R1 + tile_rows, cs]
    return (drop_out, temp_out)


def solution(mesh):
    in_specs = (
        P("row", "col"),
        P("row", "col"),
        P("row", "col"),
        P("row", "col"),
        P("row", None),
        P("col", "row", None),
        P("col", "row", None),
    )
    out_specs = (P("row", "col"), P("col", "row", None))
    return jax.shard_map(body, mesh=mesh, in_specs=in_specs, out_specs=out_specs, check_vma=False)
```

```python
import functools
import os

import jax
import jax.numpy as jnp
from jax import lax
from jax.experimental import pallas as pl
from jax.experimental.pallas import tpu as pltpu
from jax.sharding import PartitionSpec as P

INTERPRET = os.environ.get("SOL_INTERPRET") == "1"
UNROLL = 8

COARSE = 8
SWEEPS = 4
HEAT_SWEEPS = 4
OUTER = 2


COND_SLOPE = 0.5
LEAK_SLOPE = 0.7
VIA_CONDUCT = 4.0

HALO = 4


def extended(block, sides):
    for axis, dim, width in sides:
        count = lax.axis_size(axis)
        forward = [(i, i + 1) for i in range(count - 1)]
        backward = [(target, source) for source, target in forward]
        low = lax.ppermute(
            lax.slice_in_dim(block, block.shape[dim] - width, None, axis=dim), axis, forward
        )
        high = lax.ppermute(lax.slice_in_dim(block, 0, width, axis=dim), axis, backward)
        block = jnp.concatenate([low, block, high], axis=dim)
    return block


def spread_cols(coarse, fine_cols):
    n = coarse.shape[1]
    ids = jnp.arange(fine_cols, dtype=jnp.int32) // COARSE
    onehot = (jnp.arange(n, dtype=jnp.int32)[:, None] == ids[None, :]).astype(jnp.float32)
    return jnp.dot(coarse, onehot, precision=lax.Precision.HIGHEST)


def fine_of(coarse, fine_cols):
    wide = spread_cols(coarse, fine_cols)
    rows = wide.shape[0]
    return jnp.broadcast_to(wide[:, None, :], (rows, COARSE, fine_cols)).reshape(rows * COARSE, fine_cols)


def coarse_of(fine):
    rows, cols = fine.shape
    summed_rows = jnp.sum(fine.reshape(rows // COARSE, COARSE, cols), axis=1)
    n = cols // COARSE
    ids = jnp.arange(cols, dtype=jnp.int32) // COARSE
    onehot = (ids[:, None] == jnp.arange(n, dtype=jnp.int32)[None, :]).astype(jnp.float32)
    return jnp.dot(summed_rows, onehot, precision=lax.Precision.HIGHEST) * (1.0 / (COARSE * COARSE))


def row_above(x, above):
    sub = lax.broadcasted_iota(jnp.int32, x.shape, 0)
    edge = jnp.broadcast_to(above[x.shape[0] - 1:, :], x.shape)
    return jnp.where(sub == 0, edge, pltpu.roll(x, 1, 0))


def row_below(x, below):
    n = x.shape[0]
    sub = lax.broadcasted_iota(jnp.int32, x.shape, 0)
    edge = jnp.broadcast_to(below[:1, :], x.shape)
    return jnp.where(sub == n - 1, edge, pltpu.roll(x, n - 1, 0))


def rows_of(k):
    return pl.ds(pl.multiple_of(k * 8, 8), 8)


def chunk(ref, k, count):
    return ref[rows_of(jnp.clip(k, 0, count - 1)), :]


def power_kernel(*refs, zero_start, stacked, offset):
    refs = list(refs)
    d_ref = None if zero_start else refs.pop(0)
    if stacked:
        p_ref = refs.pop(0)
        c_ref, l_ref, v_ref = p_ref.at[0], p_ref.at[1], p_ref.at[2]
    else:
        c_ref, l_ref, v_ref = refs.pop(0), refs.pop(0), refs.pop(0)
        v_ref = v_ref.at[2]
    rok_ref, cok_ref, o_ref, wn_ref, ws_ref, ww_ref, we_ref, inv_ref, buf_ref = refs
    n, w = o_ref.shape
    count = n // 8

    def weights(k, carry):
        sl = rows_of(k)
        x = c_ref[sl, :]
        a = (x + row_above(x, chunk(c_ref, k - 1, count))) * 0.5
        b = (x + row_below(x, chunk(c_ref, k + 1, count))) * 0.5
        e = (x + pltpu.roll(x, 1, 1)) * 0.5
        f = (x + pltpu.roll(x, w - 1, 1)) * 0.5
        wn_ref[sl, :] = a
        ws_ref[sl, :] = b
        ww_ref[sl, :] = e
        we_ref[sl, :] = f
        ok = (rok_ref[sl, :] > 0.5) & (cok_ref[...] > 0.5)
        inv = jnp.where(ok, 1.0 / (a + b + e + f + v_ref[rows_of(k + offset), :]), 0.0)
        inv_ref[sl, :] = inv
        if zero_start:
            buf_ref[sl, :] = jnp.where(inv != 0.0, l_ref[sl, :] * inv, 0.0)
        return carry

    lax.fori_loop(0, count, weights, 0, unroll=UNROLL)

    def sweep(src, dst):
        def body(k, carry):
            sl = rows_of(k)
            x = src[sl, :]
            summed = (
                l_ref[sl, :]
                + wn_ref[sl, :] * row_above(x, chunk(src, k - 1, count))
                + ws_ref[sl, :] * row_below(x, chunk(src, k + 1, count))
                + ww_ref[sl, :] * pltpu.roll(x, 1, 1)
                + we_ref[sl, :] * pltpu.roll(x, w - 1, 1)
            )
            inv = inv_ref[sl, :]
            dst[sl, :] = jnp.where(inv != 0.0, summed * inv, 0.0)
            return carry

        lax.fori_loop(0, count, body, 0, unroll=UNROLL)

    def first_sweep(k, carry):
        sl = rows_of(k)
        x = d_ref[rows_of(k + offset), :]
        summed = (
            l_ref[sl, :]
            + wn_ref[sl, :] * row_above(x, d_ref[rows_of(jnp.maximum(k - 1, 0) + offset), :])
            + ws_ref[sl, :] * row_below(x, d_ref[rows_of(jnp.minimum(k + 1, count - 1) + offset), :])
            + ww_ref[sl, :] * pltpu.roll(x, 1, 1)
            + we_ref[sl, :] * pltpu.roll(x, w - 1, 1)
        )
        inv = inv_ref[sl, :]
        buf_ref[sl, :] = jnp.where(inv != 0.0, summed * inv, 0.0)
        return carry

    if not zero_start:
        lax.fori_loop(0, count, first_sweep, 0, unroll=UNROLL)
    sweep(buf_ref, o_ref)
    sweep(o_ref, buf_ref)
    sweep(buf_ref, o_ref)


def run_power(drop, parts, row_ok, col_ok, offset=0):
    stacked = not isinstance(parts, (tuple, list))
    n, w = parts.shape[1:] if stacked else parts[0].shape
    operands = ([] if drop is None else [drop]) + ([parts] if stacked else list(parts)) + [row_ok, col_ok]
    kernel = functools.partial(power_kernel, zero_start=drop is None, stacked=stacked, offset=offset)
    return pl.pallas_call(
        kernel,
        out_shape=jax.ShapeDtypeStruct((n, w), jnp.float32),
        scratch_shapes=[pltpu.VMEM((n, w), jnp.float32) for _ in range(6)],
        compiler_params=pltpu.CompilerParams(vmem_limit_bytes=60 * 1024 * 1024),
        interpret=INTERPRET,
    )(*operands)


def thermal_kernel(*refs, stride, stored, zero_start):
    refs = list(refs)
    t_ref = None if zero_start else refs.pop(0)
    s_ref, lk_ref, vk_ref, rok_ref, o_ref = refs[:5]
    scratch = refs[5:]
    n, w = lk_ref.shape
    count = n // 8
    lane = lax.broadcasted_iota(jnp.int32, (8, w), 1)
    first = lane == 0
    last = lane == w - 1
    if stored:
        wn_ref, ws_ref, ww_ref, we_ref, wb_ref, wa_ref, inv_ref, buf_ref = scratch
    else:
        wb_ref, wa_ref, inv_ref, buf_ref = scratch

    def lateral(x, k, ref):
        up = row_above(x, chunk(ref, k - 1, count))
        dn = row_below(x, chunk(ref, k + 1, count))
        lf = jnp.where(first, 0.0, pltpu.roll(x, 1, 1))
        rt = jnp.where(last, 0.0, pltpu.roll(x, w - 1, 1))
        return up, dn, lf, rt

    def lateral_weights(k):
        sl = rows_of(k)
        x = lk_ref[sl, :]
        up, dn, lf, rt = lateral(x, k, lk_ref)
        return (x + up) * 0.5, (x + dn) * 0.5, (x + lf) * 0.5, (x + rt) * 0.5

    def weights(k, carry):
        sl = rows_of(k)
        a, b, e, f = lateral_weights(k)
        if stored:
            wn_ref[sl, :] = a
            ws_ref[sl, :] = b
            ww_ref[sl, :] = e
            we_ref[sl, :] = f
        v = vk_ref[sl, :]
        lo = (v + chunk(vk_ref, k - stride, count)) * 0.5
        hi = (v + chunk(vk_ref, k + stride, count)) * 0.5
        wb_ref[sl, :] = lo
        wa_ref[sl, :] = hi
        inv = jnp.where(rok_ref[sl, :] > 0.5, 1.0 / (a + b + e + f + lo + hi), 0.0)
        inv_ref[sl, :] = inv
        if zero_start:
            buf_ref[sl, :] = jnp.where(inv != 0.0, s_ref[sl, :] * inv, 0.0)
        return carry

    lax.fori_loop(0, count, weights, 0, unroll=UNROLL)

    def sweep(src, dst):
        def body(k, carry):
            sl = rows_of(k)
            if stored:
                a, b, e, f = wn_ref[sl, :], ws_ref[sl, :], ww_ref[sl, :], we_ref[sl, :]
            else:
                a, b, e, f = lateral_weights(k)
            x = src[sl, :]
            up, dn, lf, rt = lateral(x, k, src)
            summed = (
                s_ref[sl, :]
                + a * up
                + b * dn
                + e * lf
                + f * rt
                + wb_ref[sl, :] * chunk(src, k - stride, count)
                + wa_ref[sl, :] * chunk(src, k + stride, count)
            )
            inv = inv_ref[sl, :]
            dst[sl, :] = jnp.where(inv != 0.0, summed * inv, 0.0)
            return carry

        lax.fori_loop(0, count, body, 0, unroll=UNROLL)

    if not zero_start:
        sweep(t_ref, buf_ref)
    sweep(buf_ref, o_ref)
    sweep(o_ref, buf_ref)
    sweep(buf_ref, o_ref)


def run_thermal(temp, source, lat, vert, row_ok, stride):
    n, w = lat.shape
    stored = 13 * n * w * 4 <= 40 * 1024 * 1024
    kernel = functools.partial(thermal_kernel, stride=stride, stored=stored, zero_start=temp is None)
    return pl.pallas_call(
        kernel,
        out_shape=jax.ShapeDtypeStruct((n, w), jnp.float32),
        scratch_shapes=[pltpu.VMEM((n, w), jnp.float32) for _ in range(8 if stored else 4)],
        compiler_params=pltpu.CompilerParams(vmem_limit_bytes=60 * 1024 * 1024),
        interpret=INTERPRET,
    )(*([] if temp is None else [temp]), source, lat, vert, row_ok)


def inside_of(start, count, total):
    idx = start + jnp.arange(count, dtype=jnp.int32)
    return (idx >= 0) & (idx < total)


def body(demand, leakage, conductance, vias, layer_of, lateral_k, vertical_k):
    tile_rows, tile_cols = demand.shape
    group_layers, cell_rows, therm_cols = lateral_k.shape
    cell_cols = tile_cols // COARSE
    n_r = lax.axis_size("row")
    n_c = lax.axis_size("col")
    r_idx = lax.axis_index("row")
    c_idx = lax.axis_index("col")
    all_layers = group_layers * n_c
    all_rows = cell_rows * n_r
    total_rows = tile_rows * n_r
    total_cols = tile_cols * n_c

    T0 = 2 * HEAT_SWEEPS
    T1 = HEAT_SWEEPS
    H0 = T0 - 1
    H1 = T1 - 1
    S = SWEEPS
    R1 = H1 * COARSE + SWEEPS
    R0 = max(H0 * COARSE, R1) + SWEEPS
    CW = 64
    PR = -(-R1 // COARSE)
    PC = CW // COARSE

    via_g = VIA_CONDUCT * vias.astype(jnp.float32)
    load0 = demand + leakage

    p0 = extended(jnp.stack([conductance, load0, via_g, demand, leakage]), (("row", 1, R0), ("col", 2, CW)))
    k_layers = extended(jnp.stack([lateral_k, vertical_k]), (("col", 1, T1),))

    cols_w = tile_cols + 2 * CW
    col_ok = inside_of(c_idx * tile_cols - CW, cols_w, total_cols).astype(jnp.float32)[None, :]

    rows0 = tile_rows + 2 * R0
    row_ok0 = inside_of(r_idx * tile_rows - R0, rows0, total_rows).astype(jnp.float32)[:, None]
    drop0 = run_power(None, p0, row_ok0, col_ok)
    k_layers, layer_in, drop0 = lax.optimization_barrier((k_layers, layer_of, drop0))
    k_ext = extended(k_layers, (("row", 2, T0),))
    layer_ext = extended(layer_in, (("row", 0, T0),))
    hr0 = H0 * COARSE
    rs = slice(R0 - hr0, R0 + tile_rows + hr0)
    cs = slice(CW, CW + tile_cols)
    d_h = drop0[rs, cs]
    heat0 = coarse_of(p0[1][rs, cs] * (1.0 - d_h) + p0[0][rs, cs] * d_h * d_h)

    def gather_heat(heat):
        copies = jnp.broadcast_to(heat[None], (n_c,) + heat.shape)
        gathered = lax.all_to_all(copies, "col", split_axis=0, concat_axis=0, tiled=True)
        gathered = gathered.transpose(1, 0, 2).reshape(heat.shape[0], n_c * cell_cols)
        return jnp.pad(gathered, ((1, 1), (0, 0)))

    def thermal(temp_ext, heat_ext, halo):
        layers = group_layers + 2 * T1
        rows = cell_rows + 2 * halo
        ks = k_ext[:, :, T0 - halo:T0 + cell_rows + halo]
        tlay = c_idx * group_layers - T1 + jnp.arange(layers, dtype=jnp.int32)
        inside = inside_of(c_idx * group_layers - T1, layers, all_layers)[:, None] & inside_of(r_idx * cell_rows - halo, rows, all_rows)[None, :]
        lay_in = layer_ext[T0 - halo:T0 + cell_rows + halo]
        picker = (lay_in[None, :, :] == tlay[:, None, None]) & inside[:, :, None]
        source = jnp.where(picker, heat_ext[None, :, :], 0.0)
        flat = (layers * rows, therm_cols)
        out = run_thermal(
            None if temp_ext is None else temp_ext.reshape(flat), source.reshape(flat), ks[0].reshape(flat), ks[1].reshape(flat),
            inside.astype(jnp.float32).reshape(layers * rows, 1), rows // 8,
        )
        return out.reshape(layers, rows, therm_cols)

    temp0 = thermal(None, gather_heat(heat0), T0)
    temp0 = temp0[T1:T1 + group_layers, T0 - T1:T0 + cell_rows + T1]

    own_layers = c_idx * group_layers + jnp.arange(group_layers, dtype=jnp.int32)
    t_own = temp0[:, T1 - PR:T1 + cell_rows + PR]
    lay_w = layer_ext[T0 - PR:T0 + cell_rows + PR]
    partial = jnp.sum(jnp.where(lay_w[None, :, :] == own_layers[:, None, None], t_own, 0.0), axis=0)
    partial = jnp.pad(partial, ((0, 0), (PC, PC)))
    windows = jnp.stack([partial[:, j * cell_cols:j * cell_cols + cell_cols + 2 * PC] for j in range(n_c)])
    windows = lax.all_to_all(windows, "col", split_axis=0, concat_axis=0, tiled=True)
    cell_temp = jnp.sum(windows, axis=0)

    denom_c = 1.0 + COND_SLOPE * cell_temp
    grow_c = jnp.exp(LEAK_SLOPE * cell_temp)
    rows1 = tile_rows + 2 * R1
    fo = PR * COARSE - R1
    denom_f = fine_of(denom_c, cols_w)[fo:fo + rows1]
    grow_f = fine_of(grow_c, cols_w)[fo:fo + rows1]
    rs1 = slice(R0 - R1, R0 - R1 + rows1)
    cond1 = p0[0][rs1] / denom_f
    load1 = p0[3][rs1] + p0[4][rs1] * grow_f
    row_ok1 = inside_of(r_idx * tile_rows - R1, rows1, total_rows).astype(jnp.float32)[:, None]
    drop1 = run_power(drop0, (cond1, load1, p0), row_ok1, col_ok, offset=(R0 - R1) // 8)
    hr1 = H1 * COARSE
    rh = slice(R1 - hr1, R1 + tile_rows + hr1)
    d_h1 = drop1[rh, cs]
    heat1 = coarse_of(load1[rh, cs] * (1.0 - d_h1) + cond1[rh, cs] * d_h1 * d_h1)
    temp1 = thermal(extended(temp0, (("col", 0, T1),)), gather_heat(heat1), T1)
    temp_out = temp1[T1:T1 + group_layers, T1:T1 + cell_rows]
    drop_out = drop1[R1:R1 + tile_rows, cs]
    return (drop_out, temp_out)


def solution(mesh):
    in_specs = (
        P("row", "col"),
        P("row", "col"),
        P("row", "col"),
        P("row", "col"),
        P("row", None),
        P("col", "row", None),
        P("col", "row", None),
    )
    out_specs = (P("row", "col"), P("col", "row", None))
    return jax.shard_map(body, mesh=mesh, in_specs=in_specs, out_specs=out_specs, check_vma=False)
```

```python
import functools
import os

import jax
import jax.numpy as jnp
from jax import lax
from jax.experimental import pallas as pl
from jax.experimental.pallas import tpu as pltpu
from jax.sharding import PartitionSpec as P

INTERPRET = os.environ.get("SOL_INTERPRET") == "1"
UNROLL = 8

COARSE = 8
SWEEPS = 4
HEAT_SWEEPS = 4
OUTER = 2


COND_SLOPE = 0.5
LEAK_SLOPE = 0.7
VIA_CONDUCT = 4.0

HALO = 4


def extended(block, sides):
    for axis, dim, width in sides:
        count = lax.axis_size(axis)
        forward = [(i, i + 1) for i in range(count - 1)]
        backward = [(target, source) for source, target in forward]
        low = lax.ppermute(
            lax.slice_in_dim(block, block.shape[dim] - width, None, axis=dim), axis, forward
        )
        high = lax.ppermute(lax.slice_in_dim(block, 0, width, axis=dim), axis, backward)
        block = jnp.concatenate([low, block, high], axis=dim)
    return block


def spread_cols(coarse, fine_cols):
    n = coarse.shape[1]
    ids = jnp.arange(fine_cols, dtype=jnp.int32) // COARSE
    onehot = (jnp.arange(n, dtype=jnp.int32)[:, None] == ids[None, :]).astype(jnp.float32)
    return jnp.dot(coarse, onehot, precision=lax.Precision.HIGHEST)


def fine_of(coarse, fine_cols):
    wide = spread_cols(coarse, fine_cols)
    rows = wide.shape[0]
    return jnp.broadcast_to(wide[:, None, :], (rows, COARSE, fine_cols)).reshape(rows * COARSE, fine_cols)


def coarse_of(fine):
    rows, cols = fine.shape
    summed_rows = jnp.sum(fine.reshape(rows // COARSE, COARSE, cols), axis=1)
    n = cols // COARSE
    ids = jnp.arange(cols, dtype=jnp.int32) // COARSE
    onehot = (ids[:, None] == jnp.arange(n, dtype=jnp.int32)[None, :]).astype(jnp.float32)
    return jnp.dot(summed_rows, onehot, precision=lax.Precision.HIGHEST) * (1.0 / (COARSE * COARSE))


def row_above(x, above):
    sub = lax.broadcasted_iota(jnp.int32, x.shape, 0)
    edge = jnp.broadcast_to(above[x.shape[0] - 1:, :], x.shape)
    return jnp.where(sub == 0, edge, pltpu.roll(x, 1, 0))


def row_below(x, below):
    n = x.shape[0]
    sub = lax.broadcasted_iota(jnp.int32, x.shape, 0)
    edge = jnp.broadcast_to(below[:1, :], x.shape)
    return jnp.where(sub == n - 1, edge, pltpu.roll(x, n - 1, 0))


def rows_of(k):
    return pl.ds(pl.multiple_of(k * 8, 8), 8)


def chunk(ref, k, count):
    return ref[rows_of(jnp.clip(k, 0, count - 1)), :]


def power_kernel(*refs, zero_start, stacked, offset):
    refs = list(refs)
    d_ref = None if zero_start else refs.pop(0)
    if stacked:
        p_ref = refs.pop(0)
        c_ref, l_ref, v_ref = p_ref.at[0], p_ref.at[1], p_ref.at[2]
    else:
        c_ref, l_ref, v_ref = refs.pop(0), refs.pop(0), refs.pop(0)
        v_ref = v_ref.at[2]
    rok_ref, cok_ref, o_ref, wn_ref, ws_ref, ww_ref, we_ref, inv_ref, buf_ref = refs
    n, w = o_ref.shape
    count = n // 8

    def weights(k, carry):
        sl = rows_of(k)
        x = c_ref[sl, :]
        a = (x + row_above(x, chunk(c_ref, k - 1, count))) * 0.5
        b = (x + row_below(x, chunk(c_ref, k + 1, count))) * 0.5
        e = (x + pltpu.roll(x, 1, 1)) * 0.5
        f = (x + pltpu.roll(x, w - 1, 1)) * 0.5
        wn_ref[sl, :] = a
        ws_ref[sl, :] = b
        ww_ref[sl, :] = e
        we_ref[sl, :] = f
        ok = (rok_ref[sl, :] > 0.5) & (cok_ref[...] > 0.5)
        inv = jnp.where(ok, 1.0 / (a + b + e + f + v_ref[rows_of(k + offset), :]), 0.0)
        inv_ref[sl, :] = inv
        if zero_start:
            buf_ref[sl, :] = jnp.where(inv != 0.0, l_ref[sl, :] * inv, 0.0)
        return carry

    lax.fori_loop(0, count, weights, 0, unroll=UNROLL)

    def sweep(src, dst):
        def body(k, carry):
            sl = rows_of(k)
            x = src[sl, :]
            summed = (
                l_ref[sl, :]
                + wn_ref[sl, :] * row_above(x, chunk(src, k - 1, count))
                + ws_ref[sl, :] * row_below(x, chunk(src, k + 1, count))
                + ww_ref[sl, :] * pltpu.roll(x, 1, 1)
                + we_ref[sl, :] * pltpu.roll(x, w - 1, 1)
            )
            inv = inv_ref[sl, :]
            dst[sl, :] = jnp.where(inv != 0.0, summed * inv, 0.0)
            return carry

        lax.fori_loop(0, count, body, 0, unroll=UNROLL)

    def first_sweep(k, carry):
        sl = rows_of(k)
        x = d_ref[rows_of(k + offset), :]
        summed = (
            l_ref[sl, :]
            + wn_ref[sl, :] * row_above(x, d_ref[rows_of(jnp.maximum(k - 1, 0) + offset), :])
            + ws_ref[sl, :] * row_below(x, d_ref[rows_of(jnp.minimum(k + 1, count - 1) + offset), :])
            + ww_ref[sl, :] * pltpu.roll(x, 1, 1)
            + we_ref[sl, :] * pltpu.roll(x, w - 1, 1)
        )
        inv = inv_ref[sl, :]
        buf_ref[sl, :] = jnp.where(inv != 0.0, summed * inv, 0.0)
        return carry

    if not zero_start:
        lax.fori_loop(0, count, first_sweep, 0, unroll=UNROLL)
    sweep(buf_ref, o_ref)
    sweep(o_ref, buf_ref)
    sweep(buf_ref, o_ref)


def run_power(drop, parts, row_ok, col_ok, offset=0):
    stacked = not isinstance(parts, (tuple, list))
    n, w = parts.shape[1:] if stacked else parts[0].shape
    operands = ([] if drop is None else [drop]) + ([parts] if stacked else list(parts)) + [row_ok, col_ok]
    kernel = functools.partial(power_kernel, zero_start=drop is None, stacked=stacked, offset=offset)
    return pl.pallas_call(
        kernel,
        out_shape=jax.ShapeDtypeStruct((n, w), jnp.float32),
        scratch_shapes=[pltpu.VMEM((n, w), jnp.float32) for _ in range(6)],
        compiler_params=pltpu.CompilerParams(vmem_limit_bytes=60 * 1024 * 1024),
        interpret=INTERPRET,
    )(*operands)


def thermal_kernel(*refs, stride, stored, zero_start):
    refs = list(refs)
    t_ref = None if zero_start else refs.pop(0)
    s_ref, lk_ref, vk_ref, rok_ref, o_ref = refs[:5]
    scratch = refs[5:]
    n, w = lk_ref.shape
    count = n // 8
    lane = lax.broadcasted_iota(jnp.int32, (8, w), 1)
    first = lane == 0
    last = lane == w - 1
    if stored:
        wn_ref, ws_ref, ww_ref, we_ref, wb_ref, wa_ref, inv_ref, buf_ref = scratch
    else:
        wb_ref, wa_ref, inv_ref, buf_ref = scratch

    def lateral(x, k, ref):
        up = row_above(x, chunk(ref, k - 1, count))
        dn = row_below(x, chunk(ref, k + 1, count))
        lf = jnp.where(first, 0.0, pltpu.roll(x, 1, 1))
        rt = jnp.where(last, 0.0, pltpu.roll(x, w - 1, 1))
        return up, dn, lf, rt

    def lateral_weights(k):
        sl = rows_of(k)
        x = lk_ref[sl, :]
        up, dn, lf, rt = lateral(x, k, lk_ref)
        return (x + up) * 0.5, (x + dn) * 0.5, (x + lf) * 0.5, (x + rt) * 0.5

    def weights(k, carry):
        sl = rows_of(k)
        a, b, e, f = lateral_weights(k)
        if stored:
            wn_ref[sl, :] = a
            ws_ref[sl, :] = b
            ww_ref[sl, :] = e
            we_ref[sl, :] = f
        v = vk_ref[sl, :]
        lo = (v + chunk(vk_ref, k - stride, count)) * 0.5
        hi = (v + chunk(vk_ref, k + stride, count)) * 0.5
        wb_ref[sl, :] = lo
        wa_ref[sl, :] = hi
        inv = jnp.where(rok_ref[sl, :] > 0.5, 1.0 / (a + b + e + f + lo + hi), 0.0)
        inv_ref[sl, :] = inv
        if zero_start:
            buf_ref[sl, :] = jnp.where(inv != 0.0, s_ref[sl, :] * inv, 0.0)
        return carry

    lax.fori_loop(0, count, weights, 0, unroll=UNROLL)

    def sweep(src, dst):
        def body(k, carry):
            sl = rows_of(k)
            if stored:
                a, b, e, f = wn_ref[sl, :], ws_ref[sl, :], ww_ref[sl, :], we_ref[sl, :]
            else:
                a, b, e, f = lateral_weights(k)
            x = src[sl, :]
            up, dn, lf, rt = lateral(x, k, src)
            summed = (
                s_ref[sl, :]
                + a * up
                + b * dn
                + e * lf
                + f * rt
                + wb_ref[sl, :] * chunk(src, k - stride, count)
                + wa_ref[sl, :] * chunk(src, k + stride, count)
            )
            inv = inv_ref[sl, :]
            dst[sl, :] = jnp.where(inv != 0.0, summed * inv, 0.0)
            return carry

        lax.fori_loop(0, count, body, 0, unroll=UNROLL)

    if not zero_start:
        sweep(t_ref, buf_ref)
    sweep(buf_ref, o_ref)
    sweep(o_ref, buf_ref)
    sweep(buf_ref, o_ref)


def run_thermal(temp, source, lat, vert, row_ok, stride):
    n, w = lat.shape
    stored = 13 * n * w * 4 <= 40 * 1024 * 1024
    kernel = functools.partial(thermal_kernel, stride=stride, stored=stored, zero_start=temp is None)
    return pl.pallas_call(
        kernel,
        out_shape=jax.ShapeDtypeStruct((n, w), jnp.float32),
        scratch_shapes=[pltpu.VMEM((n, w), jnp.float32) for _ in range(8 if stored else 4)],
        compiler_params=pltpu.CompilerParams(vmem_limit_bytes=60 * 1024 * 1024),
        interpret=INTERPRET,
    )(*([] if temp is None else [temp]), source, lat, vert, row_ok)


def inside_of(start, count, total):
    idx = start + jnp.arange(count, dtype=jnp.int32)
    return (idx >= 0) & (idx < total)


def body(demand, leakage, conductance, vias, layer_of, lateral_k, vertical_k):
    tile_rows, tile_cols = demand.shape
    group_layers, cell_rows, therm_cols = lateral_k.shape
    cell_cols = tile_cols // COARSE
    n_r = lax.axis_size("row")
    n_c = lax.axis_size("col")
    r_idx = lax.axis_index("row")
    c_idx = lax.axis_index("col")
    all_layers = group_layers * n_c
    all_rows = cell_rows * n_r
    total_rows = tile_rows * n_r
    total_cols = tile_cols * n_c

    T0 = 2 * HEAT_SWEEPS
    T1 = HEAT_SWEEPS
    H0 = T0 - 1
    H1 = T1 - 1
    S = SWEEPS
    R1 = -(-(H1 * COARSE + SWEEPS) // 8) * 8
    R0 = -(-(max(H0 * COARSE, R1) + SWEEPS) // 8) * 8
    CW = 64
    PR = -(-R1 // COARSE)
    PC = CW // COARSE

    via_g = VIA_CONDUCT * vias.astype(jnp.float32)
    load0 = demand + leakage

    p0 = extended(jnp.stack([conductance, load0, via_g]), (("row", 1, R0), ("col", 2, CW)))
    p1 = extended(jnp.stack([demand, leakage]), (("row", 1, R1), ("col", 2, CW)))
    k_ext = extended(jnp.stack([lateral_k, vertical_k]), (("col", 1, T1), ("row", 2, T0)))
    layer_ext = extended(layer_of, (("row", 0, T0),))

    cols_w = tile_cols + 2 * CW
    col_ok = inside_of(c_idx * tile_cols - CW, cols_w, total_cols).astype(jnp.float32)[None, :]

    rows0 = tile_rows + 2 * R0
    row_ok0 = inside_of(r_idx * tile_rows - R0, rows0, total_rows).astype(jnp.float32)[:, None]
    drop0 = run_power(None, p0, row_ok0, col_ok)
    hr0 = H0 * COARSE
    rs = slice(R0 - hr0, R0 + tile_rows + hr0)
    cs = slice(CW, CW + tile_cols)
    d_h = drop0[rs, cs]
    heat0 = coarse_of(p0[1][rs, cs] * (1.0 - d_h) + p0[0][rs, cs] * d_h * d_h)

    def gather_heat(heat):
        copies = jnp.broadcast_to(heat[None], (n_c,) + heat.shape)
        gathered = lax.all_to_all(copies, "col", split_axis=0, concat_axis=0, tiled=True)
        gathered = gathered.transpose(1, 0, 2).reshape(heat.shape[0], n_c * cell_cols)
        return jnp.pad(gathered, ((1, 1), (0, 0)))

    def thermal(temp_ext, heat_ext, halo):
        layers = group_layers + 2 * T1
        rows = cell_rows + 2 * halo
        ks = k_ext[:, :, T0 - halo:T0 + cell_rows + halo]
        tlay = c_idx * group_layers - T1 + jnp.arange(layers, dtype=jnp.int32)
        inside = inside_of(c_idx * group_layers - T1, layers, all_layers)[:, None] & inside_of(r_idx * cell_rows - halo, rows, all_rows)[None, :]
        lay_in = layer_ext[T0 - halo:T0 + cell_rows + halo]
        picker = (lay_in[None, :, :] == tlay[:, None, None]) & inside[:, :, None]
        source = jnp.where(picker, heat_ext[None, :, :], 0.0)
        flat = (layers * rows, therm_cols)
        out = run_thermal(
            None if temp_ext is None else temp_ext.reshape(flat), source.reshape(flat), ks[0].reshape(flat), ks[1].reshape(flat),
            inside.astype(jnp.float32).reshape(layers * rows, 1), rows // 8,
        )
        return out.reshape(layers, rows, therm_cols)

    temp0 = thermal(None, gather_heat(heat0), T0)
    temp0 = temp0[T1:T1 + group_layers, T0 - T1:T0 + cell_rows + T1]

    own_layers = c_idx * group_layers + jnp.arange(group_layers, dtype=jnp.int32)
    t_own = temp0[:, T1 - PR:T1 + cell_rows + PR]
    lay_w = layer_ext[T0 - PR:T0 + cell_rows + PR]
    partial = jnp.sum(jnp.where(lay_w[None, :, :] == own_layers[:, None, None], t_own, 0.0), axis=0)
    partial = jnp.pad(partial, ((0, 0), (PC, PC)))
    windows = jnp.stack([partial[:, j * cell_cols:j * cell_cols + cell_cols + 2 * PC] for j in range(n_c)])
    windows = lax.all_to_all(windows, "col", split_axis=0, concat_axis=0, tiled=True)
    cell_temp = jnp.sum(windows, axis=0)

    denom_c = 1.0 + COND_SLOPE * cell_temp
    grow_c = jnp.exp(LEAK_SLOPE * cell_temp)
    rows1 = tile_rows + 2 * R1
    fo = PR * COARSE - R1
    denom_f = fine_of(denom_c, cols_w)[fo:fo + rows1]
    grow_f = fine_of(grow_c, cols_w)[fo:fo + rows1]
    rs1 = slice(R0 - R1, R0 - R1 + rows1)
    cond1 = p0[0][rs1] / denom_f
    load1 = p1[0] + p1[1] * grow_f
    row_ok1 = inside_of(r_idx * tile_rows - R1, rows1, total_rows).astype(jnp.float32)[:, None]
    drop1 = run_power(drop0, (cond1, load1, p0), row_ok1, col_ok, offset=(R0 - R1) // 8)
    hr1 = H1 * COARSE
    rh = slice(R1 - hr1, R1 + tile_rows + hr1)
    d_h1 = drop1[rh, cs]
    heat1 = coarse_of(load1[rh, cs] * (1.0 - d_h1) + cond1[rh, cs] * d_h1 * d_h1)
    temp1 = thermal(extended(temp0, (("col", 0, T1),)), gather_heat(heat1), T1)
    temp_out = temp1[T1:T1 + group_layers, T1:T1 + cell_rows]
    drop_out = drop1[R1:R1 + tile_rows, cs]
    return (drop_out, temp_out)


def solution(mesh):
    in_specs = (
        P("row", "col"),
        P("row", "col"),
        P("row", "col"),
        P("row", "col"),
        P("row", None),
        P("col", "row", None),
        P("col", "row", None),
    )
    out_specs = (P("row", "col"), P("col", "row", None))
    return jax.shard_map(body, mesh=mesh, in_specs=in_specs, out_specs=out_specs, check_vma=False)
```

```python
import functools
import os

import jax
import jax.numpy as jnp
from jax import lax
from jax.experimental import pallas as pl
from jax.experimental.pallas import tpu as pltpu
from jax.sharding import PartitionSpec as P

INTERPRET = os.environ.get("SOL_INTERPRET") == "1"
POWER_UNROLL = 4
THERMAL_UNROLL = 16

COARSE = 8
SWEEPS = 4
HEAT_SWEEPS = 4
OUTER = 2


COND_SLOPE = 0.5
LEAK_SLOPE = 0.7
VIA_CONDUCT = 4.0

HALO = 4


def extended(block, sides):
    for axis, dim, width in sides:
        count = lax.axis_size(axis)
        forward = [(i, i + 1) for i in range(count - 1)]
        backward = [(target, source) for source, target in forward]
        low = lax.ppermute(
            lax.slice_in_dim(block, block.shape[dim] - width, None, axis=dim), axis, forward
        )
        high = lax.ppermute(lax.slice_in_dim(block, 0, width, axis=dim), axis, backward)
        block = jnp.concatenate([low, block, high], axis=dim)
    return block


def spread_cols(coarse, fine_cols):
    n = coarse.shape[1]
    ids = jnp.arange(fine_cols, dtype=jnp.int32) // COARSE
    onehot = (jnp.arange(n, dtype=jnp.int32)[:, None] == ids[None, :]).astype(jnp.float32)
    return jnp.dot(coarse, onehot, precision=lax.Precision.HIGHEST)


def fine_of(coarse, fine_cols):
    wide = spread_cols(coarse, fine_cols)
    rows = wide.shape[0]
    return jnp.broadcast_to(wide[:, None, :], (rows, COARSE, fine_cols)).reshape(rows * COARSE, fine_cols)


def coarse_of(fine):
    rows, cols = fine.shape
    summed_rows = jnp.sum(fine.reshape(rows // COARSE, COARSE, cols), axis=1)
    n = cols // COARSE
    ids = jnp.arange(cols, dtype=jnp.int32) // COARSE
    onehot = (ids[:, None] == jnp.arange(n, dtype=jnp.int32)[None, :]).astype(jnp.float32)
    return jnp.dot(summed_rows, onehot, precision=lax.Precision.HIGHEST) * (1.0 / (COARSE * COARSE))


def row_above(x, above):
    sub = lax.broadcasted_iota(jnp.int32, x.shape, 0)
    edge = jnp.broadcast_to(above[x.shape[0] - 1:, :], x.shape)
    return jnp.where(sub == 0, edge, pltpu.roll(x, 1, 0))


def row_below(x, below):
    n = x.shape[0]
    sub = lax.broadcasted_iota(jnp.int32, x.shape, 0)
    edge = jnp.broadcast_to(below[:1, :], x.shape)
    return jnp.where(sub == n - 1, edge, pltpu.roll(x, n - 1, 0))


def rows_of(k):
    return pl.ds(pl.multiple_of(k * 8, 8), 8)


def chunk(ref, k, count):
    return ref[rows_of(jnp.clip(k, 0, count - 1)), :]


def power_kernel(*refs, zero_start, stacked, offset):
    refs = list(refs)
    d_ref = None if zero_start else refs.pop(0)
    if stacked:
        p_ref = refs.pop(0)
        c_ref, l_ref, v_ref = p_ref.at[0], p_ref.at[1], p_ref.at[2]
    else:
        c_ref, l_ref, v_ref = refs.pop(0), refs.pop(0), refs.pop(0)
        v_ref = v_ref.at[2]
    rok_ref, cok_ref, o_ref, wn_ref, ws_ref, ww_ref, we_ref, inv_ref, buf_ref = refs
    n, w = o_ref.shape
    count = n // 8

    def weights(k, carry):
        sl = rows_of(k)
        x = c_ref[sl, :]
        a = (x + row_above(x, chunk(c_ref, k - 1, count))) * 0.5
        b = (x + row_below(x, chunk(c_ref, k + 1, count))) * 0.5
        e = (x + pltpu.roll(x, 1, 1)) * 0.5
        f = (x + pltpu.roll(x, w - 1, 1)) * 0.5
        wn_ref[sl, :] = a
        ws_ref[sl, :] = b
        ww_ref[sl, :] = e
        we_ref[sl, :] = f
        ok = (rok_ref[sl, :] > 0.5) & (cok_ref[...] > 0.5)
        inv = jnp.where(ok, 1.0 / (a + b + e + f + v_ref[rows_of(k + offset), :]), 0.0)
        inv_ref[sl, :] = inv
        if zero_start:
            buf_ref[sl, :] = jnp.where(inv != 0.0, l_ref[sl, :] * inv, 0.0)
        return carry

    lax.fori_loop(0, count, weights, 0, unroll=POWER_UNROLL)

    def sweep(src, dst):
        def body(k, carry):
            sl = rows_of(k)
            x = src[sl, :]
            summed = (
                l_ref[sl, :]
                + wn_ref[sl, :] * row_above(x, chunk(src, k - 1, count))
                + ws_ref[sl, :] * row_below(x, chunk(src, k + 1, count))
                + ww_ref[sl, :] * pltpu.roll(x, 1, 1)
                + we_ref[sl, :] * pltpu.roll(x, w - 1, 1)
            )
            inv = inv_ref[sl, :]
            dst[sl, :] = jnp.where(inv != 0.0, summed * inv, 0.0)
            return carry

        lax.fori_loop(0, count, body, 0, unroll=POWER_UNROLL)

    def first_sweep(k, carry):
        sl = rows_of(k)
        x = d_ref[rows_of(k + offset), :]
        summed = (
            l_ref[sl, :]
            + wn_ref[sl, :] * row_above(x, d_ref[rows_of(jnp.maximum(k - 1, 0) + offset), :])
            + ws_ref[sl, :] * row_below(x, d_ref[rows_of(jnp.minimum(k + 1, count - 1) + offset), :])
            + ww_ref[sl, :] * pltpu.roll(x, 1, 1)
            + we_ref[sl, :] * pltpu.roll(x, w - 1, 1)
        )
        inv = inv_ref[sl, :]
        buf_ref[sl, :] = jnp.where(inv != 0.0, summed * inv, 0.0)
        return carry

    if not zero_start:
        lax.fori_loop(0, count, first_sweep, 0, unroll=POWER_UNROLL)
    sweep(buf_ref, o_ref)
    sweep(o_ref, buf_ref)
    sweep(buf_ref, o_ref)


def run_power(drop, parts, row_ok, col_ok, offset=0):
    stacked = not isinstance(parts, (tuple, list))
    n, w = parts.shape[1:] if stacked else parts[0].shape
    operands = ([] if drop is None else [drop]) + ([parts] if stacked else list(parts)) + [row_ok, col_ok]
    kernel = functools.partial(power_kernel, zero_start=drop is None, stacked=stacked, offset=offset)
    return pl.pallas_call(
        kernel,
        out_shape=jax.ShapeDtypeStruct((n, w), jnp.float32),
        scratch_shapes=[pltpu.VMEM((n, w), jnp.float32) for _ in range(6)],
        compiler_params=pltpu.CompilerParams(vmem_limit_bytes=60 * 1024 * 1024),
        interpret=INTERPRET,
    )(*operands)


def thermal_kernel(*refs, stride, stored, zero_start):
    refs = list(refs)
    t_ref = None if zero_start else refs.pop(0)
    s_ref, lk_ref, vk_ref, rok_ref, o_ref = refs[:5]
    scratch = refs[5:]
    n, w = lk_ref.shape
    count = n // 8
    lane = lax.broadcasted_iota(jnp.int32, (8, w), 1)
    first = lane == 0
    last = lane == w - 1
    if stored:
        wn_ref, ws_ref, ww_ref, we_ref, wb_ref, wa_ref, inv_ref, buf_ref = scratch
    else:
        wb_ref, wa_ref, inv_ref, buf_ref = scratch

    def lateral(x, k, ref):
        up = row_above(x, chunk(ref, k - 1, count))
        dn = row_below(x, chunk(ref, k + 1, count))
        lf = jnp.where(first, 0.0, pltpu.roll(x, 1, 1))
        rt = jnp.where(last, 0.0, pltpu.roll(x, w - 1, 1))
        return up, dn, lf, rt

    def lateral_weights(k):
        sl = rows_of(k)
        x = lk_ref[sl, :]
        up, dn, lf, rt = lateral(x, k, lk_ref)
        return (x + up) * 0.5, (x + dn) * 0.5, (x + lf) * 0.5, (x + rt) * 0.5

    def weights(k, carry):
        sl = rows_of(k)
        a, b, e, f = lateral_weights(k)
        if stored:
            wn_ref[sl, :] = a
            ws_ref[sl, :] = b
            ww_ref[sl, :] = e
            we_ref[sl, :] = f
        v = vk_ref[sl, :]
        lo = (v + chunk(vk_ref, k - stride, count)) * 0.5
        hi = (v + chunk(vk_ref, k + stride, count)) * 0.5
        wb_ref[sl, :] = lo
        wa_ref[sl, :] = hi
        inv = jnp.where(rok_ref[sl, :] > 0.5, 1.0 / (a + b + e + f + lo + hi), 0.0)
        inv_ref[sl, :] = inv
        if zero_start:
            buf_ref[sl, :] = jnp.where(inv != 0.0, s_ref[sl, :] * inv, 0.0)
        return carry

    lax.fori_loop(0, count, weights, 0, unroll=THERMAL_UNROLL)

    def sweep(src, dst):
        def body(k, carry):
            sl = rows_of(k)
            if stored:
                a, b, e, f = wn_ref[sl, :], ws_ref[sl, :], ww_ref[sl, :], we_ref[sl, :]
            else:
                a, b, e, f = lateral_weights(k)
            x = src[sl, :]
            up, dn, lf, rt = lateral(x, k, src)
            summed = (
                s_ref[sl, :]
                + a * up
                + b * dn
                + e * lf
                + f * rt
                + wb_ref[sl, :] * chunk(src, k - stride, count)
                + wa_ref[sl, :] * chunk(src, k + stride, count)
            )
            inv = inv_ref[sl, :]
            dst[sl, :] = jnp.where(inv != 0.0, summed * inv, 0.0)
            return carry

        lax.fori_loop(0, count, body, 0, unroll=THERMAL_UNROLL)

    if not zero_start:
        sweep(t_ref, buf_ref)
    sweep(buf_ref, o_ref)
    sweep(o_ref, buf_ref)
    sweep(buf_ref, o_ref)


def run_thermal(temp, source, lat, vert, row_ok, stride):
    n, w = lat.shape
    stored = 13 * n * w * 4 <= 40 * 1024 * 1024
    kernel = functools.partial(thermal_kernel, stride=stride, stored=stored, zero_start=temp is None)
    return pl.pallas_call(
        kernel,
        out_shape=jax.ShapeDtypeStruct((n, w), jnp.float32),
        scratch_shapes=[pltpu.VMEM((n, w), jnp.float32) for _ in range(8 if stored else 4)],
        compiler_params=pltpu.CompilerParams(vmem_limit_bytes=60 * 1024 * 1024),
        interpret=INTERPRET,
    )(*([] if temp is None else [temp]), source, lat, vert, row_ok)


def inside_of(start, count, total):
    idx = start + jnp.arange(count, dtype=jnp.int32)
    return (idx >= 0) & (idx < total)


def body(demand, leakage, conductance, vias, layer_of, lateral_k, vertical_k):
    tile_rows, tile_cols = demand.shape
    group_layers, cell_rows, therm_cols = lateral_k.shape
    cell_cols = tile_cols // COARSE
    n_r = lax.axis_size("row")
    n_c = lax.axis_size("col")
    r_idx = lax.axis_index("row")
    c_idx = lax.axis_index("col")
    all_layers = group_layers * n_c
    all_rows = cell_rows * n_r
    total_rows = tile_rows * n_r
    total_cols = tile_cols * n_c

    T0 = 2 * HEAT_SWEEPS
    T1 = HEAT_SWEEPS
    H0 = T0 - 1
    H1 = T1 - 1
    S = SWEEPS
    R1 = H1 * COARSE + SWEEPS
    R0 = max(H0 * COARSE, R1) + SWEEPS
    CW = 64
    PR = -(-R1 // COARSE)
    PC = CW // COARSE

    via_g = VIA_CONDUCT * vias.astype(jnp.float32)
    load0 = demand + leakage

    p0 = extended(jnp.stack([conductance, load0, via_g]), (("row", 1, R0), ("col", 2, CW)))
    p1 = extended(jnp.stack([demand, leakage]), (("row", 1, R1), ("col", 2, CW)))
    k_ext = extended(jnp.stack([lateral_k, vertical_k]), (("col", 1, T1), ("row", 2, T0)))
    layer_ext = extended(layer_of, (("row", 0, T0),))

    cols_w = tile_cols + 2 * CW
    col_ok = inside_of(c_idx * tile_cols - CW, cols_w, total_cols).astype(jnp.float32)[None, :]

    rows0 = tile_rows + 2 * R0
    row_ok0 = inside_of(r_idx * tile_rows - R0, rows0, total_rows).astype(jnp.float32)[:, None]
    drop0 = run_power(None, p0, row_ok0, col_ok)
    hr0 = H0 * COARSE
    rs = slice(R0 - hr0, R0 + tile_rows + hr0)
    cs = slice(CW, CW + tile_cols)
    d_h = drop0[rs, cs]
    heat0 = coarse_of(p0[1][rs, cs] * (1.0 - d_h) + p0[0][rs, cs] * d_h * d_h)

    def gather_heat(heat):
        copies = jnp.broadcast_to(heat[None], (n_c,) + heat.shape)
        gathered = lax.all_to_all(copies, "col", split_axis=0, concat_axis=0, tiled=True)
        gathered = gathered.transpose(1, 0, 2).reshape(heat.shape[0], n_c * cell_cols)
        return jnp.pad(gathered, ((1, 1), (0, 0)))

    def thermal(temp_ext, heat_ext, halo):
        layers = group_layers + 2 * T1
        rows = cell_rows + 2 * halo
        ks = k_ext[:, :, T0 - halo:T0 + cell_rows + halo]
        tlay = c_idx * group_layers - T1 + jnp.arange(layers, dtype=jnp.int32)
        inside = inside_of(c_idx * group_layers - T1, layers, all_layers)[:, None] & inside_of(r_idx * cell_rows - halo, rows, all_rows)[None, :]
        lay_in = layer_ext[T0 - halo:T0 + cell_rows + halo]
        picker = (lay_in[None, :, :] == tlay[:, None, None]) & inside[:, :, None]
        source = jnp.where(picker, heat_ext[None, :, :], 0.0)
        flat = (layers * rows, therm_cols)
        out = run_thermal(
            None if temp_ext is None else temp_ext.reshape(flat), source.reshape(flat), ks[0].reshape(flat), ks[1].reshape(flat),
            inside.astype(jnp.float32).reshape(layers * rows, 1), rows // 8,
        )
        return out.reshape(layers, rows, therm_cols)

    temp0 = thermal(None, gather_heat(heat0), T0)
    temp0 = temp0[T1:T1 + group_layers, T0 - T1:T0 + cell_rows + T1]

    own_layers = c_idx * group_layers + jnp.arange(group_layers, dtype=jnp.int32)
    t_own = temp0[:, T1 - PR:T1 + cell_rows + PR]
    lay_w = layer_ext[T0 - PR:T0 + cell_rows + PR]
    partial = jnp.sum(jnp.where(lay_w[None, :, :] == own_layers[:, None, None], t_own, 0.0), axis=0)
    partial = jnp.pad(partial, ((0, 0), (PC, PC)))
    windows = jnp.stack([partial[:, j * cell_cols:j * cell_cols + cell_cols + 2 * PC] for j in range(n_c)])
    windows = lax.all_to_all(windows, "col", split_axis=0, concat_axis=0, tiled=True)
    cell_temp = jnp.sum(windows, axis=0)

    denom_c = 1.0 + COND_SLOPE * cell_temp
    grow_c = jnp.exp(LEAK_SLOPE * cell_temp)
    rows1 = tile_rows + 2 * R1
    fo = PR * COARSE - R1
    denom_f = fine_of(denom_c, cols_w)[fo:fo + rows1]
    grow_f = fine_of(grow_c, cols_w)[fo:fo + rows1]
    rs1 = slice(R0 - R1, R0 - R1 + rows1)
    cond1 = p0[0][rs1] / denom_f
    load1 = p1[0] + p1[1] * grow_f
    row_ok1 = inside_of(r_idx * tile_rows - R1, rows1, total_rows).astype(jnp.float32)[:, None]
    drop1 = run_power(drop0, (cond1, load1, p0), row_ok1, col_ok, offset=(R0 - R1) // 8)
    hr1 = H1 * COARSE
    rh = slice(R1 - hr1, R1 + tile_rows + hr1)
    d_h1 = drop1[rh, cs]
    heat1 = coarse_of(load1[rh, cs] * (1.0 - d_h1) + cond1[rh, cs] * d_h1 * d_h1)
    temp1 = thermal(extended(temp0, (("col", 0, T1),)), gather_heat(heat1), T1)
    temp_out = temp1[T1:T1 + group_layers, T1:T1 + cell_rows]
    drop_out = drop1[R1:R1 + tile_rows, cs]
    return (drop_out, temp_out)


def solution(mesh):
    in_specs = (
        P("row", "col"),
        P("row", "col"),
        P("row", "col"),
        P("row", "col"),
        P("row", None),
        P("col", "row", None),
        P("col", "row", None),
    )
    out_specs = (P("row", "col"), P("col", "row", None))
    return jax.shard_map(body, mesh=mesh, in_specs=in_specs, out_specs=out_specs, check_vma=False)
```

```python
import functools
import os

import jax
import jax.numpy as jnp
from jax import lax
from jax.experimental import pallas as pl
from jax.experimental.pallas import tpu as pltpu
from jax.sharding import PartitionSpec as P

INTERPRET = os.environ.get("SOL_INTERPRET") == "1"
POWER_UNROLL = 4
THERMAL_UNROLL = 16

COARSE = 8
SWEEPS = 4
HEAT_SWEEPS = 4
OUTER = 2


COND_SLOPE = 0.5
LEAK_SLOPE = 0.7
VIA_CONDUCT = 4.0

HALO = 4


def extended(block, sides):
    for axis, dim, width in sides:
        count = lax.axis_size(axis)
        forward = [(i, i + 1) for i in range(count - 1)]
        backward = [(target, source) for source, target in forward]
        low = lax.ppermute(
            lax.slice_in_dim(block, block.shape[dim] - width, None, axis=dim), axis, forward
        )
        high = lax.ppermute(lax.slice_in_dim(block, 0, width, axis=dim), axis, backward)
        block = jnp.concatenate([low, block, high], axis=dim)
    return block


def spread_cols(coarse, fine_cols):
    n = coarse.shape[1]
    ids = jnp.arange(fine_cols, dtype=jnp.int32) // COARSE
    onehot = (jnp.arange(n, dtype=jnp.int32)[:, None] == ids[None, :]).astype(jnp.float32)
    return jnp.dot(coarse, onehot, precision=lax.Precision.HIGHEST)


def fine_of(coarse, fine_cols):
    wide = spread_cols(coarse, fine_cols)
    rows = wide.shape[0]
    return jnp.broadcast_to(wide[:, None, :], (rows, COARSE, fine_cols)).reshape(rows * COARSE, fine_cols)


def coarse_of(fine):
    rows, cols = fine.shape
    summed_rows = jnp.sum(fine.reshape(rows // COARSE, COARSE, cols), axis=1)
    n = cols // COARSE
    ids = jnp.arange(cols, dtype=jnp.int32) // COARSE
    onehot = (ids[:, None] == jnp.arange(n, dtype=jnp.int32)[None, :]).astype(jnp.float32)
    return jnp.dot(summed_rows, onehot, precision=lax.Precision.HIGHEST) * (1.0 / (COARSE * COARSE))


def row_above(x, above):
    sub = lax.broadcasted_iota(jnp.int32, x.shape, 0)
    edge = jnp.broadcast_to(above[x.shape[0] - 1:, :], x.shape)
    return jnp.where(sub == 0, edge, pltpu.roll(x, 1, 0))


def row_below(x, below):
    n = x.shape[0]
    sub = lax.broadcasted_iota(jnp.int32, x.shape, 0)
    edge = jnp.broadcast_to(below[:1, :], x.shape)
    return jnp.where(sub == n - 1, edge, pltpu.roll(x, n - 1, 0))


def rows_of(k):
    return pl.ds(pl.multiple_of(k * 8, 8), 8)


def chunk(ref, k, count):
    return ref[rows_of(jnp.clip(k, 0, count - 1)), :]


def power_kernel(*refs, zero_start, stacked, offset):
    refs = list(refs)
    d_ref = None if zero_start else refs.pop(0)
    if stacked:
        p_ref = refs.pop(0)
        c_ref, l_ref, v_ref = p_ref.at[0], p_ref.at[1], p_ref.at[2]
    else:
        c_ref, l_ref, v_ref = refs.pop(0), refs.pop(0), refs.pop(0)
        v_ref = v_ref.at[2]
    rok_ref, cok_ref, o_ref, wn_ref, ws_ref, ww_ref, we_ref, inv_ref, buf_ref = refs
    n, w = o_ref.shape
    count = n // 8

    def weights(k, carry):
        sl = rows_of(k)
        x = c_ref[sl, :]
        a = (x + row_above(x, chunk(c_ref, k - 1, count))) * 0.5
        b = (x + row_below(x, chunk(c_ref, k + 1, count))) * 0.5
        e = (x + pltpu.roll(x, 1, 1)) * 0.5
        f = (x + pltpu.roll(x, w - 1, 1)) * 0.5
        wn_ref[sl, :] = a
        ws_ref[sl, :] = b
        ww_ref[sl, :] = e
        we_ref[sl, :] = f
        ok = (rok_ref[sl, :] > 0.5) & (cok_ref[...] > 0.5)
        inv = jnp.where(ok, 1.0 / (a + b + e + f + v_ref[rows_of(k + offset), :]), 0.0)
        inv_ref[sl, :] = inv
        if zero_start:
            buf_ref[sl, :] = jnp.where(inv != 0.0, l_ref[sl, :] * inv, 0.0)
        return carry

    lax.fori_loop(0, count, weights, 0, unroll=POWER_UNROLL)

    def sweep(src, dst):
        def body(k, carry):
            sl = rows_of(k)
            x = src[sl, :]
            summed = (
                l_ref[sl, :]
                + wn_ref[sl, :] * row_above(x, chunk(src, k - 1, count))
                + ws_ref[sl, :] * row_below(x, chunk(src, k + 1, count))
                + ww_ref[sl, :] * pltpu.roll(x, 1, 1)
                + we_ref[sl, :] * pltpu.roll(x, w - 1, 1)
            )
            inv = inv_ref[sl, :]
            dst[sl, :] = jnp.where(inv != 0.0, summed * inv, 0.0)
            return carry

        lax.fori_loop(0, count, body, 0, unroll=POWER_UNROLL)

    def first_sweep(k, carry):
        sl = rows_of(k)
        x = d_ref[rows_of(k + offset), :]
        summed = (
            l_ref[sl, :]
            + wn_ref[sl, :] * row_above(x, d_ref[rows_of(jnp.maximum(k - 1, 0) + offset), :])
            + ws_ref[sl, :] * row_below(x, d_ref[rows_of(jnp.minimum(k + 1, count - 1) + offset), :])
            + ww_ref[sl, :] * pltpu.roll(x, 1, 1)
            + we_ref[sl, :] * pltpu.roll(x, w - 1, 1)
        )
        inv = inv_ref[sl, :]
        buf_ref[sl, :] = jnp.where(inv != 0.0, summed * inv, 0.0)
        return carry

    if not zero_start:
        lax.fori_loop(0, count, first_sweep, 0, unroll=POWER_UNROLL)
    sweep(buf_ref, o_ref)
    sweep(o_ref, buf_ref)
    sweep(buf_ref, o_ref)


def run_power(drop, parts, row_ok, col_ok, offset=0):
    stacked = not isinstance(parts, (tuple, list))
    n, w = parts.shape[1:] if stacked else parts[0].shape
    operands = ([] if drop is None else [drop]) + ([parts] if stacked else list(parts)) + [row_ok, col_ok]
    kernel = functools.partial(power_kernel, zero_start=drop is None, stacked=stacked, offset=offset)
    return pl.pallas_call(
        kernel,
        out_shape=jax.ShapeDtypeStruct((n, w), jnp.float32),
        scratch_shapes=[pltpu.VMEM((n, w), jnp.float32) for _ in range(6)],
        compiler_params=pltpu.CompilerParams(vmem_limit_bytes=60 * 1024 * 1024),
        interpret=INTERPRET,
    )(*operands)


def thermal_kernel(*refs, stride, stored, zero_start):
    refs = list(refs)
    t_ref = None if zero_start else refs.pop(0)
    s_ref, lk_ref, vk_ref, rok_ref, o_ref = refs[:5]
    scratch = refs[5:]
    n, w = lk_ref.shape
    count = n // 8
    lane = lax.broadcasted_iota(jnp.int32, (8, w), 1)
    first = lane == 0
    last = lane == w - 1
    if stored:
        wn_ref, ws_ref, ww_ref, we_ref, wb_ref, wa_ref, inv_ref, buf_ref = scratch
    else:
        wb_ref, wa_ref, inv_ref, buf_ref = scratch

    def lateral(x, k, ref):
        up = row_above(x, chunk(ref, k - 1, count))
        dn = row_below(x, chunk(ref, k + 1, count))
        lf = jnp.where(first, 0.0, pltpu.roll(x, 1, 1))
        rt = jnp.where(last, 0.0, pltpu.roll(x, w - 1, 1))
        return up, dn, lf, rt

    def lateral_weights(k):
        sl = rows_of(k)
        x = lk_ref[sl, :]
        up, dn, lf, rt = lateral(x, k, lk_ref)
        return (x + up) * 0.5, (x + dn) * 0.5, (x + lf) * 0.5, (x + rt) * 0.5

    def weights(k, carry):
        sl = rows_of(k)
        a, b, e, f = lateral_weights(k)
        if stored:
            wn_ref[sl, :] = a
            ws_ref[sl, :] = b
            ww_ref[sl, :] = e
            we_ref[sl, :] = f
        v = vk_ref[sl, :]
        lo = (v + chunk(vk_ref, k - stride, count)) * 0.5
        hi = (v + chunk(vk_ref, k + stride, count)) * 0.5
        wb_ref[sl, :] = lo
        wa_ref[sl, :] = hi
        inv = jnp.where(rok_ref[sl, :] > 0.5, 1.0 / (a + b + e + f + lo + hi), 0.0)
        inv_ref[sl, :] = inv
        if zero_start:
            buf_ref[sl, :] = jnp.where(inv != 0.0, s_ref[sl, :] * inv, 0.0)
        return carry

    lax.fori_loop(0, count, weights, 0, unroll=THERMAL_UNROLL)

    def sweep(src, dst):
        def body(k, carry):
            sl = rows_of(k)
            if stored:
                a, b, e, f = wn_ref[sl, :], ws_ref[sl, :], ww_ref[sl, :], we_ref[sl, :]
            else:
                a, b, e, f = lateral_weights(k)
            x = src[sl, :]
            up, dn, lf, rt = lateral(x, k, src)
            summed = (
                s_ref[sl, :]
                + a * up
                + b * dn
                + e * lf
                + f * rt
                + wb_ref[sl, :] * chunk(src, k - stride, count)
                + wa_ref[sl, :] * chunk(src, k + stride, count)
            )
            inv = inv_ref[sl, :]
            dst[sl, :] = jnp.where(inv != 0.0, summed * inv, 0.0)
            return carry

        lax.fori_loop(0, count, body, 0, unroll=THERMAL_UNROLL)

    if not zero_start:
        sweep(t_ref, buf_ref)
    sweep(buf_ref, o_ref)
    sweep(o_ref, buf_ref)
    sweep(buf_ref, o_ref)


def run_thermal(temp, source, lat, vert, row_ok, stride):
    n, w = lat.shape
    stored = 13 * n * w * 4 <= 40 * 1024 * 1024
    kernel = functools.partial(thermal_kernel, stride=stride, stored=stored, zero_start=temp is None)
    return pl.pallas_call(
        kernel,
        out_shape=jax.ShapeDtypeStruct((n, w), jnp.float32),
        scratch_shapes=[pltpu.VMEM((n, w), jnp.float32) for _ in range(8 if stored else 4)],
        compiler_params=pltpu.CompilerParams(vmem_limit_bytes=60 * 1024 * 1024),
        interpret=INTERPRET,
    )(*([] if temp is None else [temp]), source, lat, vert, row_ok)


def inside_of(start, count, total):
    idx = start + jnp.arange(count, dtype=jnp.int32)
    return (idx >= 0) & (idx < total)


def body(demand, leakage, conductance, vias, layer_of, lateral_k, vertical_k):
    tile_rows, tile_cols = demand.shape
    group_layers, cell_rows, therm_cols = lateral_k.shape
    cell_cols = tile_cols // COARSE
    n_r = lax.axis_size("row")
    n_c = lax.axis_size("col")
    r_idx = lax.axis_index("row")
    c_idx = lax.axis_index("col")
    all_layers = group_layers * n_c
    all_rows = cell_rows * n_r
    total_rows = tile_rows * n_r
    total_cols = tile_cols * n_c

    T0 = 2 * HEAT_SWEEPS
    T1 = HEAT_SWEEPS
    H0 = T0 - 1
    H1 = T1 - 1
    S = SWEEPS
    R1 = H1 * COARSE + SWEEPS
    R0 = max(H0 * COARSE, R1) + SWEEPS
    CW = 64
    PR = -(-R1 // COARSE)
    PC = CW // COARSE

    via_g = VIA_CONDUCT * vias.astype(jnp.float32)
    load0 = demand + leakage

    p0 = extended(jnp.stack([conductance, load0, via_g, leakage]), (("row", 1, R0), ("col", 2, CW)))
    k_ext = extended(jnp.stack([lateral_k, vertical_k]), (("col", 1, T1), ("row", 2, T0)))
    layer_ext = extended(layer_of, (("row", 0, T0),))

    cols_w = tile_cols + 2 * CW
    col_ok = inside_of(c_idx * tile_cols - CW, cols_w, total_cols).astype(jnp.float32)[None, :]

    rows0 = tile_rows + 2 * R0
    row_ok0 = inside_of(r_idx * tile_rows - R0, rows0, total_rows).astype(jnp.float32)[:, None]
    drop0 = run_power(None, p0, row_ok0, col_ok)
    hr0 = H0 * COARSE
    rs = slice(R0 - hr0, R0 + tile_rows + hr0)
    cs = slice(CW, CW + tile_cols)
    d_h = drop0[rs, cs]
    heat0 = coarse_of(p0[1][rs, cs] * (1.0 - d_h) + p0[0][rs, cs] * d_h * d_h)

    def gather_heat(heat):
        copies = jnp.broadcast_to(heat[None], (n_c,) + heat.shape)
        gathered = lax.all_to_all(copies, "col", split_axis=0, concat_axis=0, tiled=True)
        gathered = gathered.transpose(1, 0, 2).reshape(heat.shape[0], n_c * cell_cols)
        return jnp.pad(gathered, ((1, 1), (0, 0)))

    def thermal(temp_ext, heat_ext, halo):
        layers = group_layers + 2 * T1
        rows = cell_rows + 2 * halo
        ks = k_ext[:, :, T0 - halo:T0 + cell_rows + halo]
        tlay = c_idx * group_layers - T1 + jnp.arange(layers, dtype=jnp.int32)
        inside = inside_of(c_idx * group_layers - T1, layers, all_layers)[:, None] & inside_of(r_idx * cell_rows - halo, rows, all_rows)[None, :]
        lay_in = layer_ext[T0 - halo:T0 + cell_rows + halo]
        picker = (lay_in[None, :, :] == tlay[:, None, None]) & inside[:, :, None]
        source = jnp.where(picker, heat_ext[None, :, :], 0.0)
        flat = (layers * rows, therm_cols)
        out = run_thermal(
            None if temp_ext is None else temp_ext.reshape(flat), source.reshape(flat), ks[0].reshape(flat), ks[1].reshape(flat),
            inside.astype(jnp.float32).reshape(layers * rows, 1), rows // 8,
        )
        return out.reshape(layers, rows, therm_cols)

    temp0 = thermal(None, gather_heat(heat0), T0)
    temp0 = temp0[T1:T1 + group_layers, T0 - T1:T0 + cell_rows + T1]

    own_layers = c_idx * group_layers + jnp.arange(group_layers, dtype=jnp.int32)
    t_own = temp0[:, T1 - PR:T1 + cell_rows + PR]
    lay_w = layer_ext[T0 - PR:T0 + cell_rows + PR]
    partial = jnp.sum(jnp.where(lay_w[None, :, :] == own_layers[:, None, None], t_own, 0.0), axis=0)
    partial = jnp.pad(partial, ((0, 0), (PC, PC)))
    windows = jnp.stack([partial[:, j * cell_cols:j * cell_cols + cell_cols + 2 * PC] for j in range(n_c)])
    windows = lax.all_to_all(windows, "col", split_axis=0, concat_axis=0, tiled=True)
    cell_temp = jnp.sum(windows, axis=0)

    denom_c = 1.0 + COND_SLOPE * cell_temp
    grow_c = jnp.expm1(LEAK_SLOPE * cell_temp)
    rows1 = tile_rows + 2 * R1
    fo = PR * COARSE - R1
    denom_f = fine_of(denom_c, cols_w)[fo:fo + rows1]
    grow_f = fine_of(grow_c, cols_w)[fo:fo + rows1]
    rs1 = slice(R0 - R1, R0 - R1 + rows1)
    cond1 = p0[0][rs1] / denom_f
    load1 = p0[1][rs1] + p0[3][rs1] * grow_f
    row_ok1 = inside_of(r_idx * tile_rows - R1, rows1, total_rows).astype(jnp.float32)[:, None]
    drop1 = run_power(drop0, (cond1, load1, p0), row_ok1, col_ok, offset=(R0 - R1) // 8)
    hr1 = H1 * COARSE
    rh = slice(R1 - hr1, R1 + tile_rows + hr1)
    d_h1 = drop1[rh, cs]
    heat1 = coarse_of(load1[rh, cs] * (1.0 - d_h1) + cond1[rh, cs] * d_h1 * d_h1)
    temp1 = thermal(extended(temp0, (("col", 0, T1),)), gather_heat(heat1), T1)
    temp_out = temp1[T1:T1 + group_layers, T1:T1 + cell_rows]
    drop_out = drop1[R1:R1 + tile_rows, cs]
    return (drop_out, temp_out)


def solution(mesh):
    in_specs = (
        P("row", "col"),
        P("row", "col"),
        P("row", "col"),
        P("row", "col"),
        P("row", None),
        P("col", "row", None),
        P("col", "row", None),
    )
    out_specs = (P("row", "col"), P("col", "row", None))
    return jax.shard_map(body, mesh=mesh, in_specs=in_specs, out_specs=out_specs, check_vma=False)
```

```python
import functools
import os

import jax
import jax.numpy as jnp
from jax import lax
from jax.experimental import pallas as pl
from jax.experimental.pallas import tpu as pltpu
from jax.sharding import PartitionSpec as P

INTERPRET = os.environ.get("SOL_INTERPRET") == "1"
POWER_UNROLL = 4
THERMAL_UNROLL = 16

COARSE = 8
SWEEPS = 4
HEAT_SWEEPS = 4
OUTER = 2


COND_SLOPE = 0.5
LEAK_SLOPE = 0.7
VIA_CONDUCT = 4.0

HALO = 4


def extended(block, sides):
    for axis, dim, width in sides:
        count = lax.axis_size(axis)
        forward = [(i, i + 1) for i in range(count - 1)]
        backward = [(target, source) for source, target in forward]
        low = lax.ppermute(
            lax.slice_in_dim(block, block.shape[dim] - width, None, axis=dim), axis, forward
        )
        high = lax.ppermute(lax.slice_in_dim(block, 0, width, axis=dim), axis, backward)
        block = jnp.concatenate([low, block, high], axis=dim)
    return block


def spread_cols(coarse, fine_cols):
    n = coarse.shape[1]
    ids = jnp.arange(fine_cols, dtype=jnp.int32) // COARSE
    onehot = (jnp.arange(n, dtype=jnp.int32)[:, None] == ids[None, :]).astype(jnp.float32)
    return jnp.dot(coarse, onehot, precision=lax.Precision.HIGHEST)


def fine_of(coarse, fine_cols):
    wide = spread_cols(coarse, fine_cols)
    rows = wide.shape[0]
    return jnp.broadcast_to(wide[:, None, :], (rows, COARSE, fine_cols)).reshape(rows * COARSE, fine_cols)


def coarse_of(fine):
    rows, cols = fine.shape
    summed_rows = jnp.sum(fine.reshape(rows // COARSE, COARSE, cols), axis=1)
    n = cols // COARSE
    ids = jnp.arange(cols, dtype=jnp.int32) // COARSE
    onehot = (ids[:, None] == jnp.arange(n, dtype=jnp.int32)[None, :]).astype(jnp.float32)
    return jnp.dot(summed_rows, onehot, precision=lax.Precision.HIGHEST) * (1.0 / (COARSE * COARSE))


def row_above(x, above):
    sub = lax.broadcasted_iota(jnp.int32, x.shape, 0)
    edge = jnp.broadcast_to(above[x.shape[0] - 1:, :], x.shape)
    return jnp.where(sub == 0, edge, pltpu.roll(x, 1, 0))


def row_below(x, below):
    n = x.shape[0]
    sub = lax.broadcasted_iota(jnp.int32, x.shape, 0)
    edge = jnp.broadcast_to(below[:1, :], x.shape)
    return jnp.where(sub == n - 1, edge, pltpu.roll(x, n - 1, 0))


def rows_of(k):
    return pl.ds(pl.multiple_of(k * 8, 8), 8)


def chunk(ref, k, count):
    return ref[rows_of(jnp.clip(k, 0, count - 1)), :]


def power_kernel(*refs, zero_start, stacked, offset):
    refs = list(refs)
    d_ref = None if zero_start else refs.pop(0)
    if stacked:
        p_ref = refs.pop(0)
        c_ref, l_ref, v_ref = p_ref.at[0], p_ref.at[1], p_ref.at[2]
    else:
        c_ref, l_ref, v_ref = refs.pop(0), refs.pop(0), refs.pop(0)
        v_ref = v_ref.at[2]
    rok_ref, cok_ref, o_ref, wn_ref, ws_ref, ww_ref, we_ref, inv_ref, buf_ref = refs
    n, w = o_ref.shape
    count = n // 8

    def weights(k, carry):
        sl = rows_of(k)
        x = c_ref[sl, :]
        a = (x + row_above(x, chunk(c_ref, k - 1, count))) * 0.5
        b = (x + row_below(x, chunk(c_ref, k + 1, count))) * 0.5
        e = (x + pltpu.roll(x, 1, 1)) * 0.5
        f = (x + pltpu.roll(x, w - 1, 1)) * 0.5
        wn_ref[sl, :] = a
        ws_ref[sl, :] = b
        ww_ref[sl, :] = e
        we_ref[sl, :] = f
        ok = (rok_ref[sl, :] > 0.5) & (cok_ref[...] > 0.5)
        inv = jnp.where(ok, 1.0 / (a + b + e + f + v_ref[rows_of(k + offset), :]), 0.0)
        inv_ref[sl, :] = inv
        if zero_start:
            buf_ref[sl, :] = jnp.where(inv != 0.0, l_ref[sl, :] * inv, 0.0)
        return carry

    lax.fori_loop(0, count, weights, 0, unroll=POWER_UNROLL)

    def sweep(src, dst):
        def body(k, carry):
            sl = rows_of(k)
            x = src[sl, :]
            summed = (
                l_ref[sl, :]
                + wn_ref[sl, :] * row_above(x, chunk(src, k - 1, count))
                + ws_ref[sl, :] * row_below(x, chunk(src, k + 1, count))
                + ww_ref[sl, :] * pltpu.roll(x, 1, 1)
                + we_ref[sl, :] * pltpu.roll(x, w - 1, 1)
            )
            inv = inv_ref[sl, :]
            dst[sl, :] = jnp.where(inv != 0.0, summed * inv, 0.0)
            return carry

        lax.fori_loop(0, count, body, 0, unroll=POWER_UNROLL)

    def first_sweep(k, carry):
        sl = rows_of(k)
        x = d_ref[rows_of(k + offset), :]
        summed = (
            l_ref[sl, :]
            + wn_ref[sl, :] * row_above(x, d_ref[rows_of(jnp.maximum(k - 1, 0) + offset), :])
            + ws_ref[sl, :] * row_below(x, d_ref[rows_of(jnp.minimum(k + 1, count - 1) + offset), :])
            + ww_ref[sl, :] * pltpu.roll(x, 1, 1)
            + we_ref[sl, :] * pltpu.roll(x, w - 1, 1)
        )
        inv = inv_ref[sl, :]
        buf_ref[sl, :] = jnp.where(inv != 0.0, summed * inv, 0.0)
        return carry

    if not zero_start:
        lax.fori_loop(0, count, first_sweep, 0, unroll=POWER_UNROLL)
    sweep(buf_ref, o_ref)
    sweep(o_ref, buf_ref)
    sweep(buf_ref, o_ref)


def run_power(drop, parts, row_ok, col_ok, offset=0):
    stacked = not isinstance(parts, (tuple, list))
    n, w = parts.shape[1:] if stacked else parts[0].shape
    operands = ([] if drop is None else [drop]) + ([parts] if stacked else list(parts)) + [row_ok, col_ok]
    kernel = functools.partial(power_kernel, zero_start=drop is None, stacked=stacked, offset=offset)
    return pl.pallas_call(
        kernel,
        out_shape=jax.ShapeDtypeStruct((n, w), jnp.float32),
        scratch_shapes=[pltpu.VMEM((n, w), jnp.float32) for _ in range(6)],
        compiler_params=pltpu.CompilerParams(vmem_limit_bytes=60 * 1024 * 1024),
        interpret=INTERPRET,
    )(*operands)


def thermal_kernel(*refs, stride, stored, zero_start):
    refs = list(refs)
    t_ref = None if zero_start else refs.pop(0)
    s_ref, lk_ref, vk_ref, rok_ref, o_ref = refs[:5]
    scratch = refs[5:]
    n, w = lk_ref.shape
    count = n // 8
    lane = lax.broadcasted_iota(jnp.int32, (8, w), 1)
    first = lane == 0
    last = lane == w - 1
    if stored:
        wn_ref, ws_ref, ww_ref, we_ref, wb_ref, wa_ref, inv_ref, buf_ref = scratch
    else:
        wb_ref, wa_ref, inv_ref, buf_ref = scratch

    def lateral(x, k, ref):
        up = row_above(x, chunk(ref, k - 1, count))
        dn = row_below(x, chunk(ref, k + 1, count))
        lf = jnp.where(first, 0.0, pltpu.roll(x, 1, 1))
        rt = jnp.where(last, 0.0, pltpu.roll(x, w - 1, 1))
        return up, dn, lf, rt

    def lateral_weights(k):
        sl = rows_of(k)
        x = lk_ref[sl, :]
        up, dn, lf, rt = lateral(x, k, lk_ref)
        return (x + up) * 0.5, (x + dn) * 0.5, (x + lf) * 0.5, (x + rt) * 0.5

    def weights(k, carry):
        sl = rows_of(k)
        a, b, e, f = lateral_weights(k)
        if stored:
            wn_ref[sl, :] = a
            ws_ref[sl, :] = b
            ww_ref[sl, :] = e
            we_ref[sl, :] = f
        v = vk_ref[sl, :]
        lo = (v + chunk(vk_ref, k - stride, count)) * 0.5
        hi = (v + chunk(vk_ref, k + stride, count)) * 0.5
        wb_ref[sl, :] = lo
        wa_ref[sl, :] = hi
        inv = jnp.where(rok_ref[sl, :] > 0.5, 1.0 / (a + b + e + f + lo + hi), 0.0)
        inv_ref[sl, :] = inv
        if zero_start:
            buf_ref[sl, :] = jnp.where(inv != 0.0, s_ref[sl, :] * inv, 0.0)
        return carry

    lax.fori_loop(0, count, weights, 0, unroll=THERMAL_UNROLL)

    def sweep(src, dst):
        def body(k, carry):
            sl = rows_of(k)
            if stored:
                a, b, e, f = wn_ref[sl, :], ws_ref[sl, :], ww_ref[sl, :], we_ref[sl, :]
            else:
                a, b, e, f = lateral_weights(k)
            x = src[sl, :]
            up, dn, lf, rt = lateral(x, k, src)
            summed = (
                s_ref[sl, :]
                + a * up
                + b * dn
                + e * lf
                + f * rt
                + wb_ref[sl, :] * chunk(src, k - stride, count)
                + wa_ref[sl, :] * chunk(src, k + stride, count)
            )
            inv = inv_ref[sl, :]
            dst[sl, :] = jnp.where(inv != 0.0, summed * inv, 0.0)
            return carry

        lax.fori_loop(0, count, body, 0, unroll=THERMAL_UNROLL)

    if not zero_start:
        sweep(t_ref, buf_ref)
    sweep(buf_ref, o_ref)
    sweep(o_ref, buf_ref)
    sweep(buf_ref, o_ref)


def run_thermal(temp, source, lat, vert, row_ok, stride):
    n, w = lat.shape
    stored = 13 * n * w * 4 <= 40 * 1024 * 1024
    kernel = functools.partial(thermal_kernel, stride=stride, stored=stored, zero_start=temp is None)
    return pl.pallas_call(
        kernel,
        out_shape=jax.ShapeDtypeStruct((n, w), jnp.float32),
        scratch_shapes=[pltpu.VMEM((n, w), jnp.float32) for _ in range(8 if stored else 4)],
        compiler_params=pltpu.CompilerParams(vmem_limit_bytes=60 * 1024 * 1024),
        interpret=INTERPRET,
    )(*([] if temp is None else [temp]), source, lat, vert, row_ok)


def inside_of(start, count, total):
    idx = start + jnp.arange(count, dtype=jnp.int32)
    return (idx >= 0) & (idx < total)


def body(demand, leakage, conductance, vias, layer_of, lateral_k, vertical_k):
    tile_rows, tile_cols = demand.shape
    group_layers, cell_rows, therm_cols = lateral_k.shape
    cell_cols = tile_cols // COARSE
    n_r = lax.axis_size("row")
    n_c = lax.axis_size("col")
    r_idx = lax.axis_index("row")
    c_idx = lax.axis_index("col")
    all_layers = group_layers * n_c
    all_rows = cell_rows * n_r
    total_rows = tile_rows * n_r
    total_cols = tile_cols * n_c

    T0 = 2 * HEAT_SWEEPS
    T1 = HEAT_SWEEPS
    H0 = T0 - 1
    H1 = T1 - 1
    S = SWEEPS
    R1 = H1 * COARSE + SWEEPS
    R0 = max(H0 * COARSE, R1) + SWEEPS
    CW = 128
    PR = -(-R1 // COARSE)
    PC = CW // COARSE

    via_g = VIA_CONDUCT * vias.astype(jnp.float32)
    load0 = demand + leakage

    p0 = extended(jnp.stack([conductance, load0, via_g, leakage]), (("row", 1, R0), ("col", 2, CW)))
    k_ext = extended(jnp.stack([lateral_k, vertical_k]), (("col", 1, T1), ("row", 2, T0)))
    layer_ext = extended(layer_of, (("row", 0, T0),))

    cols_w = tile_cols + 2 * CW
    col_ok = inside_of(c_idx * tile_cols - CW, cols_w, total_cols).astype(jnp.float32)[None, :]

    rows0 = tile_rows + 2 * R0
    row_ok0 = inside_of(r_idx * tile_rows - R0, rows0, total_rows).astype(jnp.float32)[:, None]
    drop0 = run_power(None, p0, row_ok0, col_ok)
    hr0 = H0 * COARSE
    rs = slice(R0 - hr0, R0 + tile_rows + hr0)
    cs = slice(CW, CW + tile_cols)
    d_h = drop0[rs, cs]
    heat0 = coarse_of(p0[1][rs, cs] * (1.0 - d_h) + p0[0][rs, cs] * d_h * d_h)

    def gather_heat(heat):
        copies = jnp.broadcast_to(heat[None], (n_c,) + heat.shape)
        gathered = lax.all_to_all(copies, "col", split_axis=0, concat_axis=0, tiled=True)
        gathered = gathered.transpose(1, 0, 2).reshape(heat.shape[0], n_c * cell_cols)
        return jnp.pad(gathered, ((1, 1), (0, 0)))

    def thermal(temp_ext, heat_ext, halo):
        layers = group_layers + 2 * T1
        rows = cell_rows + 2 * halo
        ks = k_ext[:, :, T0 - halo:T0 + cell_rows + halo]
        tlay = c_idx * group_layers - T1 + jnp.arange(layers, dtype=jnp.int32)
        inside = inside_of(c_idx * group_layers - T1, layers, all_layers)[:, None] & inside_of(r_idx * cell_rows - halo, rows, all_rows)[None, :]
        lay_in = layer_ext[T0 - halo:T0 + cell_rows + halo]
        picker = (lay_in[None, :, :] == tlay[:, None, None]) & inside[:, :, None]
        source = jnp.where(picker, heat_ext[None, :, :], 0.0)
        flat = (layers * rows, therm_cols)
        out = run_thermal(
            None if temp_ext is None else temp_ext.reshape(flat), source.reshape(flat), ks[0].reshape(flat), ks[1].reshape(flat),
            inside.astype(jnp.float32).reshape(layers * rows, 1), rows // 8,
        )
        return out.reshape(layers, rows, therm_cols)

    temp0 = thermal(None, gather_heat(heat0), T0)
    temp0 = temp0[T1:T1 + group_layers, T0 - T1:T0 + cell_rows + T1]

    own_layers = c_idx * group_layers + jnp.arange(group_layers, dtype=jnp.int32)
    t_own = temp0[:, T1 - PR:T1 + cell_rows + PR]
    lay_w = layer_ext[T0 - PR:T0 + cell_rows + PR]
    partial = jnp.sum(jnp.where(lay_w[None, :, :] == own_layers[:, None, None], t_own, 0.0), axis=0)
    partial = jnp.pad(partial, ((0, 0), (PC, PC)))
    windows = jnp.stack([partial[:, j * cell_cols:j * cell_cols + cell_cols + 2 * PC] for j in range(n_c)])
    windows = lax.all_to_all(windows, "col", split_axis=0, concat_axis=0, tiled=True)
    cell_temp = jnp.sum(windows, axis=0)

    denom_c = 1.0 + COND_SLOPE * cell_temp
    grow_c = jnp.expm1(LEAK_SLOPE * cell_temp)
    rows1 = tile_rows + 2 * R1
    fo = PR * COARSE - R1
    denom_f = fine_of(denom_c, cols_w)[fo:fo + rows1]
    grow_f = fine_of(grow_c, cols_w)[fo:fo + rows1]
    rs1 = slice(R0 - R1, R0 - R1 + rows1)
    cond1 = p0[0][rs1] / denom_f
    load1 = p0[1][rs1] + p0[3][rs1] * grow_f
    row_ok1 = inside_of(r_idx * tile_rows - R1, rows1, total_rows).astype(jnp.float32)[:, None]
    drop1 = run_power(drop0, (cond1, load1, p0), row_ok1, col_ok, offset=(R0 - R1) // 8)
    hr1 = H1 * COARSE
    rh = slice(R1 - hr1, R1 + tile_rows + hr1)
    d_h1 = drop1[rh, cs]
    heat1 = coarse_of(load1[rh, cs] * (1.0 - d_h1) + cond1[rh, cs] * d_h1 * d_h1)
    temp1 = thermal(extended(temp0, (("col", 0, T1),)), gather_heat(heat1), T1)
    temp_out = temp1[T1:T1 + group_layers, T1:T1 + cell_rows]
    drop_out = drop1[R1:R1 + tile_rows, cs]
    return (drop_out, temp_out)


def solution(mesh):
    in_specs = (
        P("row", "col"),
        P("row", "col"),
        P("row", "col"),
        P("row", "col"),
        P("row", None),
        P("col", "row", None),
        P("col", "row", None),
    )
    out_specs = (P("row", "col"), P("col", "row", None))
    return jax.shard_map(body, mesh=mesh, in_specs=in_specs, out_specs=out_specs, check_vma=False)
```

```python
import functools
import os

import jax
import jax.numpy as jnp
from jax import lax
from jax.experimental import pallas as pl
from jax.experimental.pallas import tpu as pltpu
from jax.sharding import PartitionSpec as P

INTERPRET = os.environ.get("SOL_INTERPRET") == "1"
POWER_UNROLL = 2
THERMAL_UNROLL = 16

COARSE = 8
SWEEPS = 4
HEAT_SWEEPS = 4
OUTER = 2


COND_SLOPE = 0.5
LEAK_SLOPE = 0.7
VIA_CONDUCT = 4.0

HALO = 4


def extended(block, sides):
    for axis, dim, width in sides:
        count = lax.axis_size(axis)
        forward = [(i, i + 1) for i in range(count - 1)]
        backward = [(target, source) for source, target in forward]
        low = lax.ppermute(
            lax.slice_in_dim(block, block.shape[dim] - width, None, axis=dim), axis, forward
        )
        high = lax.ppermute(lax.slice_in_dim(block, 0, width, axis=dim), axis, backward)
        block = jnp.concatenate([low, block, high], axis=dim)
    return block


def spread_cols(coarse, fine_cols):
    n = coarse.shape[1]
    ids = jnp.arange(fine_cols, dtype=jnp.int32) // COARSE
    onehot = (jnp.arange(n, dtype=jnp.int32)[:, None] == ids[None, :]).astype(jnp.float32)
    return jnp.dot(coarse, onehot, precision=lax.Precision.HIGHEST)


def fine_of(coarse, fine_cols):
    wide = spread_cols(coarse, fine_cols)
    rows = wide.shape[0]
    return jnp.broadcast_to(wide[:, None, :], (rows, COARSE, fine_cols)).reshape(rows * COARSE, fine_cols)


def coarse_of(fine):
    rows, cols = fine.shape
    summed_rows = jnp.sum(fine.reshape(rows // COARSE, COARSE, cols), axis=1)
    n = cols // COARSE
    ids = jnp.arange(cols, dtype=jnp.int32) // COARSE
    onehot = (ids[:, None] == jnp.arange(n, dtype=jnp.int32)[None, :]).astype(jnp.float32)
    return jnp.dot(summed_rows, onehot, precision=lax.Precision.HIGHEST) * (1.0 / (COARSE * COARSE))


def row_above(x, above):
    sub = lax.broadcasted_iota(jnp.int32, x.shape, 0)
    edge = jnp.broadcast_to(above[x.shape[0] - 1:, :], x.shape)
    return jnp.where(sub == 0, edge, pltpu.roll(x, 1, 0))


def row_below(x, below):
    n = x.shape[0]
    sub = lax.broadcasted_iota(jnp.int32, x.shape, 0)
    edge = jnp.broadcast_to(below[:1, :], x.shape)
    return jnp.where(sub == n - 1, edge, pltpu.roll(x, n - 1, 0))


def rows_of(k):
    return pl.ds(pl.multiple_of(k * 8, 8), 8)


def chunk(ref, k, count):
    return ref[rows_of(jnp.clip(k, 0, count - 1)), :]


def power_kernel(*refs, zero_start, stacked, offset):
    refs = list(refs)
    d_ref = None if zero_start else refs.pop(0)
    if stacked:
        p_ref = refs.pop(0)
        c_ref, l_ref, v_ref = p_ref.at[0], p_ref.at[1], p_ref.at[2]
    else:
        c_ref, l_ref, v_ref = refs.pop(0), refs.pop(0), refs.pop(0)
        v_ref = v_ref.at[2]
    rok_ref, cok_ref, o_ref, wn_ref, ws_ref, ww_ref, we_ref, inv_ref, buf_ref = refs
    n, w = o_ref.shape
    count = n // 8

    def weights(k, carry):
        sl = rows_of(k)
        x = c_ref[sl, :]
        a = (x + row_above(x, chunk(c_ref, k - 1, count))) * 0.5
        b = (x + row_below(x, chunk(c_ref, k + 1, count))) * 0.5
        e = (x + pltpu.roll(x, 1, 1)) * 0.5
        f = (x + pltpu.roll(x, w - 1, 1)) * 0.5
        wn_ref[sl, :] = a
        ws_ref[sl, :] = b
        ww_ref[sl, :] = e
        we_ref[sl, :] = f
        ok = (rok_ref[sl, :] > 0.5) & (cok_ref[...] > 0.5)
        inv = jnp.where(ok, 1.0 / (a + b + e + f + v_ref[rows_of(k + offset), :]), 0.0)
        inv_ref[sl, :] = inv
        if zero_start:
            buf_ref[sl, :] = jnp.where(inv != 0.0, l_ref[sl, :] * inv, 0.0)
        return carry

    lax.fori_loop(0, count, weights, 0, unroll=POWER_UNROLL)

    def sweep(src, dst):
        def body(k, carry):
            sl = rows_of(k)
            x = src[sl, :]
            summed = (
                l_ref[sl, :]
                + wn_ref[sl, :] * row_above(x, chunk(src, k - 1, count))
                + ws_ref[sl, :] * row_below(x, chunk(src, k + 1, count))
                + ww_ref[sl, :] * pltpu.roll(x, 1, 1)
                + we_ref[sl, :] * pltpu.roll(x, w - 1, 1)
            )
            inv = inv_ref[sl, :]
            dst[sl, :] = jnp.where(inv != 0.0, summed * inv, 0.0)
            return carry

        lax.fori_loop(0, count, body, 0, unroll=POWER_UNROLL)

    def first_sweep(k, carry):
        sl = rows_of(k)
        x = d_ref[rows_of(k + offset), :]
        summed = (
            l_ref[sl, :]
            + wn_ref[sl, :] * row_above(x, d_ref[rows_of(jnp.maximum(k - 1, 0) + offset), :])
            + ws_ref[sl, :] * row_below(x, d_ref[rows_of(jnp.minimum(k + 1, count - 1) + offset), :])
            + ww_ref[sl, :] * pltpu.roll(x, 1, 1)
            + we_ref[sl, :] * pltpu.roll(x, w - 1, 1)
        )
        inv = inv_ref[sl, :]
        buf_ref[sl, :] = jnp.where(inv != 0.0, summed * inv, 0.0)
        return carry

    if not zero_start:
        lax.fori_loop(0, count, first_sweep, 0, unroll=POWER_UNROLL)
    sweep(buf_ref, o_ref)
    sweep(o_ref, buf_ref)
    sweep(buf_ref, o_ref)


def run_power(drop, parts, row_ok, col_ok, offset=0):
    stacked = not isinstance(parts, (tuple, list))
    n, w = parts.shape[1:] if stacked else parts[0].shape
    operands = ([] if drop is None else [drop]) + ([parts] if stacked else list(parts)) + [row_ok, col_ok]
    kernel = functools.partial(power_kernel, zero_start=drop is None, stacked=stacked, offset=offset)
    return pl.pallas_call(
        kernel,
        out_shape=jax.ShapeDtypeStruct((n, w), jnp.float32),
        scratch_shapes=[pltpu.VMEM((n, w), jnp.float32) for _ in range(6)],
        compiler_params=pltpu.CompilerParams(vmem_limit_bytes=60 * 1024 * 1024),
        interpret=INTERPRET,
    )(*operands)


def thermal_kernel(*refs, stride, stored, zero_start):
    refs = list(refs)
    t_ref = None if zero_start else refs.pop(0)
    s_ref, lk_ref, vk_ref, rok_ref, o_ref = refs[:5]
    scratch = refs[5:]
    n, w = lk_ref.shape
    count = n // 8
    lane = lax.broadcasted_iota(jnp.int32, (8, w), 1)
    first = lane == 0
    last = lane == w - 1
    if stored:
        wn_ref, ws_ref, ww_ref, we_ref, wb_ref, wa_ref, inv_ref, buf_ref = scratch
    else:
        wb_ref, wa_ref, inv_ref, buf_ref = scratch

    def lateral(x, k, ref):
        up = row_above(x, chunk(ref, k - 1, count))
        dn = row_below(x, chunk(ref, k + 1, count))
        lf = jnp.where(first, 0.0, pltpu.roll(x, 1, 1))
        rt = jnp.where(last, 0.0, pltpu.roll(x, w - 1, 1))
        return up, dn, lf, rt

    def lateral_weights(k):
        sl = rows_of(k)
        x = lk_ref[sl, :]
        up, dn, lf, rt = lateral(x, k, lk_ref)
        return (x + up) * 0.5, (x + dn) * 0.5, (x + lf) * 0.5, (x + rt) * 0.5

    def weights(k, carry):
        sl = rows_of(k)
        a, b, e, f = lateral_weights(k)
        if stored:
            wn_ref[sl, :] = a
            ws_ref[sl, :] = b
            ww_ref[sl, :] = e
            we_ref[sl, :] = f
        v = vk_ref[sl, :]
        lo = (v + chunk(vk_ref, k - stride, count)) * 0.5
        hi = (v + chunk(vk_ref, k + stride, count)) * 0.5
        wb_ref[sl, :] = lo
        wa_ref[sl, :] = hi
        inv = jnp.where(rok_ref[sl, :] > 0.5, 1.0 / (a + b + e + f + lo + hi), 0.0)
        inv_ref[sl, :] = inv
        if zero_start:
            buf_ref[sl, :] = jnp.where(inv != 0.0, s_ref[sl, :] * inv, 0.0)
        return carry

    lax.fori_loop(0, count, weights, 0, unroll=THERMAL_UNROLL)

    def sweep(src, dst):
        def body(k, carry):
            sl = rows_of(k)
            if stored:
                a, b, e, f = wn_ref[sl, :], ws_ref[sl, :], ww_ref[sl, :], we_ref[sl, :]
            else:
                a, b, e, f = lateral_weights(k)
            x = src[sl, :]
            up, dn, lf, rt = lateral(x, k, src)
            summed = (
                s_ref[sl, :]
                + a * up
                + b * dn
                + e * lf
                + f * rt
                + wb_ref[sl, :] * chunk(src, k - stride, count)
                + wa_ref[sl, :] * chunk(src, k + stride, count)
            )
            inv = inv_ref[sl, :]
            dst[sl, :] = jnp.where(inv != 0.0, summed * inv, 0.0)
            return carry

        lax.fori_loop(0, count, body, 0, unroll=THERMAL_UNROLL)

    if not zero_start:
        sweep(t_ref, buf_ref)
    sweep(buf_ref, o_ref)
    sweep(o_ref, buf_ref)
    sweep(buf_ref, o_ref)


def run_thermal(temp, source, lat, vert, row_ok, stride):
    n, w = lat.shape
    stored = 13 * n * w * 4 <= 40 * 1024 * 1024
    kernel = functools.partial(thermal_kernel, stride=stride, stored=stored, zero_start=temp is None)
    return pl.pallas_call(
        kernel,
        out_shape=jax.ShapeDtypeStruct((n, w), jnp.float32),
        scratch_shapes=[pltpu.VMEM((n, w), jnp.float32) for _ in range(8 if stored else 4)],
        compiler_params=pltpu.CompilerParams(vmem_limit_bytes=60 * 1024 * 1024),
        interpret=INTERPRET,
    )(*([] if temp is None else [temp]), source, lat, vert, row_ok)


def inside_of(start, count, total):
    idx = start + jnp.arange(count, dtype=jnp.int32)
    return (idx >= 0) & (idx < total)


def body(demand, leakage, conductance, vias, layer_of, lateral_k, vertical_k):
    tile_rows, tile_cols = demand.shape
    group_layers, cell_rows, therm_cols = lateral_k.shape
    cell_cols = tile_cols // COARSE
    n_r = lax.axis_size("row")
    n_c = lax.axis_size("col")
    r_idx = lax.axis_index("row")
    c_idx = lax.axis_index("col")
    all_layers = group_layers * n_c
    all_rows = cell_rows * n_r
    total_rows = tile_rows * n_r
    total_cols = tile_cols * n_c

    T0 = 2 * HEAT_SWEEPS
    T1 = HEAT_SWEEPS
    H0 = T0 - 1
    H1 = T1 - 1
    S = SWEEPS
    R1 = H1 * COARSE + SWEEPS
    R0 = max(H0 * COARSE, R1) + SWEEPS
    CW = 64
    PR = -(-R1 // COARSE)
    PC = CW // COARSE

    via_g = VIA_CONDUCT * vias.astype(jnp.float32)
    load0 = demand + leakage

    p0 = extended(jnp.stack([conductance, load0, via_g, leakage]), (("row", 1, R0), ("col", 2, CW)))
    k_ext = extended(jnp.stack([lateral_k, vertical_k]), (("col", 1, T1), ("row", 2, T0)))
    layer_ext = extended(layer_of, (("row", 0, T0),))

    cols_w = tile_cols + 2 * CW
    col_ok = inside_of(c_idx * tile_cols - CW, cols_w, total_cols).astype(jnp.float32)[None, :]

    rows0 = tile_rows + 2 * R0
    row_ok0 = inside_of(r_idx * tile_rows - R0, rows0, total_rows).astype(jnp.float32)[:, None]
    drop0 = run_power(None, p0, row_ok0, col_ok)
    hr0 = H0 * COARSE
    rs = slice(R0 - hr0, R0 + tile_rows + hr0)
    cs = slice(CW, CW + tile_cols)
    d_h = drop0[rs, cs]
    heat0 = coarse_of(p0[1][rs, cs] * (1.0 - d_h) + p0[0][rs, cs] * d_h * d_h)

    def gather_heat(heat):
        copies = jnp.broadcast_to(heat[None], (n_c,) + heat.shape)
        gathered = lax.all_to_all(copies, "col", split_axis=0, concat_axis=0, tiled=True)
        gathered = gathered.transpose(1, 0, 2).reshape(heat.shape[0], n_c * cell_cols)
        return jnp.pad(gathered, ((1, 1), (0, 0)))

    def thermal(temp_ext, heat_ext, halo):
        layers = group_layers + 2 * T1
        rows = cell_rows + 2 * halo
        ks = k_ext[:, :, T0 - halo:T0 + cell_rows + halo]
        tlay = c_idx * group_layers - T1 + jnp.arange(layers, dtype=jnp.int32)
        inside = inside_of(c_idx * group_layers - T1, layers, all_layers)[:, None] & inside_of(r_idx * cell_rows - halo, rows, all_rows)[None, :]
        lay_in = layer_ext[T0 - halo:T0 + cell_rows + halo]
        picker = (lay_in[None, :, :] == tlay[:, None, None]) & inside[:, :, None]
        source = jnp.where(picker, heat_ext[None, :, :], 0.0)
        flat = (layers * rows, therm_cols)
        out = run_thermal(
            None if temp_ext is None else temp_ext.reshape(flat), source.reshape(flat), ks[0].reshape(flat), ks[1].reshape(flat),
            inside.astype(jnp.float32).reshape(layers * rows, 1), rows // 8,
        )
        return out.reshape(layers, rows, therm_cols)

    temp0 = thermal(None, gather_heat(heat0), T0)
    temp0 = temp0[T1:T1 + group_layers, T0 - T1:T0 + cell_rows + T1]

    own_layers = c_idx * group_layers + jnp.arange(group_layers, dtype=jnp.int32)
    t_own = temp0[:, T1 - PR:T1 + cell_rows + PR]
    lay_w = layer_ext[T0 - PR:T0 + cell_rows + PR]
    partial = jnp.sum(jnp.where(lay_w[None, :, :] == own_layers[:, None, None], t_own, 0.0), axis=0)
    partial = jnp.pad(partial, ((0, 0), (PC, PC)))
    windows = jnp.stack([partial[:, j * cell_cols:j * cell_cols + cell_cols + 2 * PC] for j in range(n_c)])
    windows = lax.all_to_all(windows, "col", split_axis=0, concat_axis=0, tiled=True)
    cell_temp = jnp.sum(windows, axis=0)

    denom_c = 1.0 + COND_SLOPE * cell_temp
    grow_c = jnp.expm1(LEAK_SLOPE * cell_temp)
    rows1 = tile_rows + 2 * R1
    fo = PR * COARSE - R1
    denom_f = fine_of(denom_c, cols_w)[fo:fo + rows1]
    grow_f = fine_of(grow_c, cols_w)[fo:fo + rows1]
    rs1 = slice(R0 - R1, R0 - R1 + rows1)
    cond1 = p0[0][rs1] / denom_f
    load1 = p0[1][rs1] + p0[3][rs1] * grow_f
    row_ok1 = inside_of(r_idx * tile_rows - R1, rows1, total_rows).astype(jnp.float32)[:, None]
    drop1 = run_power(drop0, (cond1, load1, p0), row_ok1, col_ok, offset=(R0 - R1) // 8)
    hr1 = H1 * COARSE
    rh = slice(R1 - hr1, R1 + tile_rows + hr1)
    d_h1 = drop1[rh, cs]
    heat1 = coarse_of(load1[rh, cs] * (1.0 - d_h1) + cond1[rh, cs] * d_h1 * d_h1)
    temp1 = thermal(extended(temp0, (("col", 0, T1),)), gather_heat(heat1), T1)
    temp_out = temp1[T1:T1 + group_layers, T1:T1 + cell_rows]
    drop_out = drop1[R1:R1 + tile_rows, cs]
    return (drop_out, temp_out)


def solution(mesh):
    in_specs = (
        P("row", "col"),
        P("row", "col"),
        P("row", "col"),
        P("row", "col"),
        P("row", None),
        P("col", "row", None),
        P("col", "row", None),
    )
    out_specs = (P("row", "col"), P("col", "row", None))
    return jax.shard_map(body, mesh=mesh, in_specs=in_specs, out_specs=out_specs, check_vma=False)
```

```python
import functools
import os

import jax
import jax.numpy as jnp
from jax import lax
from jax.experimental import pallas as pl
from jax.experimental.pallas import tpu as pltpu
from jax.sharding import PartitionSpec as P

INTERPRET = os.environ.get("SOL_INTERPRET") == "1"
POWER_UNROLL = 4
THERMAL_UNROLL = 32

COARSE = 8
SWEEPS = 4
HEAT_SWEEPS = 4
OUTER = 2


COND_SLOPE = 0.5
LEAK_SLOPE = 0.7
VIA_CONDUCT = 4.0

HALO = 4


def extended(block, sides):
    for axis, dim, width in sides:
        count = lax.axis_size(axis)
        forward = [(i, i + 1) for i in range(count - 1)]
        backward = [(target, source) for source, target in forward]
        low = lax.ppermute(
            lax.slice_in_dim(block, block.shape[dim] - width, None, axis=dim), axis, forward
        )
        high = lax.ppermute(lax.slice_in_dim(block, 0, width, axis=dim), axis, backward)
        block = jnp.concatenate([low, block, high], axis=dim)
    return block


def spread_cols(coarse, fine_cols):
    n = coarse.shape[1]
    ids = jnp.arange(fine_cols, dtype=jnp.int32) // COARSE
    onehot = (jnp.arange(n, dtype=jnp.int32)[:, None] == ids[None, :]).astype(jnp.float32)
    return jnp.dot(coarse, onehot, precision=lax.Precision.HIGHEST)


def fine_of(coarse, fine_cols):
    wide = spread_cols(coarse, fine_cols)
    rows = wide.shape[0]
    return jnp.broadcast_to(wide[:, None, :], (rows, COARSE, fine_cols)).reshape(rows * COARSE, fine_cols)


def coarse_of(fine):
    rows, cols = fine.shape
    summed_rows = jnp.sum(fine.reshape(rows // COARSE, COARSE, cols), axis=1)
    n = cols // COARSE
    ids = jnp.arange(cols, dtype=jnp.int32) // COARSE
    onehot = (ids[:, None] == jnp.arange(n, dtype=jnp.int32)[None, :]).astype(jnp.float32)
    return jnp.dot(summed_rows, onehot, precision=lax.Precision.HIGHEST) * (1.0 / (COARSE * COARSE))


def row_above(x, above):
    sub = lax.broadcasted_iota(jnp.int32, x.shape, 0)
    edge = jnp.broadcast_to(above[x.shape[0] - 1:, :], x.shape)
    return jnp.where(sub == 0, edge, pltpu.roll(x, 1, 0))


def row_below(x, below):
    n = x.shape[0]
    sub = lax.broadcasted_iota(jnp.int32, x.shape, 0)
    edge = jnp.broadcast_to(below[:1, :], x.shape)
    return jnp.where(sub == n - 1, edge, pltpu.roll(x, n - 1, 0))


def rows_of(k):
    return pl.ds(pl.multiple_of(k * 8, 8), 8)


def chunk(ref, k, count):
    return ref[rows_of(jnp.clip(k, 0, count - 1)), :]


def power_kernel(*refs, zero_start, stacked, offset):
    refs = list(refs)
    d_ref = None if zero_start else refs.pop(0)
    if stacked:
        p_ref = refs.pop(0)
        c_ref, l_ref, v_ref = p_ref.at[0], p_ref.at[1], p_ref.at[2]
    else:
        c_ref, l_ref, v_ref = refs.pop(0), refs.pop(0), refs.pop(0)
        v_ref = v_ref.at[2]
    rok_ref, cok_ref, o_ref, wn_ref, ws_ref, ww_ref, we_ref, inv_ref, buf_ref = refs
    n, w = o_ref.shape
    count = n // 8

    def weights(k, carry):
        sl = rows_of(k)
        x = c_ref[sl, :]
        a = (x + row_above(x, chunk(c_ref, k - 1, count))) * 0.5
        b = (x + row_below(x, chunk(c_ref, k + 1, count))) * 0.5
        e = (x + pltpu.roll(x, 1, 1)) * 0.5
        f = (x + pltpu.roll(x, w - 1, 1)) * 0.5
        wn_ref[sl, :] = a
        ws_ref[sl, :] = b
        ww_ref[sl, :] = e
        we_ref[sl, :] = f
        ok = (rok_ref[sl, :] > 0.5) & (cok_ref[...] > 0.5)
        inv = jnp.where(ok, 1.0 / (a + b + e + f + v_ref[rows_of(k + offset), :]), 0.0)
        inv_ref[sl, :] = inv
        if zero_start:
            buf_ref[sl, :] = jnp.where(inv != 0.0, l_ref[sl, :] * inv, 0.0)
        return carry

    lax.fori_loop(0, count, weights, 0, unroll=POWER_UNROLL)

    def sweep(src, dst):
        def body(k, carry):
            sl = rows_of(k)
            x = src[sl, :]
            summed = (
                l_ref[sl, :]
                + wn_ref[sl, :] * row_above(x, chunk(src, k - 1, count))
                + ws_ref[sl, :] * row_below(x, chunk(src, k + 1, count))
                + ww_ref[sl, :] * pltpu.roll(x, 1, 1)
                + we_ref[sl, :] * pltpu.roll(x, w - 1, 1)
            )
            inv = inv_ref[sl, :]
            dst[sl, :] = jnp.where(inv != 0.0, summed * inv, 0.0)
            return carry

        lax.fori_loop(0, count, body, 0, unroll=POWER_UNROLL)

    def first_sweep(k, carry):
        sl = rows_of(k)
        x = d_ref[rows_of(k + offset), :]
        summed = (
            l_ref[sl, :]
            + wn_ref[sl, :] * row_above(x, d_ref[rows_of(jnp.maximum(k - 1, 0) + offset), :])
            + ws_ref[sl, :] * row_below(x, d_ref[rows_of(jnp.minimum(k + 1, count - 1) + offset), :])
            + ww_ref[sl, :] * pltpu.roll(x, 1, 1)
            + we_ref[sl, :] * pltpu.roll(x, w - 1, 1)
        )
        inv = inv_ref[sl, :]
        buf_ref[sl, :] = jnp.where(inv != 0.0, summed * inv, 0.0)
        return carry

    if not zero_start:
        lax.fori_loop(0, count, first_sweep, 0, unroll=POWER_UNROLL)
    sweep(buf_ref, o_ref)
    sweep(o_ref, buf_ref)
    sweep(buf_ref, o_ref)


def run_power(drop, parts, row_ok, col_ok, offset=0):
    stacked = not isinstance(parts, (tuple, list))
    n, w = parts.shape[1:] if stacked else parts[0].shape
    operands = ([] if drop is None else [drop]) + ([parts] if stacked else list(parts)) + [row_ok, col_ok]
    kernel = functools.partial(power_kernel, zero_start=drop is None, stacked=stacked, offset=offset)
    return pl.pallas_call(
        kernel,
        out_shape=jax.ShapeDtypeStruct((n, w), jnp.float32),
        scratch_shapes=[pltpu.VMEM((n, w), jnp.float32) for _ in range(6)],
        compiler_params=pltpu.CompilerParams(vmem_limit_bytes=60 * 1024 * 1024),
        interpret=INTERPRET,
    )(*operands)


def thermal_kernel(*refs, stride, stored, zero_start):
    refs = list(refs)
    t_ref = None if zero_start else refs.pop(0)
    s_ref, lk_ref, vk_ref, rok_ref, o_ref = refs[:5]
    scratch = refs[5:]
    n, w = lk_ref.shape
    count = n // 8
    lane = lax.broadcasted_iota(jnp.int32, (8, w), 1)
    first = lane == 0
    last = lane == w - 1
    if stored:
        wn_ref, ws_ref, ww_ref, we_ref, wb_ref, wa_ref, inv_ref, buf_ref = scratch
    else:
        wb_ref, wa_ref, inv_ref, buf_ref = scratch

    def lateral(x, k, ref):
        up = row_above(x, chunk(ref, k - 1, count))
        dn = row_below(x, chunk(ref, k + 1, count))
        lf = jnp.where(first, 0.0, pltpu.roll(x, 1, 1))
        rt = jnp.where(last, 0.0, pltpu.roll(x, w - 1, 1))
        return up, dn, lf, rt

    def lateral_weights(k):
        sl = rows_of(k)
        x = lk_ref[sl, :]
        up, dn, lf, rt = lateral(x, k, lk_ref)
        return (x + up) * 0.5, (x + dn) * 0.5, (x + lf) * 0.5, (x + rt) * 0.5

    def weights(k, carry):
        sl = rows_of(k)
        a, b, e, f = lateral_weights(k)
        if stored:
            wn_ref[sl, :] = a
            ws_ref[sl, :] = b
            ww_ref[sl, :] = e
            we_ref[sl, :] = f
        v = vk_ref[sl, :]
        lo = (v + chunk(vk_ref, k - stride, count)) * 0.5
        hi = (v + chunk(vk_ref, k + stride, count)) * 0.5
        wb_ref[sl, :] = lo
        wa_ref[sl, :] = hi
        inv = jnp.where(rok_ref[sl, :] > 0.5, 1.0 / (a + b + e + f + lo + hi), 0.0)
        inv_ref[sl, :] = inv
        if zero_start:
            buf_ref[sl, :] = jnp.where(inv != 0.0, s_ref[sl, :] * inv, 0.0)
        return carry

    lax.fori_loop(0, count, weights, 0, unroll=THERMAL_UNROLL)

    def sweep(src, dst):
        def body(k, carry):
            sl = rows_of(k)
            if stored:
                a, b, e, f = wn_ref[sl, :], ws_ref[sl, :], ww_ref[sl, :], we_ref[sl, :]
            else:
                a, b, e, f = lateral_weights(k)
            x = src[sl, :]
            up, dn, lf, rt = lateral(x, k, src)
            summed = (
                s_ref[sl, :]
                + a * up
                + b * dn
                + e * lf
                + f * rt
                + wb_ref[sl, :] * chunk(src, k - stride, count)
                + wa_ref[sl, :] * chunk(src, k + stride, count)
            )
            inv = inv_ref[sl, :]
            dst[sl, :] = jnp.where(inv != 0.0, summed * inv, 0.0)
            return carry

        lax.fori_loop(0, count, body, 0, unroll=THERMAL_UNROLL)

    if not zero_start:
        sweep(t_ref, buf_ref)
    sweep(buf_ref, o_ref)
    sweep(o_ref, buf_ref)
    sweep(buf_ref, o_ref)


def run_thermal(temp, source, lat, vert, row_ok, stride):
    n, w = lat.shape
    stored = 13 * n * w * 4 <= 40 * 1024 * 1024
    kernel = functools.partial(thermal_kernel, stride=stride, stored=stored, zero_start=temp is None)
    return pl.pallas_call(
        kernel,
        out_shape=jax.ShapeDtypeStruct((n, w), jnp.float32),
        scratch_shapes=[pltpu.VMEM((n, w), jnp.float32) for _ in range(8 if stored else 4)],
        compiler_params=pltpu.CompilerParams(vmem_limit_bytes=60 * 1024 * 1024),
        interpret=INTERPRET,
    )(*([] if temp is None else [temp]), source, lat, vert, row_ok)


def inside_of(start, count, total):
    idx = start + jnp.arange(count, dtype=jnp.int32)
    return (idx >= 0) & (idx < total)


def body(demand, leakage, conductance, vias, layer_of, lateral_k, vertical_k):
    tile_rows, tile_cols = demand.shape
    group_layers, cell_rows, therm_cols = lateral_k.shape
    cell_cols = tile_cols // COARSE
    n_r = lax.axis_size("row")
    n_c = lax.axis_size("col")
    r_idx = lax.axis_index("row")
    c_idx = lax.axis_index("col")
    all_layers = group_layers * n_c
    all_rows = cell_rows * n_r
    total_rows = tile_rows * n_r
    total_cols = tile_cols * n_c

    T0 = 2 * HEAT_SWEEPS
    T1 = HEAT_SWEEPS
    H0 = T0 - 1
    H1 = T1 - 1
    S = SWEEPS
    R1 = H1 * COARSE + SWEEPS
    R0 = max(H0 * COARSE, R1) + SWEEPS
    CW = 64
    PR = -(-R1 // COARSE)
    PC = CW // COARSE

    via_g = VIA_CONDUCT * vias.astype(jnp.float32)
    load0 = demand + leakage

    p0 = extended(jnp.stack([conductance, load0, via_g, leakage]), (("row", 1, R0), ("col", 2, CW)))
    k_ext = extended(jnp.stack([lateral_k, vertical_k]), (("col", 1, T1), ("row", 2, T0)))
    layer_ext = extended(layer_of, (("row", 0, T0),))

    cols_w = tile_cols + 2 * CW
    col_ok = inside_of(c_idx * tile_cols - CW, cols_w, total_cols).astype(jnp.float32)[None, :]

    rows0 = tile_rows + 2 * R0
    row_ok0 = inside_of(r_idx * tile_rows - R0, rows0, total_rows).astype(jnp.float32)[:, None]
    drop0 = run_power(None, p0, row_ok0, col_ok)
    hr0 = H0 * COARSE
    rs = slice(R0 - hr0, R0 + tile_rows + hr0)
    cs = slice(CW, CW + tile_cols)
    d_h = drop0[rs, cs]
    heat0 = coarse_of(p0[1][rs, cs] * (1.0 - d_h) + p0[0][rs, cs] * d_h * d_h)

    def gather_heat(heat):
        copies = jnp.broadcast_to(heat[None], (n_c,) + heat.shape)
        gathered = lax.all_to_all(copies, "col", split_axis=0, concat_axis=0, tiled=True)
        gathered = gathered.transpose(1, 0, 2).reshape(heat.shape[0], n_c * cell_cols)
        return jnp.pad(gathered, ((1, 1), (0, 0)))

    def thermal(temp_ext, heat_ext, halo):
        layers = group_layers + 2 * T1
        rows = cell_rows + 2 * halo
        ks = k_ext[:, :, T0 - halo:T0 + cell_rows + halo]
        tlay = c_idx * group_layers - T1 + jnp.arange(layers, dtype=jnp.int32)
        inside = inside_of(c_idx * group_layers - T1, layers, all_layers)[:, None] & inside_of(r_idx * cell_rows - halo, rows, all_rows)[None, :]
        lay_in = layer_ext[T0 - halo:T0 + cell_rows + halo]
        picker = (lay_in[None, :, :] == tlay[:, None, None]) & inside[:, :, None]
        source = jnp.where(picker, heat_ext[None, :, :], 0.0)
        flat = (layers * rows, therm_cols)
        out = run_thermal(
            None if temp_ext is None else temp_ext.reshape(flat), source.reshape(flat), ks[0].reshape(flat), ks[1].reshape(flat),
            inside.astype(jnp.float32).reshape(layers * rows, 1), rows // 8,
        )
        return out.reshape(layers, rows, therm_cols)

    temp0 = thermal(None, gather_heat(heat0), T0)
    temp0 = temp0[T1:T1 + group_layers, T0 - T1:T0 + cell_rows + T1]

    own_layers = c_idx * group_layers + jnp.arange(group_layers, dtype=jnp.int32)
    t_own = temp0[:, T1 - PR:T1 + cell_rows + PR]
    lay_w = layer_ext[T0 - PR:T0 + cell_rows + PR]
    partial = jnp.sum(jnp.where(lay_w[None, :, :] == own_layers[:, None, None], t_own, 0.0), axis=0)
    partial = jnp.pad(partial, ((0, 0), (PC, PC)))
    windows = jnp.stack([partial[:, j * cell_cols:j * cell_cols + cell_cols + 2 * PC] for j in range(n_c)])
    windows = lax.all_to_all(windows, "col", split_axis=0, concat_axis=0, tiled=True)
    cell_temp = jnp.sum(windows, axis=0)

    denom_c = 1.0 + COND_SLOPE * cell_temp
    grow_c = jnp.expm1(LEAK_SLOPE * cell_temp)
    rows1 = tile_rows + 2 * R1
    fo = PR * COARSE - R1
    denom_f = fine_of(denom_c, cols_w)[fo:fo + rows1]
    grow_f = fine_of(grow_c, cols_w)[fo:fo + rows1]
    rs1 = slice(R0 - R1, R0 - R1 + rows1)
    cond1 = p0[0][rs1] / denom_f
    load1 = p0[1][rs1] + p0[3][rs1] * grow_f
    row_ok1 = inside_of(r_idx * tile_rows - R1, rows1, total_rows).astype(jnp.float32)[:, None]
    drop1 = run_power(drop0, (cond1, load1, p0), row_ok1, col_ok, offset=(R0 - R1) // 8)
    hr1 = H1 * COARSE
    rh = slice(R1 - hr1, R1 + tile_rows + hr1)
    d_h1 = drop1[rh, cs]
    heat1 = coarse_of(load1[rh, cs] * (1.0 - d_h1) + cond1[rh, cs] * d_h1 * d_h1)
    temp1 = thermal(extended(temp0, (("col", 0, T1),)), gather_heat(heat1), T1)
    temp_out = temp1[T1:T1 + group_layers, T1:T1 + cell_rows]
    drop_out = drop1[R1:R1 + tile_rows, cs]
    return (drop_out, temp_out)


def solution(mesh):
    in_specs = (
        P("row", "col"),
        P("row", "col"),
        P("row", "col"),
        P("row", "col"),
        P("row", None),
        P("col", "row", None),
        P("col", "row", None),
    )
    out_specs = (P("row", "col"), P("col", "row", None))
    return jax.shard_map(body, mesh=mesh, in_specs=in_specs, out_specs=out_specs, check_vma=False)
```
